32 devices in a mesh: grp: 2 (over y), ctx: 8 (over z, x), pair: 2 (over core).
Axes of the slice: x: 2, y: 2, z: 4, core: 2. Of those that a mesh axis runs over, the one named last changes fastest.
Arguments:
- normed_input: bfloat16 [4, 1024, 2688], P(('grp', 'pair'), 'ctx'), parts along dimension 0, may hold values from -6 to 6
- queries: bfloat16 [4, 1024, 2048], P(('grp', 'pair'), 'ctx'), parts along dimension 0, may hold values from -64 to 64
- keys: bfloat16 [4, 1024, 1024], P(('grp', 'pair'), 'ctx'), parts along dimension 0, may hold values from -64 to 64
- value_projection: bfloat16 [2688, 1024], P('ctx'), may hold values from -0.125 to 0.125
- adapter_down: bfloat16 [2688, 16], replicated, may hold values from -0.125 to 0.125
- adapter_up: bfloat16 [16, 1024], replicated, may hold values from -1.5 to 1.5
- output_gradient: bfloat16 [4, 1024, 2048], P(('grp', 'pair'), 'ctx'), parts along dimension 0, may hold values from -6 to 6
- policy_logprob: float32 [4, 1024], P(('grp', 'pair'), 'ctx'), parts along dimension 0, may hold values from -6 to 0
- reference_logprob: float32 [4, 1024], P(('grp', 'pair'), 'ctx'), parts along dimension 0, may hold values from -8 to 0
- token_pair_index: int32 [4, 1024], P(('grp', 'pair'), 'ctx'), parts along dimension 0, may hold values from 0 to 7, never falling along the last dimension, each value on 1 to 1017 neighbouring positions
Outputs:
- input_grad: bfloat16 [4, 1024, 2688], P(('grp', 'pair'), 'ctx'), parts along dimension 0
- query_grad: bfloat16 [4, 1024, 2048], P(('grp', 'pair'), 'ctx'), parts along dimension 0
- key_grad: bfloat16 [4, 1024, 1024], P(('grp', 'pair'), 'ctx'), parts along dimension 0
- down_gradient: float32 [5376, 16], P('grp'), parts along dimension 0
- up_gradient: float32 [32, 1024], P('grp'), parts along dimension 0
The draws below stay inside these ranges and needn't reach their ends.
There are 2 independent parts, one for each index of `grp`. The reference program is written for one: setup_inputs(seed, part) draws one part's arguments, and reference() takes and returns one part's arrays. A program takes and returns all parts, laid end to end along the dimension named above; an argument that names none is the same for every part. Nothing has to cross between parts.
Inputs may be any that keep to these rules, and one draw needn't show every extreme that they name: `token_pair_index`: along each sequence the ids never fall; both sequences hold every id, each segment at most 1017 tokens and one exactly 1017.
All inputs are finite; a program needn't handle non-finite values.
Results may differ from the reference program's by a relative error of at most 0.03.
Values may be sent and summed in bfloat16 or wider, within the bound.
No kernel may reach another device: no remote copies, remote signals or barrier semaphores. Data moves between devices by JAX's collectives and lax.ppermute only.
A program may use at most 128 MiB of HBM per device.

```python
import math
import jax
import jax.numpy as jnp
import numpy as np
from jax import lax

MODEL_FEATURES = 2688
HQ = 16
KEY_VALUE_HEADS = 8
HEAD_SIZE = 128
ADAPTER_RANK = 16
WINDOW = 1024
SEGS = 8
TOK_DEV = 128
TOKENS = 1024
SEG_MOST = 1017
N_CTX = 8


def logp_pair(key):
    base = jax.random.fold_in(key, 101)
    first, second = jax.random.split(base)
    policy = -jax.random.uniform(first, (2, TOKENS), jnp.float32, 0.05, 6.0)
    ramp = jnp.arange(TOKENS, dtype=jnp.float32) / TOKENS
    noise = jax.random.normal(second, (2, TOKENS), jnp.float32) * 0.08 * (1.0 + 2.0 * ramp)
    reference = -jnp.abs(policy + noise)
    return (policy, reference)


def draw_policy_logprob(key, part):
    return logp_pair(key)[0]


def draw_reference_logprob(key, part):
    return logp_pair(key)[1]


def query_key_pair(key):
    base = jax.random.fold_in(key, 202)
    first, second = jax.random.split(base)
    query = jnp.clip(jax.random.normal(first, (2, TOKENS, HQ * HEAD_SIZE), jnp.float32), -6.0, 6.0)
    key_vals = jnp.clip(jax.random.normal(second, (2, TOKENS, KEY_VALUE_HEADS * HEAD_SIZE), jnp.float32), -6.0, 6.0)
    return (query, key_vals)


def draw_queries(key, part):
    return query_key_pair(key)[0].astype(jnp.bfloat16)


def draw_keys(key, part):
    return query_key_pair(key)[1].astype(jnp.bfloat16)


def levels(stream_key, shape, cuts, smallest, high):
    factor_of, own = 1.0, jax.random.fold_in(stream_key, 6)
    for axis_at, blocks in cuts:
        steps = jnp.exp(jax.random.uniform(jax.random.fold_in(own, axis_at), (blocks,), jnp.float32, smallest / len(cuts), high / len(cuts)))
        factor_of = factor_of * jnp.repeat(steps, shape[axis_at] // blocks).reshape([-1 if axis == axis_at else 1 for axis in range(len(shape))])
    return factor_of


def split_up(count, total, bound, skew):
    weights = [(1 << 20) // math.isqrt(rank ** skew) + 1 for rank in range(2, count + 1)]
    surplus, holding = total - bound - (count - 1), [1] * (count - 1)
    while surplus > 0:
        candidates = [i for i in range(count - 1) if holding[i] < bound]
        whole, left = sum([weights[i] for i in candidates]), surplus
        for i in candidates:
            addition = min(bound - holding[i], max(1, left * weights[i] // whole), surplus)
            holding[i] = holding[i] + addition
            surplus = surplus - addition
    return np.array([bound] + holding)


def ragged(key, number_of, total, limit, skew):
    if number_of == 2:
        one = jax.random.randint(key, (), max(1, total - limit), min(limit, total - 1) + 1)
        return jnp.stack([one, total - one])
    tallies = jnp.asarray(split_up(number_of, total, limit, skew), jnp.int32)
    couples = (number_of - 1) // 2
    source_of, taker = tallies[1:1 + 2 * couples:2], tallies[2:2 + 2 * couples:2]
    room = jnp.minimum(source_of - 1, limit - taker)
    shifted = jax.random.randint(jax.random.fold_in(key, 1), (couples,), 0, 1 << 20) % (room + 1)
    tallies = tallies.at[1:1 + 2 * couples:2].set(source_of - shifted).at[2:2 + 2 * couples:2].set(taker + shifted)
    return tallies[jax.random.permutation(jax.random.fold_in(key, 2), number_of)]


def centred(rng, shape, scale, most, shards=(), held_as=jnp.bfloat16):
    array = scale * jax.random.normal(rng, shape, jnp.float32)
    if shards:
        array = array * levels(rng, shape, shards, -0.22, 0.18)
    return jnp.clip(array, -most, most).astype(held_as)


def setup_inputs(seed: int = 0, part: int = 0) -> dict:
    seeds = jax.random.split(jax.random.key(seed), 11)
    part_keys = jax.random.split(jax.random.fold_in(seeds[10], part), 11)
    return {
        "normed_input": centred(part_keys[0], (2, TOKENS, MODEL_FEATURES), 1.0, 6.0, ((0, 2), (1, 8))),
        "queries": draw_queries(jax.random.fold_in(jax.random.fold_in(seeds[10], part), 71), part),
        "keys": draw_keys(jax.random.fold_in(jax.random.fold_in(seeds[10], part), 71), part),
        "value_projection": centred(seeds[3], (MODEL_FEATURES, KEY_VALUE_HEADS * HEAD_SIZE), MODEL_FEATURES ** -0.5, 0.125, ((0, 8),)),
        "adapter_down": centred(seeds[4], (MODEL_FEATURES, ADAPTER_RANK), MODEL_FEATURES ** -0.5, 0.125),
        "adapter_up": centred(seeds[5], (ADAPTER_RANK, KEY_VALUE_HEADS * HEAD_SIZE), ADAPTER_RANK ** -0.5, 1.5),
        "output_gradient": centred(part_keys[6], (2, TOKENS, HQ * HEAD_SIZE), 1.0, 6.0, ((0, 2), (1, 8))),
        "policy_logprob": draw_policy_logprob(jax.random.fold_in(jax.random.fold_in(seeds[10], part), 71), part),
        "reference_logprob": draw_reference_logprob(jax.random.fold_in(jax.random.fold_in(seeds[10], part), 71), part),
        "token_pair_index": jax.vmap(lambda own: jnp.searchsorted(jnp.cumsum(ragged(own, SEGS, TOKENS, SEG_MOST, 1)), jnp.arange(TOKENS), side="right"))(jax.random.split(part_keys[9], 2)).reshape((2, TOKENS)).astype(jnp.int32),
    }


DPO_BETA = 0.1
LOSS_SCALE = 256.0
ADAPTER_SCALE = 2.0
ATTN_SCALE = 168.0 ** -0.5
NEG_FILL = -1e30


def sequence_sweep(hidden_rows, query_sequence, key_sequence, output_sequence, segment_labels, token_coefficient, value_projection, adapter_down, adapter_up):
    width_kv = KEY_VALUE_HEADS * HEAD_SIZE
    group_size = HQ // KEY_VALUE_HEADS
    span = WINDOW + TOK_DEV
    rank_projection = jnp.dot(hidden_rows, adapter_down, preferred_element_type=jnp.float32).astype(jnp.bfloat16)
    values = (jnp.dot(hidden_rows, value_projection, preferred_element_type=jnp.float32)
              + ADAPTER_SCALE * jnp.dot(rank_projection, adapter_up, preferred_element_type=jnp.float32)).astype(jnp.bfloat16)
    key_pad = jnp.concatenate([jnp.zeros((WINDOW, width_kv), jnp.bfloat16), key_sequence], 0)
    value_pad = jnp.concatenate([jnp.zeros((WINDOW, width_kv), jnp.bfloat16), values], 0)
    seg_pad = jnp.concatenate([jnp.full((WINDOW,), -1, jnp.int32), segment_labels.astype(jnp.int32)], 0)

    def settle(part):
        far_rows = lax.optimization_barrier(part[:WINDOW].astype(jnp.bfloat16))
        return jnp.concatenate([far_rows.astype(jnp.float32), part[WINDOW:]], 0)

    def block_step(accum, block):
        key_acc, value_acc = accum
        block_start = (block * TOK_DEV).astype(jnp.int32)
        query_blk = lax.dynamic_slice_in_dim(query_sequence, block_start, TOK_DEV, 0).reshape(TOK_DEV, KEY_VALUE_HEADS, group_size, HEAD_SIZE).astype(jnp.float32)
        grad_blk = lax.dynamic_slice_in_dim(output_sequence, block_start, TOK_DEV, 0).reshape(TOK_DEV, KEY_VALUE_HEADS, group_size, HEAD_SIZE).astype(jnp.float32)
        key_blk = lax.dynamic_slice_in_dim(key_pad, block_start, span, 0).reshape(span, KEY_VALUE_HEADS, HEAD_SIZE).astype(jnp.float32)
        value_blk = lax.dynamic_slice_in_dim(value_pad, block_start, span, 0).reshape(span, KEY_VALUE_HEADS, HEAD_SIZE).astype(jnp.float32)
        seg_query = lax.dynamic_slice_in_dim(segment_labels.astype(jnp.int32), block_start, TOK_DEV, 0)
        seg_key = lax.dynamic_slice_in_dim(seg_pad, block_start, span, 0)
        coef_blk = lax.dynamic_slice_in_dim(token_coefficient, block_start, TOK_DEV, 0)[None, None, :, None]
        tpos = block_start + jnp.arange(TOK_DEV, dtype=jnp.int32)
        upos = block_start - WINDOW + jnp.arange(span, dtype=jnp.int32)
        allowed = (upos[None, :] <= tpos[:, None]) & (upos[None, :] > tpos[:, None] - WINDOW) & (seg_key[None, :] == seg_query[:, None])
        scores = ATTN_SCALE * jnp.einsum('tjgd,ljd->jgtl', query_blk, key_blk)
        masked = jnp.where(allowed[None, None], scores, NEG_FILL)
        row_max = jnp.max(masked, -1, keepdims=True)
        weights_exp = jnp.where(allowed[None, None], jnp.exp(masked - row_max), 0.0)
        attn_probs = weights_exp / jnp.sum(weights_exp, -1, keepdims=True)
        prob_grad = coef_blk * jnp.einsum('tjgd,ljd->jgtl', grad_blk, value_blk)
        row_delta = jnp.sum(attn_probs * prob_grad, -1, keepdims=True)
        score_grad = (ATTN_SCALE * attn_probs * (prob_grad - row_delta)).astype(jnp.bfloat16)
        query_grad = jnp.einsum('jgtl,ljd->tjgd', score_grad.astype(jnp.float32), key_blk).reshape(TOK_DEV, HQ * HEAD_SIZE).astype(jnp.bfloat16)
        key_part = jnp.einsum('jgtl,tjgd->ljd', score_grad.astype(jnp.float32), query_blk).reshape(span, width_kv)
        weighted = (attn_probs * coef_blk).astype(jnp.bfloat16)
        value_part = jnp.einsum('jgtl,tjgd->ljd', weighted.astype(jnp.float32), grad_blk).reshape(span, width_kv)
        key_acc = lax.dynamic_update_slice_in_dim(key_acc, lax.dynamic_slice_in_dim(key_acc, block_start, span, 0) + settle(key_part), block_start, 0)
        value_acc = lax.dynamic_update_slice_in_dim(value_acc, lax.dynamic_slice_in_dim(value_acc, block_start, span, 0) + settle(value_part), block_start, 0)
        return (key_acc, value_acc), query_grad

    accum_init = (jnp.zeros((TOKENS + WINDOW, width_kv), jnp.float32), jnp.zeros((TOKENS + WINDOW, width_kv), jnp.float32))
    (key_acc, value_acc), query_blocks = lax.scan(block_step, accum_init, jnp.arange(N_CTX, dtype=jnp.int32))
    query_grad = query_blocks.reshape(TOKENS, HQ * HEAD_SIZE)
    key_grad = key_acc[WINDOW:].astype(jnp.bfloat16)
    value_gradient = value_acc[WINDOW:].astype(jnp.bfloat16)
    rank_middle = jnp.dot(value_gradient, adapter_up.T, preferred_element_type=jnp.float32).astype(jnp.bfloat16)
    input_grad = (jnp.dot(value_gradient, value_projection.T, preferred_element_type=jnp.float32)
                  + ADAPTER_SCALE * jnp.dot(rank_middle, adapter_down.T, preferred_element_type=jnp.float32)).astype(jnp.bfloat16)
    up_factor = jnp.dot(rank_projection.T, value_gradient, preferred_element_type=jnp.float32)
    down_factor = jnp.dot(hidden_rows.T, rank_middle, preferred_element_type=jnp.float32)
    return input_grad, query_grad, key_grad, down_factor, up_factor


def reference(normed_input, queries, keys, value_projection, adapter_down, adapter_up, output_gradient, policy_logprob, reference_logprob, token_pair_index):
    diff_sums = jnp.stack([
        jax.ops.segment_sum(policy_logprob[pair_position] - reference_logprob[pair_position], token_pair_index[pair_position], num_segments=SEGS)
        for pair_position in range(2)], 0)
    margin = DPO_BETA * (diff_sums[0] - diff_sums[1])
    sig_term = jax.nn.sigmoid(-margin)
    coef = jnp.stack([-DPO_BETA * LOSS_SCALE * sig_term, DPO_BETA * LOSS_SCALE * sig_term], 0)
    input_list = []
    query_list = []
    key_list = []
    down_gradient = jnp.zeros((MODEL_FEATURES, ADAPTER_RANK), jnp.float32)
    up_gradient = jnp.zeros((ADAPTER_RANK, KEY_VALUE_HEADS * HEAD_SIZE), jnp.float32)
    for pair_position in range(2):
        token_coefficient = coef[pair_position][token_pair_index[pair_position]]
        input_grad, query_grad, key_grad, down_factor, up_factor = sequence_sweep(
            normed_input[pair_position], queries[pair_position], keys[pair_position], output_gradient[pair_position],
            token_pair_index[pair_position], token_coefficient, value_projection, adapter_down, adapter_up)
        input_list.append(input_grad)
        query_list.append(query_grad)
        key_list.append(key_grad)
        down_gradient = down_gradient + down_factor
        up_gradient = up_gradient + up_factor
    down_gradient = ADAPTER_SCALE * down_gradient
    up_gradient = ADAPTER_SCALE * up_gradient
    return (jnp.stack(input_list, 0), jnp.stack(query_list, 0), jnp.stack(key_list, 0), down_gradient, up_gradient)
```

```python
import jax
import jax.numpy as jnp
from jax import lax
from jax.sharding import PartitionSpec as P

HEAD_SIZE = 128
WINDOW = 1024
SEGS = 8


DPO_BETA = 0.1
LOSS_SCALE = 256.0
ADAPTER_SCALE = 2.0
ATTN_SCALE = 168.0 ** (-0.5)
NEG_FILL = -1e30


def from_partner(shard, axis, stride):
    return lax.ppermute(shard, axis, [(i, i ^ 1 << stride) for i in range(lax.axis_size(axis))])


def shifted(block, axis, distance):
    devices = range(lax.axis_size(axis))
    route = [(i - distance, i) for i in devices if i - distance in devices]
    return lax.ppermute(block, axis, route)


def shards(
    normed_input,
    queries,
    keys,
    value_projection,
    adapter_down,
    adapter_up,
    output_gradient,
    policy_logprob,
    reference_logprob,
    token_pair_index,
):
    tok_rows = normed_input.shape[1]
    width_kv = keys.shape[2]
    kv_heads = width_kv // HEAD_SIZE
    group_size = queries.shape[2] // width_kv
    hidden_rows = normed_input[0]
    own_keys = keys[0]
    pair_index = lax.axis_index("pair")
    ctx_index = lax.axis_index("ctx")
    half_cols = width_kv // 2
    own_half = lax.dynamic_slice_in_dim(value_projection, pair_index * half_cols, half_cols, 1)
    rows_half = lax.all_gather(own_half, "ctx", axis=0, tiled=True)
    full_weight = lax.all_gather(rows_half, "pair", axis=1, tiled=True)
    rank_projection = jnp.dot(hidden_rows, adapter_down, preferred_element_type=jnp.float32).astype(
        jnp.bfloat16
    )
    values = (
        jnp.dot(hidden_rows, full_weight, preferred_element_type=jnp.float32)
        + ADAPTER_SCALE * jnp.dot(rank_projection, adapter_up, preferred_element_type=jnp.float32)
    ).astype(jnp.bfloat16)
    segment_labels = token_pair_index[0]
    seg_table = (segment_labels[:, None] == jnp.arange(SEGS, dtype=jnp.int32)[None, :]).astype(
        jnp.float32
    )
    log_gap = policy_logprob[0] - reference_logprob[0]
    part_diff = jnp.sum(seg_table * log_gap[:, None], 0)
    part_count = jnp.sum(seg_table, 0)
    own_diff, counts = lax.psum((part_diff, part_count), "ctx")
    other_diff = from_partner(own_diff, "pair", 0)
    direction = 1.0 - 2.0 * pair_index.astype(jnp.float32)
    margin = DPO_BETA * (direction * (own_diff - other_diff))
    coef = -direction * DPO_BETA * LOSS_SCALE * jax.nn.sigmoid(-margin)
    starts = jnp.cumsum(counts) - counts
    tok_start = jnp.sum(seg_table * starts[None, :], 1).astype(jnp.int32)
    token_coefficient = jnp.sum(seg_table * coef[None, :], 1)
    halo_blocks = min(WINDOW // tok_rows, lax.axis_size("ctx") - 1)
    key_blocks = []
    value_blocks = []
    for distance in range(halo_blocks, 0, -1):
        got_keys, got_values = shifted((own_keys, values), "ctx", distance)
        key_blocks.append(got_keys)
        value_blocks.append(got_values)
    all_keys = jnp.concatenate(key_blocks + [own_keys], 0)
    all_values = jnp.concatenate(value_blocks + [values], 0)
    span = all_keys.shape[0]
    tpos = ctx_index * tok_rows + jnp.arange(tok_rows, dtype=jnp.int32)
    upos = ctx_index * tok_rows - halo_blocks * tok_rows + jnp.arange(span, dtype=jnp.int32)
    allowed = (
        (upos[None, :] <= tpos[:, None])
        & (upos[None, :] > tpos[:, None] - WINDOW)
        & (upos[None, :] >= tok_start[:, None])
    )
    coef_rows = token_coefficient[None, :, None]
    query_rows = queries[0].reshape(tok_rows, kv_heads, group_size, HEAD_SIZE)
    grad_rows = output_gradient[0].reshape(tok_rows, kv_heads, group_size, HEAD_SIZE)
    key_rows = all_keys.reshape(span, kv_heads, HEAD_SIZE)
    value_rows = all_values.reshape(span, kv_heads, HEAD_SIZE)
    scores = ATTN_SCALE * jnp.einsum(
        "tjgd,ljd->jgtl", query_rows, key_rows, preferred_element_type=jnp.float32
    )
    masked = jnp.where(allowed[None, None], scores, NEG_FILL)
    row_max = jnp.max(masked, -1, keepdims=True)
    weights_exp = jnp.where(allowed[None, None], jnp.exp(masked - row_max), 0.0)
    attn_probs = weights_exp / jnp.sum(weights_exp, -1, keepdims=True)
    prob_grad = coef_rows[None] * jnp.einsum(
        "tjgd,ljd->jgtl", grad_rows, value_rows, preferred_element_type=jnp.float32
    )
    row_delta = jnp.sum(attn_probs * prob_grad, -1, keepdims=True)
    score_grad = (ATTN_SCALE * attn_probs * (prob_grad - row_delta)).astype(jnp.bfloat16)
    query_grad = jnp.einsum(
        "jgtl,ljd->tjgd", score_grad, key_rows, preferred_element_type=jnp.float32
    ).astype(jnp.bfloat16).reshape(tok_rows, kv_heads * group_size * HEAD_SIZE)
    key_parts = jnp.einsum(
        "jgtl,tjgd->ljd", score_grad, query_rows, preferred_element_type=jnp.float32
    ).reshape(span, width_kv)
    weighted = (attn_probs * coef_rows[None]).astype(jnp.bfloat16)
    value_parts = jnp.einsum(
        "jgtl,tjgd->ljd", weighted, grad_rows, preferred_element_type=jnp.float32
    ).reshape(span, width_kv)
    key_total = key_parts[halo_blocks * tok_rows :]
    value_total = value_parts[halo_blocks * tok_rows :]
    for distance in range(1, halo_blocks + 1):
        block_start = (halo_blocks - distance) * tok_rows
        send_keys = key_parts[block_start : block_start + tok_rows].astype(jnp.bfloat16)
        send_values = value_parts[block_start : block_start + tok_rows].astype(jnp.bfloat16)
        back_keys, back_values = shifted((send_keys, send_values), "ctx", -distance)
        key_total = key_total + back_keys.astype(jnp.float32)
        value_total = value_total + back_values.astype(jnp.float32)
    key_grad = key_total.astype(jnp.bfloat16)
    value_gradient = value_total.astype(jnp.bfloat16)
    rank_middle = jnp.einsum(
        "sj,zj->sz", value_gradient, adapter_up, preferred_element_type=jnp.float32
    ).astype(jnp.bfloat16)
    input_grad = (
        jnp.einsum("tk,dk->td", value_gradient, full_weight, preferred_element_type=jnp.float32)
        + ADAPTER_SCALE
        * jnp.einsum("pb,wb->pw", rank_middle, adapter_down, preferred_element_type=jnp.float32)
    ).astype(jnp.bfloat16)
    up_factor = ADAPTER_SCALE * jnp.einsum(
        "tr,tk->rk", rank_projection, value_gradient, preferred_element_type=jnp.float32
    )
    down_factor = ADAPTER_SCALE * jnp.einsum(
        "td,tr->dr", hidden_rows, rank_middle, preferred_element_type=jnp.float32
    )
    down_gradient, up_gradient = lax.psum((down_factor, up_factor), ("ctx", "pair"))
    return (input_grad[None], query_grad[None], key_grad[None], down_gradient, up_gradient)


def solution(mesh):
    return jax.shard_map(
        shards,
        mesh=mesh,
        in_specs=(
            P(("grp", "pair"), "ctx", None),
            P(("grp", "pair"), "ctx", None),
            P(("grp", "pair"), "ctx", None),
            P("ctx", None),
            P(),
            P(),
            P(("grp", "pair"), "ctx", None),
            P(("grp", "pair"), "ctx"),
            P(("grp", "pair"), "ctx"),
            P(("grp", "pair"), "ctx"),
        ),
        out_specs=(
            P(("grp", "pair"), "ctx", None),
            P(("grp", "pair"), "ctx", None),
            P(("grp", "pair"), "ctx", None),
            P("grp", None),
            P("grp", None),
        ),
        check_vma=False,
    )
```

```python
import jax
import jax.numpy as jnp
from jax import lax
from jax.sharding import PartitionSpec as P

HEAD_SIZE = 128
WINDOW = 1024
SEGS = 8


DPO_BETA = 0.1
LOSS_SCALE = 256.0
ADAPTER_SCALE = 2.0
ATTN_SCALE = 168.0 ** (-0.5)
NEG_FILL = -1e30


def from_partner(shard, axis, stride):
    return lax.ppermute(shard, axis, [(i, i ^ 1 << stride) for i in range(lax.axis_size(axis))])


def shifted(block, axis, distance):
    devices = range(lax.axis_size(axis))
    route = [(i - distance, i) for i in devices if i - distance in devices]
    return lax.ppermute(block, axis, route)


def shards(
    normed_input,
    queries,
    keys,
    value_projection,
    adapter_down,
    adapter_up,
    output_gradient,
    policy_logprob,
    reference_logprob,
    token_pair_index,
):
    tok_rows = normed_input.shape[1]
    width_kv = keys.shape[2]
    kv_heads = width_kv // HEAD_SIZE
    group_size = queries.shape[2] // width_kv
    hidden_rows = normed_input[0]
    own_keys = keys[0]
    pair_index = lax.axis_index("pair")
    ctx_index = lax.axis_index("ctx")
    half_cols = width_kv // 2
    own_half = lax.dynamic_slice_in_dim(value_projection, pair_index * half_cols, half_cols, 1)
    rows_half = lax.all_gather(own_half, "ctx", axis=0, tiled=True)
    full_weight = lax.all_gather(rows_half, "pair", axis=1, tiled=True)
    rank_projection = jnp.dot(hidden_rows, adapter_down, preferred_element_type=jnp.float32).astype(
        jnp.bfloat16
    )
    values = (
        jnp.dot(hidden_rows, full_weight, preferred_element_type=jnp.float32)
        + ADAPTER_SCALE * jnp.dot(rank_projection, adapter_up, preferred_element_type=jnp.float32)
    ).astype(jnp.bfloat16)
    segment_labels = token_pair_index[0]
    seg_table = (segment_labels[:, None] == jnp.arange(SEGS, dtype=jnp.int32)[None, :]).astype(
        jnp.float32
    )
    log_gap = policy_logprob[0] - reference_logprob[0]
    part_diff = jnp.sum(seg_table * log_gap[:, None], 0)
    part_count = jnp.sum(seg_table, 0)
    own_diff, counts = lax.psum((part_diff, part_count), "ctx")
    other_diff = from_partner(own_diff, "pair", 0)
    direction = 1.0 - 2.0 * pair_index.astype(jnp.float32)
    margin = DPO_BETA * (direction * (own_diff - other_diff))
    coef = -direction * DPO_BETA * LOSS_SCALE * jax.nn.sigmoid(-margin)
    starts = jnp.cumsum(counts) - counts
    tok_start = jnp.sum(seg_table * starts[None, :], 1).astype(jnp.int32)
    token_coefficient = jnp.sum(seg_table * coef[None, :], 1)
    halo_blocks = min(WINDOW // tok_rows, lax.axis_size("ctx") - 1)
    key_blocks = []
    value_blocks = []
    for distance in range(halo_blocks, 0, -1):
        key_blocks.append(shifted(own_keys, "ctx", distance))
        value_blocks.append(shifted(values, "ctx", distance))
    all_keys = jnp.concatenate(key_blocks + [own_keys], 0)
    all_keys, own_values = lax.optimization_barrier((all_keys, values))
    all_values = jnp.concatenate(value_blocks + [own_values], 0)
    span = all_keys.shape[0]
    tpos = ctx_index * tok_rows + jnp.arange(tok_rows, dtype=jnp.int32)
    upos = ctx_index * tok_rows - halo_blocks * tok_rows + jnp.arange(span, dtype=jnp.int32)
    allowed = (
        (upos[None, :] <= tpos[:, None])
        & (upos[None, :] > tpos[:, None] - WINDOW)
        & (upos[None, :] >= tok_start[:, None])
    )
    coef_rows = token_coefficient[None, :, None]
    query_rows = queries[0].reshape(tok_rows, kv_heads, group_size, HEAD_SIZE)
    grad_rows = output_gradient[0].reshape(tok_rows, kv_heads, group_size, HEAD_SIZE)
    key_rows = all_keys.reshape(span, kv_heads, HEAD_SIZE)
    value_rows = all_values.reshape(span, kv_heads, HEAD_SIZE)
    scores = ATTN_SCALE * jnp.einsum(
        "tjgd,ljd->jgtl", query_rows, key_rows, preferred_element_type=jnp.float32
    )
    masked = jnp.where(allowed[None, None], scores, NEG_FILL)
    row_max = jnp.max(masked, -1, keepdims=True)
    weights_exp = jnp.where(allowed[None, None], jnp.exp(masked - row_max), 0.0)
    attn_probs = weights_exp / jnp.sum(weights_exp, -1, keepdims=True)
    prob_grad = coef_rows[None] * jnp.einsum(
        "tjgd,ljd->jgtl", grad_rows, value_rows, preferred_element_type=jnp.float32
    )
    row_delta = jnp.sum(attn_probs * prob_grad, -1, keepdims=True)
    score_grad = (ATTN_SCALE * attn_probs * (prob_grad - row_delta)).astype(jnp.bfloat16)
    query_grad = jnp.einsum(
        "jgtl,ljd->tjgd", score_grad, key_rows, preferred_element_type=jnp.float32
    ).astype(jnp.bfloat16).reshape(tok_rows, kv_heads * group_size * HEAD_SIZE)
    key_parts = jnp.einsum(
        "jgtl,tjgd->ljd", score_grad, query_rows, preferred_element_type=jnp.float32
    ).reshape(span, width_kv)
    weighted = (attn_probs * coef_rows[None]).astype(jnp.bfloat16)
    value_parts = jnp.einsum(
        "jgtl,tjgd->ljd", weighted, grad_rows, preferred_element_type=jnp.float32
    ).reshape(span, width_kv)
    key_total = key_parts[halo_blocks * tok_rows :]
    value_total = value_parts[halo_blocks * tok_rows :]
    for distance in range(1, halo_blocks + 1):
        block_start = (halo_blocks - distance) * tok_rows
        send_keys = key_parts[block_start : block_start + tok_rows].astype(jnp.bfloat16)
        send_values = value_parts[block_start : block_start + tok_rows].astype(jnp.bfloat16)
        back_keys, back_values = shifted((send_keys, send_values), "ctx", -distance)
        key_total = key_total + back_keys.astype(jnp.float32)
        value_total = value_total + back_values.astype(jnp.float32)
    key_grad = key_total.astype(jnp.bfloat16)
    value_gradient = value_total.astype(jnp.bfloat16)
    rank_middle = jnp.einsum(
        "sj,zj->sz", value_gradient, adapter_up, preferred_element_type=jnp.float32
    ).astype(jnp.bfloat16)
    input_grad = (
        jnp.einsum("tk,dk->td", value_gradient, full_weight, preferred_element_type=jnp.float32)
        + ADAPTER_SCALE
        * jnp.einsum("pb,wb->pw", rank_middle, adapter_down, preferred_element_type=jnp.float32)
    ).astype(jnp.bfloat16)
    up_factor = ADAPTER_SCALE * jnp.einsum(
        "tr,tk->rk", rank_projection, value_gradient, preferred_element_type=jnp.float32
    )
    down_factor = ADAPTER_SCALE * jnp.einsum(
        "td,tr->dr", hidden_rows, rank_middle, preferred_element_type=jnp.float32
    )
    down_gradient, up_gradient = lax.psum((down_factor, up_factor), ("ctx", "pair"))
    return (input_grad[None], query_grad[None], key_grad[None], down_gradient, up_gradient)


def solution(mesh):
    return jax.shard_map(
        shards,
        mesh=mesh,
        in_specs=(
            P(("grp", "pair"), "ctx", None),
            P(("grp", "pair"), "ctx", None),
            P(("grp", "pair"), "ctx", None),
            P("ctx", None),
            P(),
            P(),
            P(("grp", "pair"), "ctx", None),
            P(("grp", "pair"), "ctx"),
            P(("grp", "pair"), "ctx"),
            P(("grp", "pair"), "ctx"),
        ),
        out_specs=(
            P(("grp", "pair"), "ctx", None),
            P(("grp", "pair"), "ctx", None),
            P(("grp", "pair"), "ctx", None),
            P("grp", None),
            P("grp", None),
        ),
        check_vma=False,
    )
```

```python
import jax
import jax.numpy as jnp
from jax import lax
from jax.sharding import PartitionSpec as P

HEAD_SIZE = 128
WINDOW = 1024
SEGS = 8


DPO_BETA = 0.1
LOSS_SCALE = 256.0
ADAPTER_SCALE = 2.0
ATTN_SCALE = 168.0 ** (-0.5)
NEG_FILL = -1e30


def from_partner(shard, axis, stride):
    return lax.ppermute(shard, axis, [(i, i ^ 1 << stride) for i in range(lax.axis_size(axis))])


def butterfly_sum(parts, axes):
    for axis in axes:
        size = lax.axis_size(axis)
        if size & (size - 1):
            parts = lax.psum(parts, axis)
            continue
        stride = 0
        while 1 << stride < size:
            got = from_partner(parts, axis, stride)
            parts = jax.tree.map(jnp.add, parts, got)
            stride += 1
    return parts


def shifted(block, axis, distance):
    devices = range(lax.axis_size(axis))
    route = [(i - distance, i) for i in devices if i - distance in devices]
    return lax.ppermute(block, axis, route)


def shards(
    normed_input,
    queries,
    keys,
    value_projection,
    adapter_down,
    adapter_up,
    output_gradient,
    policy_logprob,
    reference_logprob,
    token_pair_index,
):
    tok_rows = normed_input.shape[1]
    width_kv = keys.shape[2]
    kv_heads = width_kv // HEAD_SIZE
    group_size = queries.shape[2] // width_kv
    hidden_rows = normed_input[0]
    own_keys = keys[0]
    pair_index = lax.axis_index("pair")
    ctx_index = lax.axis_index("ctx")
    half_cols = width_kv // 2
    own_half = lax.dynamic_slice_in_dim(value_projection, pair_index * half_cols, half_cols, 1)
    rows_half = lax.all_gather(own_half, "ctx", axis=0, tiled=True)
    full_weight = lax.all_gather(rows_half, "pair", axis=1, tiled=True)
    rank_projection = jnp.dot(hidden_rows, adapter_down, preferred_element_type=jnp.float32).astype(
        jnp.bfloat16
    )
    values = (
        jnp.dot(hidden_rows, full_weight, preferred_element_type=jnp.float32)
        + ADAPTER_SCALE * jnp.dot(rank_projection, adapter_up, preferred_element_type=jnp.float32)
    ).astype(jnp.bfloat16)
    segment_labels = token_pair_index[0]
    seg_table = (segment_labels[:, None] == jnp.arange(SEGS, dtype=jnp.int32)[None, :]).astype(
        jnp.float32
    )
    log_gap = policy_logprob[0] - reference_logprob[0]
    part_diff = jnp.sum(seg_table * log_gap[:, None], 0)
    part_count = jnp.sum(seg_table, 0)
    own_diff, counts = butterfly_sum((part_diff, part_count), ("ctx",))
    other_diff = from_partner(own_diff, "pair", 0)
    direction = 1.0 - 2.0 * pair_index.astype(jnp.float32)
    margin = DPO_BETA * (direction * (own_diff - other_diff))
    coef = -direction * DPO_BETA * LOSS_SCALE * jax.nn.sigmoid(-margin)
    starts = jnp.cumsum(counts) - counts
    tok_start = jnp.sum(seg_table * starts[None, :], 1).astype(jnp.int32)
    token_coefficient = jnp.sum(seg_table * coef[None, :], 1)
    halo_blocks = min(WINDOW // tok_rows, lax.axis_size("ctx") - 1)
    key_blocks = []
    value_blocks = []
    for distance in range(halo_blocks, 0, -1):
        key_blocks.append(shifted(own_keys, "ctx", distance))
        value_blocks.append(shifted(values, "ctx", distance))
    all_keys = jnp.concatenate(key_blocks + [own_keys], 0)
    all_keys, own_values = lax.optimization_barrier((all_keys, values))
    all_values = jnp.concatenate(value_blocks + [own_values], 0)
    span = all_keys.shape[0]
    tpos = ctx_index * tok_rows + jnp.arange(tok_rows, dtype=jnp.int32)
    upos = ctx_index * tok_rows - halo_blocks * tok_rows + jnp.arange(span, dtype=jnp.int32)
    allowed = (
        (upos[None, :] <= tpos[:, None])
        & (upos[None, :] > tpos[:, None] - WINDOW)
        & (upos[None, :] >= tok_start[:, None])
    )
    coef_rows = token_coefficient[None, :, None]
    query_rows = queries[0].reshape(tok_rows, kv_heads, group_size, HEAD_SIZE)
    grad_rows = output_gradient[0].reshape(tok_rows, kv_heads, group_size, HEAD_SIZE)
    key_rows = all_keys.reshape(span, kv_heads, HEAD_SIZE)
    value_rows = all_values.reshape(span, kv_heads, HEAD_SIZE)
    scores = ATTN_SCALE * jnp.einsum(
        "tjgd,ljd->jgtl", query_rows, key_rows, preferred_element_type=jnp.float32
    )
    masked = jnp.where(allowed[None, None], scores, NEG_FILL)
    row_max = jnp.max(masked, -1, keepdims=True)
    weights_exp = jnp.where(allowed[None, None], jnp.exp(masked - row_max), 0.0)
    attn_probs = weights_exp / jnp.sum(weights_exp, -1, keepdims=True)
    prob_grad = coef_rows[None] * jnp.einsum(
        "tjgd,ljd->jgtl", grad_rows, value_rows, preferred_element_type=jnp.float32
    )
    row_delta = jnp.sum(attn_probs * prob_grad, -1, keepdims=True)
    score_grad = (ATTN_SCALE * attn_probs * (prob_grad - row_delta)).astype(jnp.bfloat16)
    query_grad = jnp.einsum(
        "jgtl,ljd->tjgd", score_grad, key_rows, preferred_element_type=jnp.float32
    ).astype(jnp.bfloat16).reshape(tok_rows, kv_heads * group_size * HEAD_SIZE)
    key_parts = jnp.einsum(
        "jgtl,tjgd->ljd", score_grad, query_rows, preferred_element_type=jnp.float32
    ).reshape(span, width_kv)
    weighted = (attn_probs * coef_rows[None]).astype(jnp.bfloat16)
    value_parts = jnp.einsum(
        "jgtl,tjgd->ljd", weighted, grad_rows, preferred_element_type=jnp.float32
    ).reshape(span, width_kv)
    key_total = key_parts[halo_blocks * tok_rows :]
    value_total = value_parts[halo_blocks * tok_rows :]
    for distance in range(1, halo_blocks + 1):
        block_start = (halo_blocks - distance) * tok_rows
        send_keys = key_parts[block_start : block_start + tok_rows].astype(jnp.bfloat16)
        send_values = value_parts[block_start : block_start + tok_rows].astype(jnp.bfloat16)
        back_keys, back_values = shifted((send_keys, send_values), "ctx", -distance)
        key_total = key_total + back_keys.astype(jnp.float32)
        value_total = value_total + back_values.astype(jnp.float32)
    key_grad = key_total.astype(jnp.bfloat16)
    value_gradient = value_total.astype(jnp.bfloat16)
    rank_middle = jnp.einsum(
        "sj,zj->sz", value_gradient, adapter_up, preferred_element_type=jnp.float32
    ).astype(jnp.bfloat16)
    input_grad = (
        jnp.einsum("tk,dk->td", value_gradient, full_weight, preferred_element_type=jnp.float32)
        + ADAPTER_SCALE
        * jnp.einsum("pb,wb->pw", rank_middle, adapter_down, preferred_element_type=jnp.float32)
    ).astype(jnp.bfloat16)
    up_factor = ADAPTER_SCALE * jnp.einsum(
        "tr,tk->rk", rank_projection, value_gradient, preferred_element_type=jnp.float32
    )
    down_factor = ADAPTER_SCALE * jnp.einsum(
        "td,tr->dr", hidden_rows, rank_middle, preferred_element_type=jnp.float32
    )
    down_gradient, up_gradient = butterfly_sum((down_factor, up_factor), ("pair", "ctx"))
    return (input_grad[None], query_grad[None], key_grad[None], down_gradient, up_gradient)


def solution(mesh):
    return jax.shard_map(
        shards,
        mesh=mesh,
        in_specs=(
            P(("grp", "pair"), "ctx", None),
            P(("grp", "pair"), "ctx", None),
            P(("grp", "pair"), "ctx", None),
            P("ctx", None),
            P(),
            P(),
            P(("grp", "pair"), "ctx", None),
            P(("grp", "pair"), "ctx"),
            P(("grp", "pair"), "ctx"),
            P(("grp", "pair"), "ctx"),
        ),
        out_specs=(
            P(("grp", "pair"), "ctx", None),
            P(("grp", "pair"), "ctx", None),
            P(("grp", "pair"), "ctx", None),
            P("grp", None),
            P("grp", None),
        ),
        check_vma=False,
    )
```

```python
import jax
import jax.numpy as jnp
from jax import lax
from jax.sharding import PartitionSpec as P

HEAD_SIZE = 128
WINDOW = 1024
SEGS = 8


DPO_BETA = 0.1
LOSS_SCALE = 256.0
ADAPTER_SCALE = 2.0
ATTN_SCALE = 168.0 ** (-0.5)
NEG_FILL = -1e30


def from_partner(shard, axis, stride):
    return lax.ppermute(shard, axis, [(i, i ^ 1 << stride) for i in range(lax.axis_size(axis))])


def butterfly_sum(parts, axes):
    for axis in axes:
        size = lax.axis_size(axis)
        if size & (size - 1):
            parts = lax.psum(parts, axis)
            continue
        stride = 0
        while 1 << stride < size:
            got = from_partner(parts, axis, stride)
            parts = jax.tree.map(jnp.add, parts, got)
            stride += 1
    return parts


def tree_spread(block, levels):
    count = 2 * levels
    climbed = []
    held = block
    for step in range(1, levels):
        held = lax.ppermute(held, "ctx", [(c - 2, c) for c in range(2 * step, count)])
        climbed.append(held)
    crossed = [lax.ppermute(block, "ctx", [(c - 1, c) for c in range(1, count, 2)])]
    for step in range(1, levels):
        crossed.append(
            lax.ppermute(climbed[step - 1], "ctx", [(c ^ 1, c) for c in range(2 * step, count)])
        )
    return climbed + crossed


def tree_slots(ctx_index, levels):
    partner = jnp.bitwise_xor(ctx_index, 1)
    owners, valid = [], []
    for step in range(1, levels):
        owners.append(ctx_index - 2 * step)
        valid.append(ctx_index >= 2 * step)
    owners.append(ctx_index - 1)
    valid.append(ctx_index % 2 == 1)
    for step in range(1, levels):
        owners.append(partner - 2 * step)
        valid.append(ctx_index >= 2 * step)
    return owners, valid


def tree_return(slot_parts, levels):
    count = 2 * levels
    climbed = slot_parts[: levels - 1]
    crossed = slot_parts[levels - 1 :]
    back = [lax.ppermute(crossed[0], "ctx", [(c, c - 1) for c in range(1, count, 2)])]
    for step in range(1, levels):
        back.append(
            lax.ppermute(crossed[step], "ctx", [(c, c ^ 1) for c in range(2 * step, count)])
        )
    total = back[0].astype(jnp.float32)
    carry = None
    for step in range(levels - 1, 0, -1):
        acc = climbed[step - 1].astype(jnp.float32) + back[step].astype(jnp.float32)
        if carry is not None:
            acc = acc + carry.astype(jnp.float32)
        carry = lax.ppermute(
            acc.astype(jnp.bfloat16), "ctx", [(c, c - 2) for c in range(2 * step, count)]
        )
    if carry is not None:
        total = total + carry.astype(jnp.float32)
    return total


def shifted(block, axis, distance):
    devices = range(lax.axis_size(axis))
    route = [(i - distance, i) for i in devices if i - distance in devices]
    return lax.ppermute(block, axis, route)


def shards(
    normed_input,
    queries,
    keys,
    value_projection,
    adapter_down,
    adapter_up,
    output_gradient,
    policy_logprob,
    reference_logprob,
    token_pair_index,
):
    tok_rows = normed_input.shape[1]
    width_kv = keys.shape[2]
    kv_heads = width_kv // HEAD_SIZE
    group_size = queries.shape[2] // width_kv
    hidden_rows = normed_input[0]
    own_keys = keys[0]
    pair_index = lax.axis_index("pair")
    ctx_index = lax.axis_index("ctx")
    half_cols = width_kv // 2
    own_half = lax.dynamic_slice_in_dim(value_projection, pair_index * half_cols, half_cols, 1)
    rows_half = lax.all_gather(own_half, "ctx", axis=0, tiled=True)
    full_weight = lax.all_gather(rows_half, "pair", axis=1, tiled=True)
    rank_projection = jnp.dot(hidden_rows, adapter_down, preferred_element_type=jnp.float32).astype(
        jnp.bfloat16
    )
    values = (
        jnp.dot(hidden_rows, full_weight, preferred_element_type=jnp.float32)
        + ADAPTER_SCALE * jnp.dot(rank_projection, adapter_up, preferred_element_type=jnp.float32)
    ).astype(jnp.bfloat16)
    segment_labels = token_pair_index[0]
    seg_table = (segment_labels[:, None] == jnp.arange(SEGS, dtype=jnp.int32)[None, :]).astype(
        jnp.float32
    )
    log_gap = policy_logprob[0] - reference_logprob[0]
    part_diff = jnp.sum(seg_table * log_gap[:, None], 0)
    part_count = jnp.sum(seg_table, 0)
    own_diff, counts = butterfly_sum((part_diff, part_count), ("ctx",))
    other_diff = from_partner(own_diff, "pair", 0)
    direction = 1.0 - 2.0 * pair_index.astype(jnp.float32)
    margin = DPO_BETA * (direction * (own_diff - other_diff))
    coef = -direction * DPO_BETA * LOSS_SCALE * jax.nn.sigmoid(-margin)
    starts = jnp.cumsum(counts) - counts
    tok_start = jnp.sum(seg_table * starts[None, :], 1).astype(jnp.int32)
    token_coefficient = jnp.sum(seg_table * coef[None, :], 1)
    ctx_size = lax.axis_size("ctx")
    halo_blocks = min(WINDOW // tok_rows, ctx_size - 1)
    use_tree = halo_blocks == ctx_size - 1 and ctx_size % 2 == 0 and ctx_size >= 4
    levels = ctx_size // 2
    row_iota = jnp.arange(tok_rows, dtype=jnp.int32)
    if use_tree:
        key_blocks = tree_spread(own_keys, levels)
        value_blocks = tree_spread(values, levels)
        owners, valid = tree_slots(ctx_index, levels)
        far = jnp.int32(1 << 30)
        upos = jnp.concatenate(
            [jnp.where(ok, owner * tok_rows + row_iota, far) for owner, ok in zip(owners, valid)]
            + [ctx_index * tok_rows + row_iota],
            0,
        )
    else:
        key_blocks = []
        value_blocks = []
        for distance in range(halo_blocks, 0, -1):
            key_blocks.append(shifted(own_keys, "ctx", distance))
            value_blocks.append(shifted(values, "ctx", distance))
    all_keys = jnp.concatenate(key_blocks + [own_keys], 0)
    all_keys, own_values = lax.optimization_barrier((all_keys, values))
    all_values = jnp.concatenate(value_blocks + [own_values], 0)
    span = all_keys.shape[0]
    tpos = ctx_index * tok_rows + row_iota
    if not use_tree:
        upos = ctx_index * tok_rows - halo_blocks * tok_rows + jnp.arange(span, dtype=jnp.int32)
    allowed = (
        (upos[None, :] <= tpos[:, None])
        & (upos[None, :] > tpos[:, None] - WINDOW)
        & (upos[None, :] >= tok_start[:, None])
    )
    coef_rows = token_coefficient[None, :, None]
    query_rows = queries[0].reshape(tok_rows, kv_heads, group_size, HEAD_SIZE)
    grad_rows = output_gradient[0].reshape(tok_rows, kv_heads, group_size, HEAD_SIZE)
    key_rows = all_keys.reshape(span, kv_heads, HEAD_SIZE)
    value_rows = all_values.reshape(span, kv_heads, HEAD_SIZE)
    scores = ATTN_SCALE * jnp.einsum(
        "tjgd,ljd->jgtl", query_rows, key_rows, preferred_element_type=jnp.float32
    )
    masked = jnp.where(allowed[None, None], scores, NEG_FILL)
    row_max = jnp.max(masked, -1, keepdims=True)
    weights_exp = jnp.where(allowed[None, None], jnp.exp(masked - row_max), 0.0)
    attn_probs = weights_exp / jnp.sum(weights_exp, -1, keepdims=True)
    prob_grad = coef_rows[None] * jnp.einsum(
        "tjgd,ljd->jgtl", grad_rows, value_rows, preferred_element_type=jnp.float32
    )
    row_delta = jnp.sum(attn_probs * prob_grad, -1, keepdims=True)
    score_grad = (ATTN_SCALE * attn_probs * (prob_grad - row_delta)).astype(jnp.bfloat16)
    query_grad = jnp.einsum(
        "jgtl,ljd->tjgd", score_grad, key_rows, preferred_element_type=jnp.float32
    ).astype(jnp.bfloat16).reshape(tok_rows, kv_heads * group_size * HEAD_SIZE)
    key_parts = jnp.einsum(
        "jgtl,tjgd->ljd", score_grad, query_rows, preferred_element_type=jnp.float32
    ).reshape(span, width_kv)
    weighted = (attn_probs * coef_rows[None]).astype(jnp.bfloat16)
    value_parts = jnp.einsum(
        "jgtl,tjgd->ljd", weighted, grad_rows, preferred_element_type=jnp.float32
    ).reshape(span, width_kv)
    key_total = key_parts[halo_blocks * tok_rows :]
    value_total = value_parts[halo_blocks * tok_rows :]
    if use_tree:
        slot_rows = lambda parts: [
            parts[k * tok_rows : (k + 1) * tok_rows].astype(jnp.bfloat16) for k in range(halo_blocks)
        ]
        key_total = key_total + tree_return(slot_rows(key_parts), levels)
        value_total = value_total + tree_return(slot_rows(value_parts), levels)
    else:
        for distance in range(1, halo_blocks + 1):
            block_start = (halo_blocks - distance) * tok_rows
            send_keys = key_parts[block_start : block_start + tok_rows].astype(jnp.bfloat16)
            send_values = value_parts[block_start : block_start + tok_rows].astype(jnp.bfloat16)
            back_keys, back_values = shifted((send_keys, send_values), "ctx", -distance)
            key_total = key_total + back_keys.astype(jnp.float32)
            value_total = value_total + back_values.astype(jnp.float32)
    key_grad = key_total.astype(jnp.bfloat16)
    value_gradient = value_total.astype(jnp.bfloat16)
    rank_middle = jnp.einsum(
        "sj,zj->sz", value_gradient, adapter_up, preferred_element_type=jnp.float32
    ).astype(jnp.bfloat16)
    input_grad = (
        jnp.einsum("tk,dk->td", value_gradient, full_weight, preferred_element_type=jnp.float32)
        + ADAPTER_SCALE
        * jnp.einsum("pb,wb->pw", rank_middle, adapter_down, preferred_element_type=jnp.float32)
    ).astype(jnp.bfloat16)
    up_factor = ADAPTER_SCALE * jnp.einsum(
        "tr,tk->rk", rank_projection, value_gradient, preferred_element_type=jnp.float32
    )
    down_factor = ADAPTER_SCALE * jnp.einsum(
        "td,tr->dr", hidden_rows, rank_middle, preferred_element_type=jnp.float32
    )
    down_gradient, up_gradient = butterfly_sum((down_factor, up_factor), ("pair", "ctx"))
    return (input_grad[None], query_grad[None], key_grad[None], down_gradient, up_gradient)


def solution(mesh):
    return jax.shard_map(
        shards,
        mesh=mesh,
        in_specs=(
            P(("grp", "pair"), "ctx", None),
            P(("grp", "pair"), "ctx", None),
            P(("grp", "pair"), "ctx", None),
            P("ctx", None),
            P(),
            P(),
            P(("grp", "pair"), "ctx", None),
            P(("grp", "pair"), "ctx"),
            P(("grp", "pair"), "ctx"),
            P(("grp", "pair"), "ctx"),
        ),
        out_specs=(
            P(("grp", "pair"), "ctx", None),
            P(("grp", "pair"), "ctx", None),
            P(("grp", "pair"), "ctx", None),
            P("grp", None),
            P("grp", None),
        ),
        check_vma=False,
    )
```

```python
import jax
import jax.numpy as jnp
from jax import lax
from jax.sharding import PartitionSpec as P

HEAD_SIZE = 128
WINDOW = 1024
SEGS = 8


DPO_BETA = 0.1
LOSS_SCALE = 256.0
ADAPTER_SCALE = 2.0
ATTN_SCALE = 168.0 ** (-0.5)
NEG_FILL = -1e30


def from_partner(shard, axis, stride):
    return lax.ppermute(shard, axis, [(i, i ^ 1 << stride) for i in range(lax.axis_size(axis))])


def butterfly_sum(parts, axes):
    for axis in axes:
        size = lax.axis_size(axis)
        if size & (size - 1):
            parts = lax.psum(parts, axis)
            continue
        stride = 0
        while 1 << stride < size:
            got = from_partner(parts, axis, stride)
            parts = jax.tree.map(jnp.add, parts, got)
            stride += 1
    return parts


def tree_spread(block, levels):
    count = 2 * levels
    climbed = []
    held = block
    for step in range(1, levels):
        held = lax.ppermute(held, "ctx", [(c - 2, c) for c in range(2 * step, count)])
        climbed.append(held)
    crossed = [lax.ppermute(block, "ctx", [(c - 1, c) for c in range(1, count, 2)])]
    for step in range(1, levels):
        crossed.append(
            lax.ppermute(climbed[step - 1], "ctx", [(c ^ 1, c) for c in range(2 * step, count)])
        )
    return climbed + crossed


def tree_slots(ctx_index, levels):
    partner = jnp.bitwise_xor(ctx_index, 1)
    owners, valid = [], []
    for step in range(1, levels):
        owners.append(ctx_index - 2 * step)
        valid.append(ctx_index >= 2 * step)
    owners.append(ctx_index - 1)
    valid.append(ctx_index % 2 == 1)
    for step in range(1, levels):
        owners.append(partner - 2 * step)
        valid.append(ctx_index >= 2 * step)
    return owners, valid


def tree_return(slot_parts, levels):
    count = 2 * levels
    climbed = slot_parts[: levels - 1]
    crossed = slot_parts[levels - 1 :]
    back = [lax.ppermute(crossed[0], "ctx", [(c, c - 1) for c in range(1, count, 2)])]
    for step in range(1, levels):
        back.append(
            lax.ppermute(crossed[step], "ctx", [(c, c ^ 1) for c in range(2 * step, count)])
        )
    total = back[0].astype(jnp.float32)
    carry = None
    for step in range(levels - 1, 0, -1):
        acc = climbed[step - 1].astype(jnp.float32) + back[step].astype(jnp.float32)
        if carry is not None:
            acc = acc + carry.astype(jnp.float32)
        carry = lax.ppermute(
            acc.astype(jnp.bfloat16), "ctx", [(c, c - 2) for c in range(2 * step, count)]
        )
    if carry is not None:
        total = total + carry.astype(jnp.float32)
    return total


def shifted(block, axis, distance):
    devices = range(lax.axis_size(axis))
    route = [(i - distance, i) for i in devices if i - distance in devices]
    return lax.ppermute(block, axis, route)


def shards(
    normed_input,
    queries,
    keys,
    value_projection,
    adapter_down,
    adapter_up,
    output_gradient,
    policy_logprob,
    reference_logprob,
    token_pair_index,
):
    tok_rows = normed_input.shape[1]
    width_kv = keys.shape[2]
    kv_heads = width_kv // HEAD_SIZE
    group_size = queries.shape[2] // width_kv
    hidden_rows = normed_input[0]
    own_keys = keys[0]
    pair_index = lax.axis_index("pair")
    ctx_index = lax.axis_index("ctx")
    half_cols = width_kv // 2
    own_half = lax.dynamic_slice_in_dim(value_projection, pair_index * half_cols, half_cols, 1)
    rows_half = lax.all_gather(own_half, "ctx", axis=0, tiled=True)
    full_weight = lax.all_gather(rows_half, "pair", axis=1, tiled=True)
    rank_projection = jnp.dot(hidden_rows, adapter_down, preferred_element_type=jnp.float32).astype(
        jnp.bfloat16
    )
    values = (
        jnp.dot(hidden_rows, full_weight, preferred_element_type=jnp.float32)
        + ADAPTER_SCALE * jnp.dot(rank_projection, adapter_up, preferred_element_type=jnp.float32)
    ).astype(jnp.bfloat16)
    segment_labels = token_pair_index[0]
    seg_table = (segment_labels[:, None] == jnp.arange(SEGS, dtype=jnp.int32)[None, :]).astype(
        jnp.float32
    )
    log_gap = policy_logprob[0] - reference_logprob[0]
    part_diff = jnp.sum(seg_table * log_gap[:, None], 0)
    part_count = jnp.sum(seg_table, 0)
    both_sums = butterfly_sum(jnp.concatenate([part_diff, part_count], 0), ("ctx",))
    own_diff, counts = both_sums[:SEGS], both_sums[SEGS:]
    other_diff = from_partner(own_diff, "pair", 0)
    direction = 1.0 - 2.0 * pair_index.astype(jnp.float32)
    margin = DPO_BETA * (direction * (own_diff - other_diff))
    coef = -direction * DPO_BETA * LOSS_SCALE * jax.nn.sigmoid(-margin)
    starts = jnp.cumsum(counts) - counts
    tok_start = jnp.sum(seg_table * starts[None, :], 1).astype(jnp.int32)
    token_coefficient = jnp.sum(seg_table * coef[None, :], 1)
    ctx_size = lax.axis_size("ctx")
    halo_blocks = min(WINDOW // tok_rows, ctx_size - 1)
    use_tree = halo_blocks == ctx_size - 1 and ctx_size % 2 == 0 and ctx_size >= 4
    levels = ctx_size // 2
    row_iota = jnp.arange(tok_rows, dtype=jnp.int32)
    if use_tree:
        key_blocks = tree_spread(own_keys, levels)
        value_blocks = tree_spread(values, levels)
        owners, valid = tree_slots(ctx_index, levels)
        far = jnp.int32(1 << 30)
        upos = jnp.concatenate(
            [jnp.where(ok, owner * tok_rows + row_iota, far) for owner, ok in zip(owners, valid)]
            + [ctx_index * tok_rows + row_iota],
            0,
        )
    else:
        key_blocks = []
        value_blocks = []
        for distance in range(halo_blocks, 0, -1):
            key_blocks.append(shifted(own_keys, "ctx", distance))
            value_blocks.append(shifted(values, "ctx", distance))
    all_keys = jnp.concatenate(key_blocks + [own_keys], 0)
    all_keys, own_values = lax.optimization_barrier((all_keys, values))
    all_values = jnp.concatenate(value_blocks + [own_values], 0)
    span = all_keys.shape[0]
    tpos = ctx_index * tok_rows + row_iota
    if not use_tree:
        upos = ctx_index * tok_rows - halo_blocks * tok_rows + jnp.arange(span, dtype=jnp.int32)
    allowed = (
        (upos[None, :] <= tpos[:, None])
        & (upos[None, :] > tpos[:, None] - WINDOW)
        & (upos[None, :] >= tok_start[:, None])
    )
    coef_rows = token_coefficient[None, :, None]
    query_rows = queries[0].reshape(tok_rows, kv_heads, group_size, HEAD_SIZE)
    grad_rows = output_gradient[0].reshape(tok_rows, kv_heads, group_size, HEAD_SIZE)
    key_rows = all_keys.reshape(span, kv_heads, HEAD_SIZE)
    value_rows = all_values.reshape(span, kv_heads, HEAD_SIZE)
    scores = ATTN_SCALE * jnp.einsum(
        "tjgd,ljd->jgtl", query_rows, key_rows, preferred_element_type=jnp.float32
    )
    masked = jnp.where(allowed[None, None], scores, NEG_FILL)
    row_max = jnp.max(masked, -1, keepdims=True)
    weights_exp = jnp.where(allowed[None, None], jnp.exp(masked - row_max), 0.0)
    attn_probs = weights_exp / jnp.sum(weights_exp, -1, keepdims=True)
    prob_grad = coef_rows[None] * jnp.einsum(
        "tjgd,ljd->jgtl", grad_rows, value_rows, preferred_element_type=jnp.float32
    )
    row_delta = jnp.sum(attn_probs * prob_grad, -1, keepdims=True)
    score_grad = (ATTN_SCALE * attn_probs * (prob_grad - row_delta)).astype(jnp.bfloat16)
    query_grad = jnp.einsum(
        "jgtl,ljd->tjgd", score_grad, key_rows, preferred_element_type=jnp.float32
    ).astype(jnp.bfloat16).reshape(tok_rows, kv_heads * group_size * HEAD_SIZE)
    key_parts = jnp.einsum(
        "jgtl,tjgd->ljd", score_grad, query_rows, preferred_element_type=jnp.float32
    ).reshape(span, width_kv)
    weighted = (attn_probs * coef_rows[None]).astype(jnp.bfloat16)
    value_parts = jnp.einsum(
        "jgtl,tjgd->ljd", weighted, grad_rows, preferred_element_type=jnp.float32
    ).reshape(span, width_kv)
    key_total = key_parts[halo_blocks * tok_rows :]
    value_total = value_parts[halo_blocks * tok_rows :]
    if use_tree:
        slot_rows = lambda parts: [
            parts[k * tok_rows : (k + 1) * tok_rows].astype(jnp.bfloat16) for k in range(halo_blocks)
        ]
        joined = jnp.concatenate([key_parts, value_parts], 1)
        returned = tree_return(slot_rows(joined), levels)
        key_total = key_total + returned[:, :width_kv]
        value_total = value_total + returned[:, width_kv:]
    else:
        for distance in range(1, halo_blocks + 1):
            block_start = (halo_blocks - distance) * tok_rows
            send_keys = key_parts[block_start : block_start + tok_rows].astype(jnp.bfloat16)
            send_values = value_parts[block_start : block_start + tok_rows].astype(jnp.bfloat16)
            back_keys, back_values = shifted((send_keys, send_values), "ctx", -distance)
            key_total = key_total + back_keys.astype(jnp.float32)
            value_total = value_total + back_values.astype(jnp.float32)
    key_grad = key_total.astype(jnp.bfloat16)
    value_gradient = value_total.astype(jnp.bfloat16)
    rank_middle = jnp.einsum(
        "sj,zj->sz", value_gradient, adapter_up, preferred_element_type=jnp.float32
    ).astype(jnp.bfloat16)
    input_grad = (
        jnp.einsum("tk,dk->td", value_gradient, full_weight, preferred_element_type=jnp.float32)
        + ADAPTER_SCALE
        * jnp.einsum("pb,wb->pw", rank_middle, adapter_down, preferred_element_type=jnp.float32)
    ).astype(jnp.bfloat16)
    up_factor = ADAPTER_SCALE * jnp.einsum(
        "tr,tk->rk", rank_projection, value_gradient, preferred_element_type=jnp.float32
    )
    down_factor = ADAPTER_SCALE * jnp.einsum(
        "td,tr->dr", hidden_rows, rank_middle, preferred_element_type=jnp.float32
    )
    down_size = down_factor.size
    flat = jnp.concatenate([down_factor.reshape(-1), up_factor.reshape(-1)], 0)
    flat = butterfly_sum(flat.reshape(-1, HEAD_SIZE), ("pair", "ctx")).reshape(-1)
    down_gradient = flat[:down_size].reshape(down_factor.shape)
    up_gradient = flat[down_size:].reshape(up_factor.shape)
    return (input_grad[None], query_grad[None], key_grad[None], down_gradient, up_gradient)


def solution(mesh):
    return jax.shard_map(
        shards,
        mesh=mesh,
        in_specs=(
            P(("grp", "pair"), "ctx", None),
            P(("grp", "pair"), "ctx", None),
            P(("grp", "pair"), "ctx", None),
            P("ctx", None),
            P(),
            P(),
            P(("grp", "pair"), "ctx", None),
            P(("grp", "pair"), "ctx"),
            P(("grp", "pair"), "ctx"),
            P(("grp", "pair"), "ctx"),
        ),
        out_specs=(
            P(("grp", "pair"), "ctx", None),
            P(("grp", "pair"), "ctx", None),
            P(("grp", "pair"), "ctx", None),
            P("grp", None),
            P("grp", None),
        ),
        check_vma=False,
    )
```

```python
import jax
import jax.numpy as jnp
from jax import lax
from jax.sharding import PartitionSpec as P

HEAD_SIZE = 128
WINDOW = 1024
SEGS = 8


DPO_BETA = 0.1
LOSS_SCALE = 256.0
ADAPTER_SCALE = 2.0
ATTN_SCALE = 168.0 ** (-0.5)
NEG_FILL = -1e30


def from_partner(shard, axis, stride):
    return lax.ppermute(shard, axis, [(i, i ^ 1 << stride) for i in range(lax.axis_size(axis))])


def butterfly_sum(parts, axes):
    for axis in axes:
        size = lax.axis_size(axis)
        if size & (size - 1):
            parts = lax.psum(parts, axis)
            continue
        stride = 0
        while 1 << stride < size:
            got = from_partner(parts, axis, stride)
            parts = jax.tree.map(jnp.add, parts, got)
            stride += 1
    return parts


def tree_spread(block, levels):
    count = 2 * levels
    climbed = []
    held = block
    for step in range(1, levels):
        held = lax.ppermute(held, "ctx", [(c - 2, c) for c in range(2 * step, count)])
        climbed.append(held)
    crossed = [lax.ppermute(block, "ctx", [(c - 1, c) for c in range(1, count, 2)])]
    for step in range(1, levels):
        crossed.append(
            lax.ppermute(climbed[step - 1], "ctx", [(c ^ 1, c) for c in range(2 * step, count)])
        )
    return climbed + crossed


def tree_slots(ctx_index, levels):
    partner = jnp.bitwise_xor(ctx_index, 1)
    owners, valid = [], []
    for step in range(1, levels):
        owners.append(ctx_index - 2 * step)
        valid.append(ctx_index >= 2 * step)
    owners.append(ctx_index - 1)
    valid.append(ctx_index % 2 == 1)
    for step in range(1, levels):
        owners.append(partner - 2 * step)
        valid.append(ctx_index >= 2 * step)
    return owners, valid


def tree_return(slot_parts, levels):
    count = 2 * levels
    climbed = slot_parts[: levels - 1]
    crossed = slot_parts[levels - 1 :]
    back = [lax.ppermute(crossed[0], "ctx", [(c, c - 1) for c in range(1, count, 2)])]
    for step in range(1, levels):
        back.append(
            lax.ppermute(crossed[step], "ctx", [(c, c ^ 1) for c in range(2 * step, count)])
        )
    total = back[0].astype(jnp.float32)
    carry = None
    for step in range(levels - 1, 0, -1):
        acc = climbed[step - 1].astype(jnp.float32) + back[step].astype(jnp.float32)
        if carry is not None:
            acc = acc + carry.astype(jnp.float32)
        carry = lax.ppermute(
            acc.astype(jnp.bfloat16), "ctx", [(c, c - 2) for c in range(2 * step, count)]
        )
    if carry is not None:
        total = total + carry.astype(jnp.float32)
    return total


def shifted(block, axis, distance):
    devices = range(lax.axis_size(axis))
    route = [(i - distance, i) for i in devices if i - distance in devices]
    return lax.ppermute(block, axis, route)


def shards(
    normed_input,
    queries,
    keys,
    value_projection,
    adapter_down,
    adapter_up,
    output_gradient,
    policy_logprob,
    reference_logprob,
    token_pair_index,
):
    tok_rows = normed_input.shape[1]
    width_kv = keys.shape[2]
    kv_heads = width_kv // HEAD_SIZE
    group_size = queries.shape[2] // width_kv
    hidden_rows = normed_input[0]
    own_keys = keys[0]
    pair_index = lax.axis_index("pair")
    ctx_index = lax.axis_index("ctx")
    half_cols = width_kv // 2
    own_half = lax.dynamic_slice_in_dim(value_projection, pair_index * half_cols, half_cols, 1)
    rows_half = lax.all_gather(own_half, "ctx", axis=0, tiled=True)
    full_weight = lax.all_gather(rows_half, "pair", axis=1, tiled=True)
    rank_projection = jnp.dot(hidden_rows, adapter_down, preferred_element_type=jnp.float32).astype(
        jnp.bfloat16
    )
    values = (
        jnp.dot(hidden_rows, full_weight, preferred_element_type=jnp.float32)
        + ADAPTER_SCALE * jnp.dot(rank_projection, adapter_up, preferred_element_type=jnp.float32)
    ).astype(jnp.bfloat16)
    segment_labels = token_pair_index[0]
    seg_table = (segment_labels[:, None] == jnp.arange(SEGS, dtype=jnp.int32)[None, :]).astype(
        jnp.float32
    )
    log_gap = policy_logprob[0] - reference_logprob[0]
    part_diff = jnp.sum(seg_table * log_gap[:, None], 0)
    part_count = jnp.sum(seg_table, 0)
    both_sums = butterfly_sum(jnp.concatenate([part_diff, part_count], 0), ("ctx",))
    own_diff, counts = both_sums[:SEGS], both_sums[SEGS:]
    other_diff = from_partner(own_diff, "pair", 0)
    direction = 1.0 - 2.0 * pair_index.astype(jnp.float32)
    margin = DPO_BETA * (direction * (own_diff - other_diff))
    coef = -direction * DPO_BETA * LOSS_SCALE * jax.nn.sigmoid(-margin)
    starts = jnp.cumsum(counts) - counts
    tok_start = jnp.sum(seg_table * starts[None, :], 1).astype(jnp.int32)
    token_coefficient = jnp.sum(seg_table * coef[None, :], 1)
    ctx_size = lax.axis_size("ctx")
    halo_blocks = min(WINDOW // tok_rows, ctx_size - 1)
    use_tree = halo_blocks == ctx_size - 1 and ctx_size % 2 == 0 and ctx_size >= 4
    levels = ctx_size // 2
    row_iota = jnp.arange(tok_rows, dtype=jnp.int32)
    if use_tree:
        key_blocks = tree_spread(own_keys, levels)
        value_blocks = tree_spread(values, levels)
        owners, valid = tree_slots(ctx_index, levels)
        far = jnp.int32(1 << 30)
        upos = jnp.concatenate(
            [jnp.where(ok, owner * tok_rows + row_iota, far) for owner, ok in zip(owners, valid)]
            + [ctx_index * tok_rows + row_iota],
            0,
        )
    else:
        key_blocks = []
        value_blocks = []
        for distance in range(halo_blocks, 0, -1):
            key_blocks.append(shifted(own_keys, "ctx", distance))
            value_blocks.append(shifted(values, "ctx", distance))
    all_keys = jnp.concatenate(key_blocks + [own_keys], 0)
    all_keys, own_values = lax.optimization_barrier((all_keys, values))
    all_values = jnp.concatenate(value_blocks + [own_values], 0)
    span = all_keys.shape[0]
    tpos = ctx_index * tok_rows + row_iota
    if not use_tree:
        upos = ctx_index * tok_rows - halo_blocks * tok_rows + jnp.arange(span, dtype=jnp.int32)
    allowed = (
        (upos[None, :] <= tpos[:, None])
        & (upos[None, :] > tpos[:, None] - WINDOW)
        & (upos[None, :] >= tok_start[:, None])
    )
    coef_rows = token_coefficient[None, :, None]
    query_rows = queries[0].reshape(tok_rows, kv_heads, group_size, HEAD_SIZE)
    grad_rows = output_gradient[0].reshape(tok_rows, kv_heads, group_size, HEAD_SIZE)
    key_rows = all_keys.reshape(span, kv_heads, HEAD_SIZE)
    value_rows = all_values.reshape(span, kv_heads, HEAD_SIZE)
    scores = ATTN_SCALE * jnp.einsum(
        "tjgd,ljd->jgtl", query_rows, key_rows, preferred_element_type=jnp.float32
    )
    masked = jnp.where(allowed[None, None], scores, NEG_FILL)
    row_max = jnp.max(masked, -1, keepdims=True)
    weights_exp = jnp.where(allowed[None, None], jnp.exp(masked - row_max), 0.0)
    attn_probs = weights_exp / jnp.sum(weights_exp, -1, keepdims=True)
    prob_grad = coef_rows[None] * jnp.einsum(
        "tjgd,ljd->jgtl", grad_rows, value_rows, preferred_element_type=jnp.float32
    )
    row_delta = jnp.sum(attn_probs * prob_grad, -1, keepdims=True)
    score_grad = (ATTN_SCALE * attn_probs * (prob_grad - row_delta)).astype(jnp.bfloat16)
    query_grad = jnp.einsum(
        "jgtl,ljd->tjgd", score_grad, key_rows, preferred_element_type=jnp.float32
    ).astype(jnp.bfloat16).reshape(tok_rows, kv_heads * group_size * HEAD_SIZE)
    key_parts = jnp.einsum(
        "jgtl,tjgd->ljd", score_grad, query_rows, preferred_element_type=jnp.float32
    ).reshape(span, width_kv)
    weighted = (attn_probs * coef_rows[None]).astype(jnp.bfloat16)
    value_parts = jnp.einsum(
        "jgtl,tjgd->ljd", weighted, grad_rows, preferred_element_type=jnp.float32
    ).reshape(span, width_kv)
    key_total = key_parts[halo_blocks * tok_rows :]
    value_total = value_parts[halo_blocks * tok_rows :]
    if use_tree:
        slot_rows = lambda parts: [
            parts[k * tok_rows : (k + 1) * tok_rows].astype(jnp.bfloat16) for k in range(halo_blocks)
        ]
        key_total = key_total + tree_return(slot_rows(key_parts), levels)
        value_total = value_total + tree_return(slot_rows(value_parts), levels)
    else:
        for distance in range(1, halo_blocks + 1):
            block_start = (halo_blocks - distance) * tok_rows
            send_keys = key_parts[block_start : block_start + tok_rows].astype(jnp.bfloat16)
            send_values = value_parts[block_start : block_start + tok_rows].astype(jnp.bfloat16)
            back_keys, back_values = shifted((send_keys, send_values), "ctx", -distance)
            key_total = key_total + back_keys.astype(jnp.float32)
            value_total = value_total + back_values.astype(jnp.float32)
    key_grad = key_total.astype(jnp.bfloat16)
    value_gradient = value_total.astype(jnp.bfloat16)
    rank_middle = jnp.einsum(
        "sj,zj->sz", value_gradient, adapter_up, preferred_element_type=jnp.float32
    ).astype(jnp.bfloat16)
    input_grad = (
        jnp.einsum("tk,dk->td", value_gradient, full_weight, preferred_element_type=jnp.float32)
        + ADAPTER_SCALE
        * jnp.einsum("pb,wb->pw", rank_middle, adapter_down, preferred_element_type=jnp.float32)
    ).astype(jnp.bfloat16)
    up_factor = ADAPTER_SCALE * jnp.einsum(
        "tr,tk->rk", rank_projection, value_gradient, preferred_element_type=jnp.float32
    )
    down_factor = ADAPTER_SCALE * jnp.einsum(
        "td,tr->dr", hidden_rows, rank_middle, preferred_element_type=jnp.float32
    )
    down_size = down_factor.size
    flat = jnp.concatenate([down_factor.reshape(-1), up_factor.reshape(-1)], 0)
    flat = butterfly_sum(flat.reshape(-1, HEAD_SIZE), ("pair", "ctx")).reshape(-1)
    down_gradient = flat[:down_size].reshape(down_factor.shape)
    up_gradient = flat[down_size:].reshape(up_factor.shape)
    return (input_grad[None], query_grad[None], key_grad[None], down_gradient, up_gradient)


def solution(mesh):
    return jax.shard_map(
        shards,
        mesh=mesh,
        in_specs=(
            P(("grp", "pair"), "ctx", None),
            P(("grp", "pair"), "ctx", None),
            P(("grp", "pair"), "ctx", None),
            P("ctx", None),
            P(),
            P(),
            P(("grp", "pair"), "ctx", None),
            P(("grp", "pair"), "ctx"),
            P(("grp", "pair"), "ctx"),
            P(("grp", "pair"), "ctx"),
        ),
        out_specs=(
            P(("grp", "pair"), "ctx", None),
            P(("grp", "pair"), "ctx", None),
            P(("grp", "pair"), "ctx", None),
            P("grp", None),
            P("grp", None),
        ),
        check_vma=False,
    )
```

```python
import jax
import jax.numpy as jnp
from jax import lax
from jax.sharding import PartitionSpec as P

HEAD_SIZE = 128
WINDOW = 1024
SEGS = 8


DPO_BETA = 0.1
LOSS_SCALE = 256.0
ADAPTER_SCALE = 2.0
ATTN_SCALE = 168.0 ** (-0.5)
NEG_FILL = -1e30


def from_partner(shard, axis, stride):
    return lax.ppermute(shard, axis, [(i, i ^ 1 << stride) for i in range(lax.axis_size(axis))])


def butterfly_sum(parts, axes):
    for axis in axes:
        size = lax.axis_size(axis)
        if size & (size - 1):
            parts = lax.psum(parts, axis)
            continue
        stride = 0
        while 1 << stride < size:
            got = from_partner(parts, axis, stride)
            parts = jax.tree.map(jnp.add, parts, got)
            stride += 1
    return parts


def tree_spread(block, levels):
    count = 2 * levels
    climbed = []
    held = block
    for step in range(1, levels):
        held = lax.ppermute(held, "ctx", [(c - 2, c) for c in range(2 * step, count)])
        climbed.append(held)
    crossed = [lax.ppermute(block, "ctx", [(c - 1, c) for c in range(1, count, 2)])]
    for step in range(1, levels):
        crossed.append(
            lax.ppermute(climbed[step - 1], "ctx", [(c ^ 1, c) for c in range(2 * step, count)])
        )
    return climbed + crossed


def tree_gather(block, ctx_index, levels):
    count = 2 * levels
    partner = jnp.bitwise_xor(ctx_index, 1)
    got = [block]
    owners = [ctx_index]
    valid = [ctx_index >= 0]
    up, down = block, block
    ups, downs = [], []
    for step in range(1, levels):
        up = lax.ppermute(up, "ctx", [(c - 2, c) for c in range(2 * step, count)])
        down = lax.ppermute(down, "ctx", [(c + 2, c) for c in range(0, count - 2 * step)])
        ups.append(up)
        downs.append(down)
        got += [up, down]
        owners += [ctx_index - 2 * step, ctx_index + 2 * step]
        valid += [ctx_index >= 2 * step, ctx_index < count - 2 * step]
    got.append(lax.ppermute(block, "ctx", [(c ^ 1, c) for c in range(count)]))
    owners.append(partner)
    valid.append(ctx_index >= 0)
    for step in range(1, levels):
        got.append(lax.ppermute(ups[step - 1], "ctx", [(c ^ 1, c) for c in range(2 * step, count)]))
        got.append(
            lax.ppermute(downs[step - 1], "ctx", [(c ^ 1, c) for c in range(0, count - 2 * step)])
        )
        owners += [partner - 2 * step, partner + 2 * step]
        valid += [ctx_index >= 2 * step, ctx_index < count - 2 * step]
    rows = block.shape[0]
    whole = jnp.zeros(((count + 1) * rows,) + block.shape[1:], block.dtype)
    for piece, owner, ok in zip(got, owners, valid):
        place = jnp.where(ok, owner, count) * rows
        whole = lax.dynamic_update_slice_in_dim(whole, piece, place, 0)
    return whole[: count * rows]


def tree_slots(ctx_index, levels):
    partner = jnp.bitwise_xor(ctx_index, 1)
    owners, valid = [], []
    for step in range(1, levels):
        owners.append(ctx_index - 2 * step)
        valid.append(ctx_index >= 2 * step)
    owners.append(ctx_index - 1)
    valid.append(ctx_index % 2 == 1)
    for step in range(1, levels):
        owners.append(partner - 2 * step)
        valid.append(ctx_index >= 2 * step)
    return owners, valid


def tree_return(slot_parts, levels):
    count = 2 * levels
    climbed = slot_parts[: levels - 1]
    crossed = slot_parts[levels - 1 :]
    back = [lax.ppermute(crossed[0], "ctx", [(c, c - 1) for c in range(1, count, 2)])]
    for step in range(1, levels):
        back.append(
            lax.ppermute(crossed[step], "ctx", [(c, c ^ 1) for c in range(2 * step, count)])
        )
    total = back[0].astype(jnp.float32)
    carry = None
    for step in range(levels - 1, 0, -1):
        acc = climbed[step - 1].astype(jnp.float32) + back[step].astype(jnp.float32)
        if carry is not None:
            acc = acc + carry.astype(jnp.float32)
        carry = lax.ppermute(
            acc.astype(jnp.bfloat16), "ctx", [(c, c - 2) for c in range(2 * step, count)]
        )
    if carry is not None:
        total = total + carry.astype(jnp.float32)
    return total


def shifted(block, axis, distance):
    devices = range(lax.axis_size(axis))
    route = [(i - distance, i) for i in devices if i - distance in devices]
    return lax.ppermute(block, axis, route)


def shards(
    normed_input,
    queries,
    keys,
    value_projection,
    adapter_down,
    adapter_up,
    output_gradient,
    policy_logprob,
    reference_logprob,
    token_pair_index,
):
    tok_rows = normed_input.shape[1]
    width_kv = keys.shape[2]
    kv_heads = width_kv // HEAD_SIZE
    group_size = queries.shape[2] // width_kv
    hidden_rows = normed_input[0]
    own_keys = keys[0]
    pair_index = lax.axis_index("pair")
    ctx_index = lax.axis_index("ctx")
    half_cols = width_kv // 2
    own_half = lax.dynamic_slice_in_dim(value_projection, pair_index * half_cols, half_cols, 1)
    ctx_count = lax.axis_size("ctx")
    if ctx_count % 2 == 0 and 4 <= ctx_count <= 8:
        rows_half = tree_gather(own_half, ctx_index, ctx_count // 2)
    else:
        rows_half = lax.all_gather(own_half, "ctx", axis=0, tiled=True)
    full_weight = lax.all_gather(rows_half, "pair", axis=1, tiled=True)
    rank_projection = jnp.dot(hidden_rows, adapter_down, preferred_element_type=jnp.float32).astype(
        jnp.bfloat16
    )
    values = (
        jnp.dot(hidden_rows, full_weight, preferred_element_type=jnp.float32)
        + ADAPTER_SCALE * jnp.dot(rank_projection, adapter_up, preferred_element_type=jnp.float32)
    ).astype(jnp.bfloat16)
    segment_labels = token_pair_index[0]
    seg_table = (segment_labels[:, None] == jnp.arange(SEGS, dtype=jnp.int32)[None, :]).astype(
        jnp.float32
    )
    log_gap = policy_logprob[0] - reference_logprob[0]
    part_diff = jnp.sum(seg_table * log_gap[:, None], 0)
    part_count = jnp.sum(seg_table, 0)
    both_sums = butterfly_sum(jnp.concatenate([part_diff, part_count], 0), ("ctx",))
    own_diff, counts = both_sums[:SEGS], both_sums[SEGS:]
    other_diff = from_partner(own_diff, "pair", 0)
    direction = 1.0 - 2.0 * pair_index.astype(jnp.float32)
    margin = DPO_BETA * (direction * (own_diff - other_diff))
    coef = -direction * DPO_BETA * LOSS_SCALE * jax.nn.sigmoid(-margin)
    starts = jnp.cumsum(counts) - counts
    tok_start = jnp.sum(seg_table * starts[None, :], 1).astype(jnp.int32)
    token_coefficient = jnp.sum(seg_table * coef[None, :], 1)
    ctx_size = lax.axis_size("ctx")
    halo_blocks = min(WINDOW // tok_rows, ctx_size - 1)
    use_tree = halo_blocks == ctx_size - 1 and ctx_size % 2 == 0 and ctx_size >= 4
    levels = ctx_size // 2
    row_iota = jnp.arange(tok_rows, dtype=jnp.int32)
    if use_tree:
        key_blocks = tree_spread(own_keys, levels)
        value_blocks = tree_spread(values, levels)
        owners, valid = tree_slots(ctx_index, levels)
        far = jnp.int32(1 << 30)
        upos = jnp.concatenate(
            [jnp.where(ok, owner * tok_rows + row_iota, far) for owner, ok in zip(owners, valid)]
            + [ctx_index * tok_rows + row_iota],
            0,
        )
    else:
        key_blocks = []
        value_blocks = []
        for distance in range(halo_blocks, 0, -1):
            key_blocks.append(shifted(own_keys, "ctx", distance))
            value_blocks.append(shifted(values, "ctx", distance))
    all_keys = jnp.concatenate(key_blocks + [own_keys], 0)
    all_keys, own_values = lax.optimization_barrier((all_keys, values))
    all_values = jnp.concatenate(value_blocks + [own_values], 0)
    span = all_keys.shape[0]
    tpos = ctx_index * tok_rows + row_iota
    if not use_tree:
        upos = ctx_index * tok_rows - halo_blocks * tok_rows + jnp.arange(span, dtype=jnp.int32)
    allowed = (
        (upos[None, :] <= tpos[:, None])
        & (upos[None, :] > tpos[:, None] - WINDOW)
        & (upos[None, :] >= tok_start[:, None])
    )
    coef_rows = token_coefficient[None, :, None]
    query_rows = queries[0].reshape(tok_rows, kv_heads, group_size, HEAD_SIZE)
    grad_rows = output_gradient[0].reshape(tok_rows, kv_heads, group_size, HEAD_SIZE)
    key_rows = all_keys.reshape(span, kv_heads, HEAD_SIZE)
    value_rows = all_values.reshape(span, kv_heads, HEAD_SIZE)
    scores = ATTN_SCALE * jnp.einsum(
        "tjgd,ljd->jgtl", query_rows, key_rows, preferred_element_type=jnp.float32
    )
    masked = jnp.where(allowed[None, None], scores, NEG_FILL)
    row_max = jnp.max(masked, -1, keepdims=True)
    weights_exp = jnp.where(allowed[None, None], jnp.exp(masked - row_max), 0.0)
    attn_probs = weights_exp / jnp.sum(weights_exp, -1, keepdims=True)
    prob_grad = coef_rows[None] * jnp.einsum(
        "tjgd,ljd->jgtl", grad_rows, value_rows, preferred_element_type=jnp.float32
    )
    row_delta = jnp.sum(attn_probs * prob_grad, -1, keepdims=True)
    score_grad = (ATTN_SCALE * attn_probs * (prob_grad - row_delta)).astype(jnp.bfloat16)
    query_grad = jnp.einsum(
        "jgtl,ljd->tjgd", score_grad, key_rows, preferred_element_type=jnp.float32
    ).astype(jnp.bfloat16).reshape(tok_rows, kv_heads * group_size * HEAD_SIZE)
    key_parts = jnp.einsum(
        "jgtl,tjgd->ljd", score_grad, query_rows, preferred_element_type=jnp.float32
    ).reshape(span, width_kv)
    weighted = (attn_probs * coef_rows[None]).astype(jnp.bfloat16)
    value_parts = jnp.einsum(
        "jgtl,tjgd->ljd", weighted, grad_rows, preferred_element_type=jnp.float32
    ).reshape(span, width_kv)
    key_total = key_parts[halo_blocks * tok_rows :]
    value_total = value_parts[halo_blocks * tok_rows :]
    if use_tree:
        slot_rows = lambda parts: [
            parts[k * tok_rows : (k + 1) * tok_rows].astype(jnp.bfloat16) for k in range(halo_blocks)
        ]
        key_total = key_total + tree_return(slot_rows(key_parts), levels)
        value_total = value_total + tree_return(slot_rows(value_parts), levels)
    else:
        for distance in range(1, halo_blocks + 1):
            block_start = (halo_blocks - distance) * tok_rows
            send_keys = key_parts[block_start : block_start + tok_rows].astype(jnp.bfloat16)
            send_values = value_parts[block_start : block_start + tok_rows].astype(jnp.bfloat16)
            back_keys, back_values = shifted((send_keys, send_values), "ctx", -distance)
            key_total = key_total + back_keys.astype(jnp.float32)
            value_total = value_total + back_values.astype(jnp.float32)
    key_grad = key_total.astype(jnp.bfloat16)
    value_gradient = value_total.astype(jnp.bfloat16)
    rank_middle = jnp.einsum(
        "sj,zj->sz", value_gradient, adapter_up, preferred_element_type=jnp.float32
    ).astype(jnp.bfloat16)
    input_grad = (
        jnp.einsum("tk,dk->td", value_gradient, full_weight, preferred_element_type=jnp.float32)
        + ADAPTER_SCALE
        * jnp.einsum("pb,wb->pw", rank_middle, adapter_down, preferred_element_type=jnp.float32)
    ).astype(jnp.bfloat16)
    up_factor = ADAPTER_SCALE * jnp.einsum(
        "tr,tk->rk", rank_projection, value_gradient, preferred_element_type=jnp.float32
    )
    down_factor = ADAPTER_SCALE * jnp.einsum(
        "td,tr->dr", hidden_rows, rank_middle, preferred_element_type=jnp.float32
    )
    down_size = down_factor.size
    flat = jnp.concatenate([down_factor.reshape(-1), up_factor.reshape(-1)], 0)
    flat = butterfly_sum(flat.reshape(-1, HEAD_SIZE), ("pair", "ctx")).reshape(-1)
    down_gradient = flat[:down_size].reshape(down_factor.shape)
    up_gradient = flat[down_size:].reshape(up_factor.shape)
    return (input_grad[None], query_grad[None], key_grad[None], down_gradient, up_gradient)


def solution(mesh):
    return jax.shard_map(
        shards,
        mesh=mesh,
        in_specs=(
            P(("grp", "pair"), "ctx", None),
            P(("grp", "pair"), "ctx", None),
            P(("grp", "pair"), "ctx", None),
            P("ctx", None),
            P(),
            P(),
            P(("grp", "pair"), "ctx", None),
            P(("grp", "pair"), "ctx"),
            P(("grp", "pair"), "ctx"),
            P(("grp", "pair"), "ctx"),
        ),
        out_specs=(
            P(("grp", "pair"), "ctx", None),
            P(("grp", "pair"), "ctx", None),
            P(("grp", "pair"), "ctx", None),
            P("grp", None),
            P("grp", None),
        ),
        check_vma=False,
    )
```

```python
import jax
import jax.numpy as jnp
from jax import lax
from jax.sharding import PartitionSpec as P

HEAD_SIZE = 128
WINDOW = 1024
SEGS = 8


DPO_BETA = 0.1
LOSS_SCALE = 256.0
ADAPTER_SCALE = 2.0
ATTN_SCALE = 168.0 ** (-0.5)
NEG_FILL = -1e30


def from_partner(shard, axis, stride):
    return lax.ppermute(shard, axis, [(i, i ^ 1 << stride) for i in range(lax.axis_size(axis))])


def butterfly_sum(parts, axes):
    for axis in axes:
        size = lax.axis_size(axis)
        if size & (size - 1):
            parts = lax.psum(parts, axis)
            continue
        stride = 0
        while 1 << stride < size:
            got = from_partner(parts, axis, stride)
            parts = jax.tree.map(jnp.add, parts, got)
            stride += 1
    return parts


def tree_spread(block, levels):
    count = 2 * levels
    climbed = []
    for step in range(1, levels):
        climbed.append(
            lax.ppermute(block, "ctx", [(c - 2 * step, c) for c in range(2 * step, count)])
        )
    crossed = [lax.ppermute(block, "ctx", [(c - 1, c) for c in range(1, count, 2)])]
    for step in range(1, levels):
        crossed.append(
            lax.ppermute(climbed[step - 1], "ctx", [(c ^ 1, c) for c in range(2 * step, count)])
        )
    return climbed + crossed


def tree_gather(block, ctx_index, levels):
    count = 2 * levels
    partner = jnp.bitwise_xor(ctx_index, 1)
    got = [block]
    owners = [ctx_index]
    valid = [ctx_index >= 0]
    ups, downs = [], []
    for step in range(1, levels):
        up = lax.ppermute(block, "ctx", [(c - 2 * step, c) for c in range(2 * step, count)])
        down = lax.ppermute(block, "ctx", [(c + 2 * step, c) for c in range(0, count - 2 * step)])
        ups.append(up)
        downs.append(down)
        got += [up, down]
        owners += [ctx_index - 2 * step, ctx_index + 2 * step]
        valid += [ctx_index >= 2 * step, ctx_index < count - 2 * step]
    got.append(lax.ppermute(block, "ctx", [(c ^ 1, c) for c in range(count)]))
    owners.append(partner)
    valid.append(ctx_index >= 0)
    for step in range(1, levels):
        got.append(lax.ppermute(ups[step - 1], "ctx", [(c ^ 1, c) for c in range(2 * step, count)]))
        got.append(
            lax.ppermute(downs[step - 1], "ctx", [(c ^ 1, c) for c in range(0, count - 2 * step)])
        )
        owners += [partner - 2 * step, partner + 2 * step]
        valid += [ctx_index >= 2 * step, ctx_index < count - 2 * step]
    rows = block.shape[0]
    whole = jnp.zeros(((count + 1) * rows,) + block.shape[1:], block.dtype)
    for piece, owner, ok in zip(got, owners, valid):
        place = jnp.where(ok, owner, count) * rows
        whole = lax.dynamic_update_slice_in_dim(whole, piece, place, 0)
    return whole[: count * rows]


def tree_slots(ctx_index, levels):
    partner = jnp.bitwise_xor(ctx_index, 1)
    owners, valid = [], []
    for step in range(1, levels):
        owners.append(ctx_index - 2 * step)
        valid.append(ctx_index >= 2 * step)
    owners.append(ctx_index - 1)
    valid.append(ctx_index % 2 == 1)
    for step in range(1, levels):
        owners.append(partner - 2 * step)
        valid.append(ctx_index >= 2 * step)
    return owners, valid


def tree_return(slot_parts, levels):
    count = 2 * levels
    climbed = slot_parts[: levels - 1]
    crossed = slot_parts[levels - 1 :]
    back = [lax.ppermute(crossed[0], "ctx", [(c, c - 1) for c in range(1, count, 2)])]
    for step in range(1, levels):
        back.append(
            lax.ppermute(crossed[step], "ctx", [(c, c ^ 1) for c in range(2 * step, count)])
        )
    total = back[0].astype(jnp.float32)
    for step in range(1, levels):
        acc = climbed[step - 1].astype(jnp.float32) + back[step].astype(jnp.float32)
        home = lax.ppermute(
            acc.astype(jnp.bfloat16), "ctx", [(c, c - 2 * step) for c in range(2 * step, count)]
        )
        total = total + home.astype(jnp.float32)
    return total


def shifted(block, axis, distance):
    devices = range(lax.axis_size(axis))
    route = [(i - distance, i) for i in devices if i - distance in devices]
    return lax.ppermute(block, axis, route)


def shards(
    normed_input,
    queries,
    keys,
    value_projection,
    adapter_down,
    adapter_up,
    output_gradient,
    policy_logprob,
    reference_logprob,
    token_pair_index,
):
    tok_rows = normed_input.shape[1]
    width_kv = keys.shape[2]
    kv_heads = width_kv // HEAD_SIZE
    group_size = queries.shape[2] // width_kv
    hidden_rows = normed_input[0]
    own_keys = keys[0]
    pair_index = lax.axis_index("pair")
    ctx_index = lax.axis_index("ctx")
    half_cols = width_kv // 2
    own_half = lax.dynamic_slice_in_dim(value_projection, pair_index * half_cols, half_cols, 1)
    ctx_count = lax.axis_size("ctx")
    if ctx_count % 2 == 0 and 4 <= ctx_count <= 8:
        rows_half = tree_gather(own_half, ctx_index, ctx_count // 2)
    else:
        rows_half = lax.all_gather(own_half, "ctx", axis=0, tiled=True)
    full_weight = lax.all_gather(rows_half, "pair", axis=1, tiled=True)
    rank_projection = jnp.dot(hidden_rows, adapter_down, preferred_element_type=jnp.float32).astype(
        jnp.bfloat16
    )
    values = (
        jnp.dot(hidden_rows, full_weight, preferred_element_type=jnp.float32)
        + ADAPTER_SCALE * jnp.dot(rank_projection, adapter_up, preferred_element_type=jnp.float32)
    ).astype(jnp.bfloat16)
    segment_labels = token_pair_index[0]
    seg_table = (segment_labels[:, None] == jnp.arange(SEGS, dtype=jnp.int32)[None, :]).astype(
        jnp.float32
    )
    log_gap = policy_logprob[0] - reference_logprob[0]
    part_diff = jnp.sum(seg_table * log_gap[:, None], 0)
    part_count = jnp.sum(seg_table, 0)
    both_sums = butterfly_sum(jnp.concatenate([part_diff, part_count], 0), ("ctx",))
    own_diff, counts = both_sums[:SEGS], both_sums[SEGS:]
    other_diff = from_partner(own_diff, "pair", 0)
    direction = 1.0 - 2.0 * pair_index.astype(jnp.float32)
    margin = DPO_BETA * (direction * (own_diff - other_diff))
    coef = -direction * DPO_BETA * LOSS_SCALE * jax.nn.sigmoid(-margin)
    starts = jnp.cumsum(counts) - counts
    tok_start = jnp.sum(seg_table * starts[None, :], 1).astype(jnp.int32)
    token_coefficient = jnp.sum(seg_table * coef[None, :], 1)
    ctx_size = lax.axis_size("ctx")
    halo_blocks = min(WINDOW // tok_rows, ctx_size - 1)
    use_tree = halo_blocks == ctx_size - 1 and ctx_size % 2 == 0 and ctx_size >= 4
    levels = ctx_size // 2
    row_iota = jnp.arange(tok_rows, dtype=jnp.int32)
    if use_tree:
        key_blocks = tree_spread(own_keys, levels)
        value_blocks = tree_spread(values, levels)
        owners, valid = tree_slots(ctx_index, levels)
        far = jnp.int32(1 << 30)
        upos = jnp.concatenate(
            [jnp.where(ok, owner * tok_rows + row_iota, far) for owner, ok in zip(owners, valid)]
            + [ctx_index * tok_rows + row_iota],
            0,
        )
    else:
        key_blocks = []
        value_blocks = []
        for distance in range(halo_blocks, 0, -1):
            key_blocks.append(shifted(own_keys, "ctx", distance))
            value_blocks.append(shifted(values, "ctx", distance))
    all_keys = jnp.concatenate(key_blocks + [own_keys], 0)
    all_keys, own_values = lax.optimization_barrier((all_keys, values))
    all_values = jnp.concatenate(value_blocks + [own_values], 0)
    span = all_keys.shape[0]
    tpos = ctx_index * tok_rows + row_iota
    if not use_tree:
        upos = ctx_index * tok_rows - halo_blocks * tok_rows + jnp.arange(span, dtype=jnp.int32)
    allowed = (
        (upos[None, :] <= tpos[:, None])
        & (upos[None, :] > tpos[:, None] - WINDOW)
        & (upos[None, :] >= tok_start[:, None])
    )
    coef_rows = token_coefficient[None, :, None]
    query_rows = queries[0].reshape(tok_rows, kv_heads, group_size, HEAD_SIZE)
    grad_rows = output_gradient[0].reshape(tok_rows, kv_heads, group_size, HEAD_SIZE)
    key_rows = all_keys.reshape(span, kv_heads, HEAD_SIZE)
    value_rows = all_values.reshape(span, kv_heads, HEAD_SIZE)
    scores = ATTN_SCALE * jnp.einsum(
        "tjgd,ljd->jgtl", query_rows, key_rows, preferred_element_type=jnp.float32
    )
    masked = jnp.where(allowed[None, None], scores, NEG_FILL)
    row_max = jnp.max(masked, -1, keepdims=True)
    weights_exp = jnp.where(allowed[None, None], jnp.exp(masked - row_max), 0.0)
    attn_probs = weights_exp / jnp.sum(weights_exp, -1, keepdims=True)
    prob_grad = coef_rows[None] * jnp.einsum(
        "tjgd,ljd->jgtl", grad_rows, value_rows, preferred_element_type=jnp.float32
    )
    row_delta = jnp.sum(attn_probs * prob_grad, -1, keepdims=True)
    score_grad = (ATTN_SCALE * attn_probs * (prob_grad - row_delta)).astype(jnp.bfloat16)
    query_grad = jnp.einsum(
        "jgtl,ljd->tjgd", score_grad, key_rows, preferred_element_type=jnp.float32
    ).astype(jnp.bfloat16).reshape(tok_rows, kv_heads * group_size * HEAD_SIZE)
    key_parts = jnp.einsum(
        "jgtl,tjgd->ljd", score_grad, query_rows, preferred_element_type=jnp.float32
    ).reshape(span, width_kv)
    weighted = (attn_probs * coef_rows[None]).astype(jnp.bfloat16)
    value_parts = jnp.einsum(
        "jgtl,tjgd->ljd", weighted, grad_rows, preferred_element_type=jnp.float32
    ).reshape(span, width_kv)
    key_total = key_parts[halo_blocks * tok_rows :]
    value_total = value_parts[halo_blocks * tok_rows :]
    if use_tree:
        slot_rows = lambda parts: [
            parts[k * tok_rows : (k + 1) * tok_rows].astype(jnp.bfloat16) for k in range(halo_blocks)
        ]
        key_total = key_total + tree_return(slot_rows(key_parts), levels)
        value_total = value_total + tree_return(slot_rows(value_parts), levels)
    else:
        for distance in range(1, halo_blocks + 1):
            block_start = (halo_blocks - distance) * tok_rows
            send_keys = key_parts[block_start : block_start + tok_rows].astype(jnp.bfloat16)
            send_values = value_parts[block_start : block_start + tok_rows].astype(jnp.bfloat16)
            back_keys, back_values = shifted((send_keys, send_values), "ctx", -distance)
            key_total = key_total + back_keys.astype(jnp.float32)
            value_total = value_total + back_values.astype(jnp.float32)
    key_grad = key_total.astype(jnp.bfloat16)
    value_gradient = value_total.astype(jnp.bfloat16)
    rank_middle = jnp.einsum(
        "sj,zj->sz", value_gradient, adapter_up, preferred_element_type=jnp.float32
    ).astype(jnp.bfloat16)
    input_grad = (
        jnp.einsum("tk,dk->td", value_gradient, full_weight, preferred_element_type=jnp.float32)
        + ADAPTER_SCALE
        * jnp.einsum("pb,wb->pw", rank_middle, adapter_down, preferred_element_type=jnp.float32)
    ).astype(jnp.bfloat16)
    up_factor = ADAPTER_SCALE * jnp.einsum(
        "tr,tk->rk", rank_projection, value_gradient, preferred_element_type=jnp.float32
    )
    down_factor = ADAPTER_SCALE * jnp.einsum(
        "td,tr->dr", hidden_rows, rank_middle, preferred_element_type=jnp.float32
    )
    down_size = down_factor.size
    flat = jnp.concatenate([down_factor.reshape(-1), up_factor.reshape(-1)], 0)
    flat = butterfly_sum(flat.reshape(-1, HEAD_SIZE), ("pair", "ctx")).reshape(-1)
    down_gradient = flat[:down_size].reshape(down_factor.shape)
    up_gradient = flat[down_size:].reshape(up_factor.shape)
    return (input_grad[None], query_grad[None], key_grad[None], down_gradient, up_gradient)


def solution(mesh):
    return jax.shard_map(
        shards,
        mesh=mesh,
        in_specs=(
            P(("grp", "pair"), "ctx", None),
            P(("grp", "pair"), "ctx", None),
            P(("grp", "pair"), "ctx", None),
            P("ctx", None),
            P(),
            P(),
            P(("grp", "pair"), "ctx", None),
            P(("grp", "pair"), "ctx"),
            P(("grp", "pair"), "ctx"),
            P(("grp", "pair"), "ctx"),
        ),
        out_specs=(
            P(("grp", "pair"), "ctx", None),
            P(("grp", "pair"), "ctx", None),
            P(("grp", "pair"), "ctx", None),
            P("grp", None),
            P("grp", None),
        ),
        check_vma=False,
    )
```

```python
import jax
import jax.numpy as jnp
from jax import lax
from jax.sharding import PartitionSpec as P

HEAD_SIZE = 128
WINDOW = 1024
SEGS = 8


DPO_BETA = 0.1
LOSS_SCALE = 256.0
ADAPTER_SCALE = 2.0
ATTN_SCALE = 168.0 ** (-0.5)
NEG_FILL = -1e30


def from_partner(shard, axis, stride):
    return lax.ppermute(shard, axis, [(i, i ^ 1 << stride) for i in range(lax.axis_size(axis))])


def butterfly_sum(parts, axes):
    for axis in axes:
        size = lax.axis_size(axis)
        if size & (size - 1):
            parts = lax.psum(parts, axis)
            continue
        stride = 0
        while 1 << stride < size:
            got = from_partner(parts, axis, stride)
            parts = jax.tree.map(jnp.add, parts, got)
            stride += 1
    return parts


def tree_spread(block, levels):
    count = 2 * levels
    climbed = []
    held = block
    for step in range(1, levels):
        held = lax.ppermute(held, "ctx", [(c - 2, c) for c in range(2 * step, count)])
        climbed.append(held)
    crossed = [lax.ppermute(block, "ctx", [(c - 1, c) for c in range(1, count, 2)])]
    for step in range(1, levels):
        crossed.append(
            lax.ppermute(climbed[step - 1], "ctx", [(c ^ 1, c) for c in range(2 * step, count)])
        )
    return climbed + crossed


def tree_gather(block, ctx_index, levels):
    count = 2 * levels
    partner = jnp.bitwise_xor(ctx_index, 1)
    got = [block]
    owners = [ctx_index]
    valid = [ctx_index >= 0]
    up, down = block, block
    ups, downs = [], []
    for step in range(1, levels):
        up = lax.ppermute(up, "ctx", [(c - 2, c) for c in range(2 * step, count)])
        down = lax.ppermute(down, "ctx", [(c + 2, c) for c in range(0, count - 2 * step)])
        ups.append(up)
        downs.append(down)
        got += [up, down]
        owners += [ctx_index - 2 * step, ctx_index + 2 * step]
        valid += [ctx_index >= 2 * step, ctx_index < count - 2 * step]
    got.append(lax.ppermute(block, "ctx", [(c ^ 1, c) for c in range(count)]))
    owners.append(partner)
    valid.append(ctx_index >= 0)
    for step in range(1, levels):
        got.append(lax.ppermute(ups[step - 1], "ctx", [(c ^ 1, c) for c in range(2 * step, count)]))
        got.append(
            lax.ppermute(downs[step - 1], "ctx", [(c ^ 1, c) for c in range(0, count - 2 * step)])
        )
        owners += [partner - 2 * step, partner + 2 * step]
        valid += [ctx_index >= 2 * step, ctx_index < count - 2 * step]
    rows = block.shape[0]
    whole = jnp.zeros(((count + 1) * rows,) + block.shape[1:], block.dtype)
    for piece, owner, ok in zip(got, owners, valid):
        place = jnp.where(ok, owner, count) * rows
        whole = lax.dynamic_update_slice_in_dim(whole, piece, place, 0)
    return whole[: count * rows]


def tree_slots(ctx_index, levels):
    partner = jnp.bitwise_xor(ctx_index, 1)
    owners, valid = [], []
    for step in range(1, levels):
        owners.append(ctx_index - 2 * step)
        valid.append(ctx_index >= 2 * step)
    owners.append(ctx_index - 1)
    valid.append(ctx_index % 2 == 1)
    for step in range(1, levels):
        owners.append(partner - 2 * step)
        valid.append(ctx_index >= 2 * step)
    return owners, valid


def tree_return(slot_parts, levels):
    count = 2 * levels
    climbed = slot_parts[: levels - 1]
    crossed = slot_parts[levels - 1 :]
    back = [lax.ppermute(crossed[0], "ctx", [(c, c - 1) for c in range(1, count, 2)])]
    for step in range(1, levels):
        back.append(
            lax.ppermute(crossed[step], "ctx", [(c, c ^ 1) for c in range(2 * step, count)])
        )
    total = back[0].astype(jnp.float32)
    carry = None
    for step in range(levels - 1, 0, -1):
        acc = climbed[step - 1].astype(jnp.float32) + back[step].astype(jnp.float32)
        if carry is not None:
            acc = acc + carry.astype(jnp.float32)
        carry = lax.ppermute(
            acc.astype(jnp.bfloat16), "ctx", [(c, c - 2) for c in range(2 * step, count)]
        )
    if carry is not None:
        total = total + carry.astype(jnp.float32)
    return total


def shifted(block, axis, distance):
    devices = range(lax.axis_size(axis))
    route = [(i - distance, i) for i in devices if i - distance in devices]
    return lax.ppermute(block, axis, route)


def shards(
    normed_input,
    queries,
    keys,
    value_projection,
    adapter_down,
    adapter_up,
    output_gradient,
    policy_logprob,
    reference_logprob,
    token_pair_index,
):
    tok_rows = normed_input.shape[1]
    width_kv = keys.shape[2]
    kv_heads = width_kv // HEAD_SIZE
    group_size = queries.shape[2] // width_kv
    hidden_rows = normed_input[0]
    own_keys = keys[0]
    pair_index = lax.axis_index("pair")
    ctx_index = lax.axis_index("ctx")
    half_cols = width_kv // 2
    own_half = lax.dynamic_slice_in_dim(value_projection, pair_index * half_cols, half_cols, 1)
    ctx_count = lax.axis_size("ctx")
    if ctx_count % 2 == 0 and 4 <= ctx_count <= 8:
        rows_half = tree_gather(own_half, ctx_index, ctx_count // 2)
    else:
        rows_half = lax.all_gather(own_half, "ctx", axis=0, tiled=True)
    if lax.axis_size("pair") == 2:
        other_half = from_partner(rows_half, "pair", 0)
        full_weight = jnp.zeros((rows_half.shape[0], width_kv), rows_half.dtype)
        full_weight = lax.dynamic_update_slice_in_dim(full_weight, rows_half, pair_index * half_cols, 1)
        full_weight = lax.dynamic_update_slice_in_dim(
            full_weight, other_half, (1 - pair_index) * half_cols, 1
        )
    else:
        full_weight = lax.all_gather(rows_half, "pair", axis=1, tiled=True)
    rank_projection = jnp.dot(hidden_rows, adapter_down, preferred_element_type=jnp.float32).astype(
        jnp.bfloat16
    )
    values = (
        jnp.dot(hidden_rows, full_weight, preferred_element_type=jnp.float32)
        + ADAPTER_SCALE * jnp.dot(rank_projection, adapter_up, preferred_element_type=jnp.float32)
    ).astype(jnp.bfloat16)
    segment_labels = token_pair_index[0]
    seg_table = (segment_labels[:, None] == jnp.arange(SEGS, dtype=jnp.int32)[None, :]).astype(
        jnp.float32
    )
    log_gap = policy_logprob[0] - reference_logprob[0]
    part_diff = jnp.sum(seg_table * log_gap[:, None], 0)
    part_count = jnp.sum(seg_table, 0)
    both_sums = butterfly_sum(jnp.concatenate([part_diff, part_count], 0), ("ctx",))
    own_diff, counts = both_sums[:SEGS], both_sums[SEGS:]
    other_diff = from_partner(own_diff, "pair", 0)
    direction = 1.0 - 2.0 * pair_index.astype(jnp.float32)
    margin = DPO_BETA * (direction * (own_diff - other_diff))
    coef = -direction * DPO_BETA * LOSS_SCALE * jax.nn.sigmoid(-margin)
    starts = jnp.cumsum(counts) - counts
    tok_start = jnp.sum(seg_table * starts[None, :], 1).astype(jnp.int32)
    token_coefficient = jnp.sum(seg_table * coef[None, :], 1)
    ctx_size = lax.axis_size("ctx")
    halo_blocks = min(WINDOW // tok_rows, ctx_size - 1)
    use_tree = halo_blocks == ctx_size - 1 and ctx_size % 2 == 0 and ctx_size >= 4
    levels = ctx_size // 2
    row_iota = jnp.arange(tok_rows, dtype=jnp.int32)
    if use_tree:
        key_blocks = tree_spread(own_keys, levels)
        value_blocks = tree_spread(values, levels)
        owners, valid = tree_slots(ctx_index, levels)
        far = jnp.int32(1 << 30)
        upos = jnp.concatenate(
            [jnp.where(ok, owner * tok_rows + row_iota, far) for owner, ok in zip(owners, valid)]
            + [ctx_index * tok_rows + row_iota],
            0,
        )
    else:
        key_blocks = []
        value_blocks = []
        for distance in range(halo_blocks, 0, -1):
            key_blocks.append(shifted(own_keys, "ctx", distance))
            value_blocks.append(shifted(values, "ctx", distance))
    all_keys = jnp.concatenate(key_blocks + [own_keys], 0)
    all_keys, own_values = lax.optimization_barrier((all_keys, values))
    all_values = jnp.concatenate(value_blocks + [own_values], 0)
    span = all_keys.shape[0]
    tpos = ctx_index * tok_rows + row_iota
    if not use_tree:
        upos = ctx_index * tok_rows - halo_blocks * tok_rows + jnp.arange(span, dtype=jnp.int32)
    allowed = (
        (upos[None, :] <= tpos[:, None])
        & (upos[None, :] > tpos[:, None] - WINDOW)
        & (upos[None, :] >= tok_start[:, None])
    )
    coef_rows = token_coefficient[None, :, None]
    query_rows = queries[0].reshape(tok_rows, kv_heads, group_size, HEAD_SIZE)
    grad_rows = output_gradient[0].reshape(tok_rows, kv_heads, group_size, HEAD_SIZE)
    key_rows = all_keys.reshape(span, kv_heads, HEAD_SIZE)
    value_rows = all_values.reshape(span, kv_heads, HEAD_SIZE)
    scores = ATTN_SCALE * jnp.einsum(
        "tjgd,ljd->jgtl", query_rows, key_rows, preferred_element_type=jnp.float32
    )
    masked = jnp.where(allowed[None, None], scores, NEG_FILL)
    row_max = jnp.max(masked, -1, keepdims=True)
    weights_exp = jnp.where(allowed[None, None], jnp.exp(masked - row_max), 0.0)
    attn_probs = weights_exp / jnp.sum(weights_exp, -1, keepdims=True)
    prob_grad = coef_rows[None] * jnp.einsum(
        "tjgd,ljd->jgtl", grad_rows, value_rows, preferred_element_type=jnp.float32
    )
    row_delta = jnp.sum(attn_probs * prob_grad, -1, keepdims=True)
    score_grad = (ATTN_SCALE * attn_probs * (prob_grad - row_delta)).astype(jnp.bfloat16)
    query_grad = jnp.einsum(
        "jgtl,ljd->tjgd", score_grad, key_rows, preferred_element_type=jnp.float32
    ).astype(jnp.bfloat16).reshape(tok_rows, kv_heads * group_size * HEAD_SIZE)
    key_parts = jnp.einsum(
        "jgtl,tjgd->ljd", score_grad, query_rows, preferred_element_type=jnp.float32
    ).reshape(span, width_kv)
    weighted = (attn_probs * coef_rows[None]).astype(jnp.bfloat16)
    value_parts = jnp.einsum(
        "jgtl,tjgd->ljd", weighted, grad_rows, preferred_element_type=jnp.float32
    ).reshape(span, width_kv)
    key_total = key_parts[halo_blocks * tok_rows :]
    value_total = value_parts[halo_blocks * tok_rows :]
    if use_tree:
        slot_rows = lambda parts: [
            parts[k * tok_rows : (k + 1) * tok_rows].astype(jnp.bfloat16) for k in range(halo_blocks)
        ]
        key_total = key_total + tree_return(slot_rows(key_parts), levels)
        value_total = value_total + tree_return(slot_rows(value_parts), levels)
    else:
        for distance in range(1, halo_blocks + 1):
            block_start = (halo_blocks - distance) * tok_rows
            send_keys = key_parts[block_start : block_start + tok_rows].astype(jnp.bfloat16)
            send_values = value_parts[block_start : block_start + tok_rows].astype(jnp.bfloat16)
            back_keys, back_values = shifted((send_keys, send_values), "ctx", -distance)
            key_total = key_total + back_keys.astype(jnp.float32)
            value_total = value_total + back_values.astype(jnp.float32)
    key_grad = key_total.astype(jnp.bfloat16)
    value_gradient = value_total.astype(jnp.bfloat16)
    rank_middle = jnp.einsum(
        "sj,zj->sz", value_gradient, adapter_up, preferred_element_type=jnp.float32
    ).astype(jnp.bfloat16)
    input_grad = (
        jnp.einsum("tk,dk->td", value_gradient, full_weight, preferred_element_type=jnp.float32)
        + ADAPTER_SCALE
        * jnp.einsum("pb,wb->pw", rank_middle, adapter_down, preferred_element_type=jnp.float32)
    ).astype(jnp.bfloat16)
    up_factor = ADAPTER_SCALE * jnp.einsum(
        "tr,tk->rk", rank_projection, value_gradient, preferred_element_type=jnp.float32
    )
    down_factor = ADAPTER_SCALE * jnp.einsum(
        "td,tr->dr", hidden_rows, rank_middle, preferred_element_type=jnp.float32
    )
    down_size = down_factor.size
    flat = jnp.concatenate([down_factor.reshape(-1), up_factor.reshape(-1)], 0)
    flat = butterfly_sum(flat.reshape(-1, HEAD_SIZE), ("pair", "ctx")).reshape(-1)
    down_gradient = flat[:down_size].reshape(down_factor.shape)
    up_gradient = flat[down_size:].reshape(up_factor.shape)
    return (input_grad[None], query_grad[None], key_grad[None], down_gradient, up_gradient)


def solution(mesh):
    return jax.shard_map(
        shards,
        mesh=mesh,
        in_specs=(
            P(("grp", "pair"), "ctx", None),
            P(("grp", "pair"), "ctx", None),
            P(("grp", "pair"), "ctx", None),
            P("ctx", None),
            P(),
            P(),
            P(("grp", "pair"), "ctx", None),
            P(("grp", "pair"), "ctx"),
            P(("grp", "pair"), "ctx"),
            P(("grp", "pair"), "ctx"),
        ),
        out_specs=(
            P(("grp", "pair"), "ctx", None),
            P(("grp", "pair"), "ctx", None),
            P(("grp", "pair"), "ctx", None),
            P("grp", None),
            P("grp", None),
        ),
        check_vma=False,
    )
```

```python
import jax
import jax.numpy as jnp
from jax import lax
from jax.sharding import PartitionSpec as P

HEAD_SIZE = 128
WINDOW = 1024
SEGS = 8


DPO_BETA = 0.1
LOSS_SCALE = 256.0
ADAPTER_SCALE = 2.0
ATTN_SCALE = 168.0 ** (-0.5)
NEG_FILL = -1e30


def from_partner(shard, axis, stride):
    return lax.ppermute(shard, axis, [(i, i ^ 1 << stride) for i in range(lax.axis_size(axis))])


def butterfly_sum(parts, axes):
    for axis in axes:
        size = lax.axis_size(axis)
        if size & (size - 1):
            parts = lax.psum(parts, axis)
            continue
        stride = 0
        while 1 << stride < size:
            got = from_partner(parts, axis, stride)
            parts = jax.tree.map(jnp.add, parts, got)
            stride += 1
    return parts


def tree_spread(block, levels):
    count = 2 * levels
    climbed = []
    held = block
    for step in range(1, levels):
        held = lax.ppermute(held, "ctx", [(c - 2, c) for c in range(2 * step, count)])
        climbed.append(held)
    crossed = [lax.ppermute(block, "ctx", [(c - 1, c) for c in range(1, count, 2)])]
    for step in range(1, levels):
        crossed.append(
            lax.ppermute(climbed[step - 1], "ctx", [(c ^ 1, c) for c in range(2 * step, count)])
        )
    return climbed + crossed


def tree_gather(block, ctx_index, levels):
    count = 2 * levels
    partner = jnp.bitwise_xor(ctx_index, 1)
    got = [block]
    owners = [ctx_index]
    valid = [ctx_index >= 0]
    up, down = block, block
    ups, downs = [], []
    for step in range(1, levels):
        up = lax.ppermute(up, "ctx", [(c - 2, c) for c in range(2 * step, count)])
        down = lax.ppermute(down, "ctx", [(c + 2, c) for c in range(0, count - 2 * step)])
        ups.append(up)
        downs.append(down)
        got += [up, down]
        owners += [ctx_index - 2 * step, ctx_index + 2 * step]
        valid += [ctx_index >= 2 * step, ctx_index < count - 2 * step]
    got.append(lax.ppermute(block, "ctx", [(c ^ 1, c) for c in range(count)]))
    owners.append(partner)
    valid.append(ctx_index >= 0)
    for step in range(1, levels):
        got.append(lax.ppermute(ups[step - 1], "ctx", [(c ^ 1, c) for c in range(2 * step, count)]))
        got.append(
            lax.ppermute(downs[step - 1], "ctx", [(c ^ 1, c) for c in range(0, count - 2 * step)])
        )
        owners += [partner - 2 * step, partner + 2 * step]
        valid += [ctx_index >= 2 * step, ctx_index < count - 2 * step]
    rows = block.shape[0]
    whole = jnp.zeros(((count + 1) * rows,) + block.shape[1:], block.dtype)
    for piece, owner, ok in zip(got, owners, valid):
        place = jnp.where(ok, owner, count) * rows
        whole = lax.dynamic_update_slice_in_dim(whole, piece, place, 0)
    return whole[: count * rows]


def tree_slots(ctx_index, levels):
    partner = jnp.bitwise_xor(ctx_index, 1)
    owners, valid = [], []
    for step in range(1, levels):
        owners.append(ctx_index - 2 * step)
        valid.append(ctx_index >= 2 * step)
    owners.append(ctx_index - 1)
    valid.append(ctx_index % 2 == 1)
    for step in range(1, levels):
        owners.append(partner - 2 * step)
        valid.append(ctx_index >= 2 * step)
    return owners, valid


def tree_return(slot_parts, levels):
    count = 2 * levels
    climbed = slot_parts[: levels - 1]
    crossed = slot_parts[levels - 1 :]
    back = [lax.ppermute(crossed[0], "ctx", [(c, c - 1) for c in range(1, count, 2)])]
    for step in range(1, levels):
        back.append(
            lax.ppermute(crossed[step], "ctx", [(c, c ^ 1) for c in range(2 * step, count)])
        )
    total = back[0].astype(jnp.float32)
    carry = None
    for step in range(levels - 1, 0, -1):
        acc = climbed[step - 1].astype(jnp.float32) + back[step].astype(jnp.float32)
        if carry is not None:
            acc = acc + carry.astype(jnp.float32)
        carry = lax.ppermute(
            acc.astype(jnp.bfloat16), "ctx", [(c, c - 2) for c in range(2 * step, count)]
        )
    if carry is not None:
        total = total + carry.astype(jnp.float32)
    return total


def shifted(block, axis, distance):
    devices = range(lax.axis_size(axis))
    route = [(i - distance, i) for i in devices if i - distance in devices]
    return lax.ppermute(block, axis, route)


def shards(
    normed_input,
    queries,
    keys,
    value_projection,
    adapter_down,
    adapter_up,
    output_gradient,
    policy_logprob,
    reference_logprob,
    token_pair_index,
):
    tok_rows = normed_input.shape[1]
    width_kv = keys.shape[2]
    kv_heads = width_kv // HEAD_SIZE
    group_size = queries.shape[2] // width_kv
    hidden_rows = normed_input[0]
    own_keys = keys[0]
    pair_index = lax.axis_index("pair")
    ctx_index = lax.axis_index("ctx")
    half_cols = width_kv // 2
    own_half = lax.dynamic_slice_in_dim(value_projection, pair_index * half_cols, half_cols, 1)
    ctx_count = lax.axis_size("ctx")
    if ctx_count % 2 == 0 and 4 <= ctx_count <= 8:
        rows_half = tree_gather(own_half, ctx_index, ctx_count // 2)
    else:
        rows_half = lax.all_gather(own_half, "ctx", axis=0, tiled=True)
    if lax.axis_size("pair") == 2:
        other_half = from_partner(rows_half, "pair", 0)
        full_weight = jnp.zeros((rows_half.shape[0], width_kv), rows_half.dtype)
        full_weight = lax.dynamic_update_slice_in_dim(full_weight, rows_half, pair_index * half_cols, 1)
        full_weight = lax.dynamic_update_slice_in_dim(
            full_weight, other_half, (1 - pair_index) * half_cols, 1
        )
    else:
        full_weight = lax.all_gather(rows_half, "pair", axis=1, tiled=True)
    rank_projection = jnp.dot(hidden_rows, adapter_down, preferred_element_type=jnp.float32).astype(
        jnp.bfloat16
    )
    values = (
        jnp.dot(hidden_rows, full_weight, preferred_element_type=jnp.float32)
        + ADAPTER_SCALE * jnp.dot(rank_projection, adapter_up, preferred_element_type=jnp.float32)
    ).astype(jnp.bfloat16)
    segment_labels = token_pair_index[0]
    seg_table = (segment_labels[:, None] == jnp.arange(SEGS, dtype=jnp.int32)[None, :]).astype(
        jnp.float32
    )
    log_gap = policy_logprob[0] - reference_logprob[0]
    part_diff = jnp.sum(seg_table * log_gap[:, None], 0)
    part_count = jnp.sum(seg_table, 0)
    both_sums = butterfly_sum(jnp.concatenate([part_diff, part_count], 0), ("ctx",))
    own_diff, counts = both_sums[:SEGS], both_sums[SEGS:]
    other_diff = from_partner(own_diff, "pair", 0)
    direction = 1.0 - 2.0 * pair_index.astype(jnp.float32)
    margin = DPO_BETA * (direction * (own_diff - other_diff))
    coef = -direction * DPO_BETA * LOSS_SCALE * jax.nn.sigmoid(-margin)
    starts = jnp.cumsum(counts) - counts
    tok_start = jnp.sum(seg_table * starts[None, :], 1).astype(jnp.int32)
    token_coefficient = jnp.sum(seg_table * coef[None, :], 1)
    ctx_size = lax.axis_size("ctx")
    halo_blocks = min(WINDOW // tok_rows, ctx_size - 1)
    use_tree = halo_blocks == ctx_size - 1 and ctx_size % 2 == 0 and ctx_size >= 4
    levels = ctx_size // 2
    row_iota = jnp.arange(tok_rows, dtype=jnp.int32)
    if use_tree:
        joined_blocks = tree_spread(jnp.concatenate([own_keys, values], 1), levels)
        key_blocks = [block[:, :width_kv] for block in joined_blocks]
        value_blocks = [block[:, width_kv:] for block in joined_blocks]
        owners, valid = tree_slots(ctx_index, levels)
        far = jnp.int32(1 << 30)
        upos = jnp.concatenate(
            [jnp.where(ok, owner * tok_rows + row_iota, far) for owner, ok in zip(owners, valid)]
            + [ctx_index * tok_rows + row_iota],
            0,
        )
    else:
        key_blocks = []
        value_blocks = []
        for distance in range(halo_blocks, 0, -1):
            key_blocks.append(shifted(own_keys, "ctx", distance))
            value_blocks.append(shifted(values, "ctx", distance))
    all_keys = jnp.concatenate(key_blocks + [own_keys], 0)
    all_keys, own_values = lax.optimization_barrier((all_keys, values))
    all_values = jnp.concatenate(value_blocks + [own_values], 0)
    span = all_keys.shape[0]
    tpos = ctx_index * tok_rows + row_iota
    if not use_tree:
        upos = ctx_index * tok_rows - halo_blocks * tok_rows + jnp.arange(span, dtype=jnp.int32)
    allowed = (
        (upos[None, :] <= tpos[:, None])
        & (upos[None, :] > tpos[:, None] - WINDOW)
        & (upos[None, :] >= tok_start[:, None])
    )
    coef_rows = token_coefficient[None, :, None]
    query_rows = queries[0].reshape(tok_rows, kv_heads, group_size, HEAD_SIZE)
    grad_rows = output_gradient[0].reshape(tok_rows, kv_heads, group_size, HEAD_SIZE)
    key_rows = all_keys.reshape(span, kv_heads, HEAD_SIZE)
    value_rows = all_values.reshape(span, kv_heads, HEAD_SIZE)
    scores = ATTN_SCALE * jnp.einsum(
        "tjgd,ljd->jgtl", query_rows, key_rows, preferred_element_type=jnp.float32
    )
    masked = jnp.where(allowed[None, None], scores, NEG_FILL)
    row_max = jnp.max(masked, -1, keepdims=True)
    weights_exp = jnp.where(allowed[None, None], jnp.exp(masked - row_max), 0.0)
    attn_probs = weights_exp / jnp.sum(weights_exp, -1, keepdims=True)
    prob_grad = coef_rows[None] * jnp.einsum(
        "tjgd,ljd->jgtl", grad_rows, value_rows, preferred_element_type=jnp.float32
    )
    row_delta = jnp.sum(attn_probs * prob_grad, -1, keepdims=True)
    score_grad = (ATTN_SCALE * attn_probs * (prob_grad - row_delta)).astype(jnp.bfloat16)
    query_grad = jnp.einsum(
        "jgtl,ljd->tjgd", score_grad, key_rows, preferred_element_type=jnp.float32
    ).astype(jnp.bfloat16).reshape(tok_rows, kv_heads * group_size * HEAD_SIZE)
    key_parts = jnp.einsum(
        "jgtl,tjgd->ljd", score_grad, query_rows, preferred_element_type=jnp.float32
    ).reshape(span, width_kv)
    weighted = (attn_probs * coef_rows[None]).astype(jnp.bfloat16)
    value_parts = jnp.einsum(
        "jgtl,tjgd->ljd", weighted, grad_rows, preferred_element_type=jnp.float32
    ).reshape(span, width_kv)
    key_total = key_parts[halo_blocks * tok_rows :]
    value_total = value_parts[halo_blocks * tok_rows :]
    if use_tree:
        slot_rows = lambda parts: [
            parts[k * tok_rows : (k + 1) * tok_rows].astype(jnp.bfloat16) for k in range(halo_blocks)
        ]
        key_total = key_total + tree_return(slot_rows(key_parts), levels)
        value_total = value_total + tree_return(slot_rows(value_parts), levels)
    else:
        for distance in range(1, halo_blocks + 1):
            block_start = (halo_blocks - distance) * tok_rows
            send_keys = key_parts[block_start : block_start + tok_rows].astype(jnp.bfloat16)
            send_values = value_parts[block_start : block_start + tok_rows].astype(jnp.bfloat16)
            back_keys, back_values = shifted((send_keys, send_values), "ctx", -distance)
            key_total = key_total + back_keys.astype(jnp.float32)
            value_total = value_total + back_values.astype(jnp.float32)
    key_grad = key_total.astype(jnp.bfloat16)
    value_gradient = value_total.astype(jnp.bfloat16)
    rank_middle = jnp.einsum(
        "sj,zj->sz", value_gradient, adapter_up, preferred_element_type=jnp.float32
    ).astype(jnp.bfloat16)
    input_grad = (
        jnp.einsum("tk,dk->td", value_gradient, full_weight, preferred_element_type=jnp.float32)
        + ADAPTER_SCALE
        * jnp.einsum("pb,wb->pw", rank_middle, adapter_down, preferred_element_type=jnp.float32)
    ).astype(jnp.bfloat16)
    up_factor = ADAPTER_SCALE * jnp.einsum(
        "tr,tk->rk", rank_projection, value_gradient, preferred_element_type=jnp.float32
    )
    down_factor = ADAPTER_SCALE * jnp.einsum(
        "td,tr->dr", hidden_rows, rank_middle, preferred_element_type=jnp.float32
    )
    down_size = down_factor.size
    flat = jnp.concatenate([down_factor.reshape(-1), up_factor.reshape(-1)], 0)
    flat = butterfly_sum(flat.reshape(-1, HEAD_SIZE), ("pair", "ctx")).reshape(-1)
    down_gradient = flat[:down_size].reshape(down_factor.shape)
    up_gradient = flat[down_size:].reshape(up_factor.shape)
    return (input_grad[None], query_grad[None], key_grad[None], down_gradient, up_gradient)


def solution(mesh):
    return jax.shard_map(
        shards,
        mesh=mesh,
        in_specs=(
            P(("grp", "pair"), "ctx", None),
            P(("grp", "pair"), "ctx", None),
            P(("grp", "pair"), "ctx", None),
            P("ctx", None),
            P(),
            P(),
            P(("grp", "pair"), "ctx", None),
            P(("grp", "pair"), "ctx"),
            P(("grp", "pair"), "ctx"),
            P(("grp", "pair"), "ctx"),
        ),
        out_specs=(
            P(("grp", "pair"), "ctx", None),
            P(("grp", "pair"), "ctx", None),
            P(("grp", "pair"), "ctx", None),
            P("grp", None),
            P("grp", None),
        ),
        check_vma=False,
    )
```

```python
import jax
import jax.numpy as jnp
from jax import lax
from jax.sharding import PartitionSpec as P

HEAD_SIZE = 128
WINDOW = 1024
SEGS = 8


DPO_BETA = 0.1
LOSS_SCALE = 256.0
ADAPTER_SCALE = 2.0
ATTN_SCALE = 168.0 ** (-0.5)
NEG_FILL = -1e30


def from_partner(shard, axis, stride):
    return lax.ppermute(shard, axis, [(i, i ^ 1 << stride) for i in range(lax.axis_size(axis))])


def butterfly_sum(parts, axes):
    for axis in axes:
        size = lax.axis_size(axis)
        if size & (size - 1):
            parts = lax.psum(parts, axis)
            continue
        stride = 0
        while 1 << stride < size:
            got = from_partner(parts, axis, stride)
            parts = jax.tree.map(jnp.add, parts, got)
            stride += 1
    return parts


def tree_spread(block, levels):
    count = 2 * levels
    climbed = []
    held = block
    for step in range(1, levels):
        held = lax.ppermute(held, "ctx", [(c - 2, c) for c in range(2 * step, count)])
        climbed.append(held)
    crossed = [lax.ppermute(block, "ctx", [(c - 1, c) for c in range(1, count, 2)])]
    for step in range(1, levels):
        crossed.append(
            lax.ppermute(climbed[step - 1], "ctx", [(c ^ 1, c) for c in range(2 * step, count)])
        )
    return climbed + crossed


def tree_gather(block, ctx_index, levels):
    count = 2 * levels
    partner = jnp.bitwise_xor(ctx_index, 1)
    got = [block]
    owners = [ctx_index]
    valid = [ctx_index >= 0]
    up, down = block, block
    ups, downs = [], []
    for step in range(1, levels):
        up = lax.ppermute(up, "ctx", [(c - 2, c) for c in range(2 * step, count)])
        down = lax.ppermute(down, "ctx", [(c + 2, c) for c in range(0, count - 2 * step)])
        ups.append(up)
        downs.append(down)
        got += [up, down]
        owners += [ctx_index - 2 * step, ctx_index + 2 * step]
        valid += [ctx_index >= 2 * step, ctx_index < count - 2 * step]
    got.append(lax.ppermute(block, "ctx", [(c ^ 1, c) for c in range(count)]))
    owners.append(partner)
    valid.append(ctx_index >= 0)
    for step in range(1, levels):
        got.append(lax.ppermute(ups[step - 1], "ctx", [(c ^ 1, c) for c in range(2 * step, count)]))
        got.append(
            lax.ppermute(downs[step - 1], "ctx", [(c ^ 1, c) for c in range(0, count - 2 * step)])
        )
        owners += [partner - 2 * step, partner + 2 * step]
        valid += [ctx_index >= 2 * step, ctx_index < count - 2 * step]
    rows = block.shape[0]
    whole = jnp.zeros(((count + 1) * rows,) + block.shape[1:], block.dtype)
    for piece, owner, ok in zip(got, owners, valid):
        place = jnp.where(ok, owner, count) * rows
        whole = lax.dynamic_update_slice_in_dim(whole, piece, place, 0)
    return whole[: count * rows]


def tree_slots(ctx_index, levels):
    partner = jnp.bitwise_xor(ctx_index, 1)
    owners, valid = [], []
    for step in range(1, levels):
        owners.append(ctx_index - 2 * step)
        valid.append(ctx_index >= 2 * step)
    owners.append(ctx_index - 1)
    valid.append(ctx_index % 2 == 1)
    for step in range(1, levels):
        owners.append(partner - 2 * step)
        valid.append(ctx_index >= 2 * step)
    return owners, valid


def tree_return(slot_parts, levels):
    count = 2 * levels
    climbed = slot_parts[: levels - 1]
    crossed = slot_parts[levels - 1 :]
    back = [lax.ppermute(crossed[0], "ctx", [(c, c - 1) for c in range(1, count, 2)])]
    for step in range(1, levels):
        back.append(
            lax.ppermute(crossed[step], "ctx", [(c, c ^ 1) for c in range(2 * step, count)])
        )
    total = back[0].astype(jnp.float32)
    for step in range(1, levels):
        acc = climbed[step - 1].astype(jnp.float32) + back[step].astype(jnp.float32)
        home = lax.ppermute(
            acc.astype(jnp.bfloat16), "ctx", [(c, c - 2 * step) for c in range(2 * step, count)]
        )
        total = total + home.astype(jnp.float32)
    return total


def shifted(block, axis, distance):
    devices = range(lax.axis_size(axis))
    route = [(i - distance, i) for i in devices if i - distance in devices]
    return lax.ppermute(block, axis, route)


def shards(
    normed_input,
    queries,
    keys,
    value_projection,
    adapter_down,
    adapter_up,
    output_gradient,
    policy_logprob,
    reference_logprob,
    token_pair_index,
):
    tok_rows = normed_input.shape[1]
    width_kv = keys.shape[2]
    kv_heads = width_kv // HEAD_SIZE
    group_size = queries.shape[2] // width_kv
    hidden_rows = normed_input[0]
    own_keys = keys[0]
    pair_index = lax.axis_index("pair")
    ctx_index = lax.axis_index("ctx")
    half_cols = width_kv // 2
    own_half = lax.dynamic_slice_in_dim(value_projection, pair_index * half_cols, half_cols, 1)
    ctx_count = lax.axis_size("ctx")
    if ctx_count % 2 == 0 and 4 <= ctx_count <= 8:
        rows_half = tree_gather(own_half, ctx_index, ctx_count // 2)
    else:
        rows_half = lax.all_gather(own_half, "ctx", axis=0, tiled=True)
    if lax.axis_size("pair") == 2:
        other_half = from_partner(rows_half, "pair", 0)
        full_weight = jnp.zeros((rows_half.shape[0], width_kv), rows_half.dtype)
        full_weight = lax.dynamic_update_slice_in_dim(full_weight, rows_half, pair_index * half_cols, 1)
        full_weight = lax.dynamic_update_slice_in_dim(
            full_weight, other_half, (1 - pair_index) * half_cols, 1
        )
    else:
        full_weight = lax.all_gather(rows_half, "pair", axis=1, tiled=True)
    rank_projection = jnp.dot(hidden_rows, adapter_down, preferred_element_type=jnp.float32).astype(
        jnp.bfloat16
    )
    values = (
        jnp.dot(hidden_rows, full_weight, preferred_element_type=jnp.float32)
        + ADAPTER_SCALE * jnp.dot(rank_projection, adapter_up, preferred_element_type=jnp.float32)
    ).astype(jnp.bfloat16)
    segment_labels = token_pair_index[0]
    seg_table = (segment_labels[:, None] == jnp.arange(SEGS, dtype=jnp.int32)[None, :]).astype(
        jnp.float32
    )
    log_gap = policy_logprob[0] - reference_logprob[0]
    part_diff = jnp.sum(seg_table * log_gap[:, None], 0)
    part_count = jnp.sum(seg_table, 0)
    both_sums = butterfly_sum(jnp.concatenate([part_diff, part_count], 0), ("ctx",))
    own_diff, counts = both_sums[:SEGS], both_sums[SEGS:]
    other_diff = from_partner(own_diff, "pair", 0)
    direction = 1.0 - 2.0 * pair_index.astype(jnp.float32)
    margin = DPO_BETA * (direction * (own_diff - other_diff))
    coef = -direction * DPO_BETA * LOSS_SCALE * jax.nn.sigmoid(-margin)
    starts = jnp.cumsum(counts) - counts
    tok_start = jnp.sum(seg_table * starts[None, :], 1).astype(jnp.int32)
    token_coefficient = jnp.sum(seg_table * coef[None, :], 1)
    ctx_size = lax.axis_size("ctx")
    halo_blocks = min(WINDOW // tok_rows, ctx_size - 1)
    use_tree = halo_blocks == ctx_size - 1 and ctx_size % 2 == 0 and ctx_size >= 4
    levels = ctx_size // 2
    row_iota = jnp.arange(tok_rows, dtype=jnp.int32)
    if use_tree:
        key_blocks = tree_spread(own_keys, levels)
        value_blocks = tree_spread(values, levels)
        owners, valid = tree_slots(ctx_index, levels)
        far = jnp.int32(1 << 30)
        upos = jnp.concatenate(
            [jnp.where(ok, owner * tok_rows + row_iota, far) for owner, ok in zip(owners, valid)]
            + [ctx_index * tok_rows + row_iota],
            0,
        )
    else:
        key_blocks = []
        value_blocks = []
        for distance in range(halo_blocks, 0, -1):
            key_blocks.append(shifted(own_keys, "ctx", distance))
            value_blocks.append(shifted(values, "ctx", distance))
    all_keys = jnp.concatenate(key_blocks + [own_keys], 0)
    all_keys, own_values = lax.optimization_barrier((all_keys, values))
    all_values = jnp.concatenate(value_blocks + [own_values], 0)
    span = all_keys.shape[0]
    tpos = ctx_index * tok_rows + row_iota
    if not use_tree:
        upos = ctx_index * tok_rows - halo_blocks * tok_rows + jnp.arange(span, dtype=jnp.int32)
    allowed = (
        (upos[None, :] <= tpos[:, None])
        & (upos[None, :] > tpos[:, None] - WINDOW)
        & (upos[None, :] >= tok_start[:, None])
    )
    coef_rows = token_coefficient[None, :, None]
    query_rows = queries[0].reshape(tok_rows, kv_heads, group_size, HEAD_SIZE)
    grad_rows = output_gradient[0].reshape(tok_rows, kv_heads, group_size, HEAD_SIZE)
    key_rows = all_keys.reshape(span, kv_heads, HEAD_SIZE)
    value_rows = all_values.reshape(span, kv_heads, HEAD_SIZE)
    scores = ATTN_SCALE * jnp.einsum(
        "tjgd,ljd->jgtl", query_rows, key_rows, preferred_element_type=jnp.float32
    )
    masked = jnp.where(allowed[None, None], scores, NEG_FILL)
    row_max = jnp.max(masked, -1, keepdims=True)
    weights_exp = jnp.where(allowed[None, None], jnp.exp(masked - row_max), 0.0)
    attn_probs = weights_exp / jnp.sum(weights_exp, -1, keepdims=True)
    prob_grad = coef_rows[None] * jnp.einsum(
        "tjgd,ljd->jgtl", grad_rows, value_rows, preferred_element_type=jnp.float32
    )
    row_delta = jnp.sum(attn_probs * prob_grad, -1, keepdims=True)
    score_grad = (ATTN_SCALE * attn_probs * (prob_grad - row_delta)).astype(jnp.bfloat16)
    query_grad = jnp.einsum(
        "jgtl,ljd->tjgd", score_grad, key_rows, preferred_element_type=jnp.float32
    ).astype(jnp.bfloat16).reshape(tok_rows, kv_heads * group_size * HEAD_SIZE)
    key_parts = jnp.einsum(
        "jgtl,tjgd->ljd", score_grad, query_rows, preferred_element_type=jnp.float32
    ).reshape(span, width_kv)
    weighted = (attn_probs * coef_rows[None]).astype(jnp.bfloat16)
    value_parts = jnp.einsum(
        "jgtl,tjgd->ljd", weighted, grad_rows, preferred_element_type=jnp.float32
    ).reshape(span, width_kv)
    key_total = key_parts[halo_blocks * tok_rows :]
    value_total = value_parts[halo_blocks * tok_rows :]
    if use_tree:
        slot_rows = lambda parts: [
            parts[k * tok_rows : (k + 1) * tok_rows].astype(jnp.bfloat16) for k in range(halo_blocks)
        ]
        key_total = key_total + tree_return(slot_rows(key_parts), levels)
        value_total = value_total + tree_return(slot_rows(value_parts), levels)
    else:
        for distance in range(1, halo_blocks + 1):
            block_start = (halo_blocks - distance) * tok_rows
            send_keys = key_parts[block_start : block_start + tok_rows].astype(jnp.bfloat16)
            send_values = value_parts[block_start : block_start + tok_rows].astype(jnp.bfloat16)
            back_keys, back_values = shifted((send_keys, send_values), "ctx", -distance)
            key_total = key_total + back_keys.astype(jnp.float32)
            value_total = value_total + back_values.astype(jnp.float32)
    key_grad = key_total.astype(jnp.bfloat16)
    value_gradient = value_total.astype(jnp.bfloat16)
    rank_middle = jnp.einsum(
        "sj,zj->sz", value_gradient, adapter_up, preferred_element_type=jnp.float32
    ).astype(jnp.bfloat16)
    input_grad = (
        jnp.einsum("tk,dk->td", value_gradient, full_weight, preferred_element_type=jnp.float32)
        + ADAPTER_SCALE
        * jnp.einsum("pb,wb->pw", rank_middle, adapter_down, preferred_element_type=jnp.float32)
    ).astype(jnp.bfloat16)
    up_factor = ADAPTER_SCALE * jnp.einsum(
        "tr,tk->rk", rank_projection, value_gradient, preferred_element_type=jnp.float32
    )
    down_factor = ADAPTER_SCALE * jnp.einsum(
        "td,tr->dr", hidden_rows, rank_middle, preferred_element_type=jnp.float32
    )
    down_size = down_factor.size
    flat = jnp.concatenate([down_factor.reshape(-1), up_factor.reshape(-1)], 0)
    flat = butterfly_sum(flat.reshape(-1, HEAD_SIZE), ("pair", "ctx")).reshape(-1)
    down_gradient = flat[:down_size].reshape(down_factor.shape)
    up_gradient = flat[down_size:].reshape(up_factor.shape)
    return (input_grad[None], query_grad[None], key_grad[None], down_gradient, up_gradient)


def solution(mesh):
    return jax.shard_map(
        shards,
        mesh=mesh,
        in_specs=(
            P(("grp", "pair"), "ctx", None),
            P(("grp", "pair"), "ctx", None),
            P(("grp", "pair"), "ctx", None),
            P("ctx", None),
            P(),
            P(),
            P(("grp", "pair"), "ctx", None),
            P(("grp", "pair"), "ctx"),
            P(("grp", "pair"), "ctx"),
            P(("grp", "pair"), "ctx"),
        ),
        out_specs=(
            P(("grp", "pair"), "ctx", None),
            P(("grp", "pair"), "ctx", None),
            P(("grp", "pair"), "ctx", None),
            P("grp", None),
            P("grp", None),
        ),
        check_vma=False,
    )
```

```python
import jax
import jax.numpy as jnp
from jax import lax
from jax.sharding import PartitionSpec as P

HEAD_SIZE = 128
WINDOW = 1024
SEGS = 8


DPO_BETA = 0.1
LOSS_SCALE = 256.0
ADAPTER_SCALE = 2.0
ATTN_SCALE = 168.0 ** (-0.5)
NEG_FILL = -1e30


def from_partner(shard, axis, stride):
    return lax.ppermute(shard, axis, [(i, i ^ 1 << stride) for i in range(lax.axis_size(axis))])


def butterfly_sum(parts, axes):
    for axis in axes:
        size = lax.axis_size(axis)
        if size & (size - 1):
            parts = lax.psum(parts, axis)
            continue
        stride = 0
        while 1 << stride < size:
            got = from_partner(parts, axis, stride)
            parts = jax.tree.map(jnp.add, parts, got)
            stride += 1
    return parts


def tree_spread(block, levels):
    count = 2 * levels
    climbed = []
    held = block
    for step in range(1, levels):
        held = lax.ppermute(held, "ctx", [(c - 2, c) for c in range(2 * step, count)])
        climbed.append(held)
    crossed = [lax.ppermute(block, "ctx", [(c - 1, c) for c in range(1, count, 2)])]
    for step in range(1, levels):
        crossed.append(
            lax.ppermute(climbed[step - 1], "ctx", [(c ^ 1, c) for c in range(2 * step, count)])
        )
    return climbed + crossed


def tree_gather(block, ctx_index, levels):
    count = 2 * levels
    partner = jnp.bitwise_xor(ctx_index, 1)
    got = [block]
    owners = [ctx_index]
    valid = [ctx_index >= 0]
    up, down = block, block
    ups, downs = [], []
    for step in range(1, levels):
        up = lax.ppermute(up, "ctx", [(c - 2, c) for c in range(2 * step, count)])
        down = lax.ppermute(down, "ctx", [(c + 2, c) for c in range(0, count - 2 * step)])
        ups.append(up)
        downs.append(down)
        got += [up, down]
        owners += [ctx_index - 2 * step, ctx_index + 2 * step]
        valid += [ctx_index >= 2 * step, ctx_index < count - 2 * step]
    got.append(lax.ppermute(block, "ctx", [(c ^ 1, c) for c in range(count)]))
    owners.append(partner)
    valid.append(ctx_index >= 0)
    for step in range(1, levels):
        got.append(lax.ppermute(ups[step - 1], "ctx", [(c ^ 1, c) for c in range(2 * step, count)]))
        got.append(
            lax.ppermute(downs[step - 1], "ctx", [(c ^ 1, c) for c in range(0, count - 2 * step)])
        )
        owners += [partner - 2 * step, partner + 2 * step]
        valid += [ctx_index >= 2 * step, ctx_index < count - 2 * step]
    rows = block.shape[0]
    whole = jnp.zeros(((count + 1) * rows,) + block.shape[1:], block.dtype)
    for piece, owner, ok in zip(got, owners, valid):
        place = jnp.where(ok, owner, count) * rows
        whole = lax.dynamic_update_slice_in_dim(whole, piece, place, 0)
    return whole[: count * rows]


def tree_slots(ctx_index, levels):
    partner = jnp.bitwise_xor(ctx_index, 1)
    owners, valid = [], []
    for step in range(1, levels):
        owners.append(ctx_index - 2 * step)
        valid.append(ctx_index >= 2 * step)
    owners.append(ctx_index - 1)
    valid.append(ctx_index % 2 == 1)
    for step in range(1, levels):
        owners.append(partner - 2 * step)
        valid.append(ctx_index >= 2 * step)
    return owners, valid


def tree_return(slot_parts, levels):
    count = 2 * levels
    climbed = slot_parts[: levels - 1]
    crossed = slot_parts[levels - 1 :]
    back = [lax.ppermute(crossed[0], "ctx", [(c, c - 1) for c in range(1, count, 2)])]
    for step in range(1, levels):
        back.append(
            lax.ppermute(crossed[step], "ctx", [(c, c ^ 1) for c in range(2 * step, count)])
        )
    total = back[0].astype(jnp.float32)
    carry = None
    for step in range(levels - 1, 0, -1):
        acc = climbed[step - 1].astype(jnp.float32) + back[step].astype(jnp.float32)
        if carry is not None:
            acc = acc + carry.astype(jnp.float32)
        carry = lax.ppermute(
            acc.astype(jnp.bfloat16), "ctx", [(c, c - 2) for c in range(2 * step, count)]
        )
    if carry is not None:
        total = total + carry.astype(jnp.float32)
    return total


def shifted(block, axis, distance):
    devices = range(lax.axis_size(axis))
    route = [(i - distance, i) for i in devices if i - distance in devices]
    return lax.ppermute(block, axis, route)


def shards(
    normed_input,
    queries,
    keys,
    value_projection,
    adapter_down,
    adapter_up,
    output_gradient,
    policy_logprob,
    reference_logprob,
    token_pair_index,
):
    tok_rows = normed_input.shape[1]
    width_kv = keys.shape[2]
    kv_heads = width_kv // HEAD_SIZE
    group_size = queries.shape[2] // width_kv
    hidden_rows = normed_input[0]
    own_keys = keys[0]
    pair_index = lax.axis_index("pair")
    ctx_index = lax.axis_index("ctx")
    half_cols = width_kv // 2
    own_half = lax.dynamic_slice_in_dim(value_projection, pair_index * half_cols, half_cols, 1)
    ctx_count = lax.axis_size("ctx")
    if ctx_count % 2 == 0 and 4 <= ctx_count <= 8:
        rows_half = tree_gather(own_half, ctx_index, ctx_count // 2)
    else:
        rows_half = lax.all_gather(own_half, "ctx", axis=0, tiled=True)
    split_pair = lax.axis_size("pair") == 2
    if split_pair:
        other_half = from_partner(rows_half, "pair", 0)
        mine_at = pair_index * half_cols
        other_at = (1 - pair_index) * half_cols
    else:
        full_weight = lax.all_gather(rows_half, "pair", axis=1, tiled=True)
    rank_projection = jnp.dot(hidden_rows, adapter_down, preferred_element_type=jnp.float32).astype(
        jnp.bfloat16
    )
    low_up = ADAPTER_SCALE * jnp.dot(rank_projection, adapter_up, preferred_element_type=jnp.float32)
    if split_pair:
        mine_cols = jnp.dot(hidden_rows, rows_half, preferred_element_type=jnp.float32)
        other_cols = jnp.dot(hidden_rows, other_half, preferred_element_type=jnp.float32)
        values = jnp.zeros((tok_rows, width_kv), jnp.float32)
        values = lax.dynamic_update_slice_in_dim(values, mine_cols, mine_at, 1)
        values = lax.dynamic_update_slice_in_dim(values, other_cols, other_at, 1)
        values = (values + low_up).astype(jnp.bfloat16)
    else:
        values = (
            jnp.dot(hidden_rows, full_weight, preferred_element_type=jnp.float32) + low_up
        ).astype(jnp.bfloat16)
    segment_labels = token_pair_index[0]
    seg_table = (segment_labels[:, None] == jnp.arange(SEGS, dtype=jnp.int32)[None, :]).astype(
        jnp.float32
    )
    log_gap = policy_logprob[0] - reference_logprob[0]
    part_diff = jnp.sum(seg_table * log_gap[:, None], 0)
    part_count = jnp.sum(seg_table, 0)
    both_sums = butterfly_sum(jnp.concatenate([part_diff, part_count], 0), ("ctx",))
    own_diff, counts = both_sums[:SEGS], both_sums[SEGS:]
    other_diff = from_partner(own_diff, "pair", 0)
    direction = 1.0 - 2.0 * pair_index.astype(jnp.float32)
    margin = DPO_BETA * (direction * (own_diff - other_diff))
    coef = -direction * DPO_BETA * LOSS_SCALE * jax.nn.sigmoid(-margin)
    starts = jnp.cumsum(counts) - counts
    tok_start = jnp.sum(seg_table * starts[None, :], 1).astype(jnp.int32)
    token_coefficient = jnp.sum(seg_table * coef[None, :], 1)
    ctx_size = lax.axis_size("ctx")
    halo_blocks = min(WINDOW // tok_rows, ctx_size - 1)
    use_tree = halo_blocks == ctx_size - 1 and ctx_size % 2 == 0 and ctx_size >= 4
    levels = ctx_size // 2
    row_iota = jnp.arange(tok_rows, dtype=jnp.int32)
    if use_tree:
        key_blocks = tree_spread(own_keys, levels)
        value_blocks = tree_spread(values, levels)
        owners, valid = tree_slots(ctx_index, levels)
        far = jnp.int32(1 << 30)
        upos = jnp.concatenate(
            [jnp.where(ok, owner * tok_rows + row_iota, far) for owner, ok in zip(owners, valid)]
            + [ctx_index * tok_rows + row_iota],
            0,
        )
    else:
        key_blocks = []
        value_blocks = []
        for distance in range(halo_blocks, 0, -1):
            key_blocks.append(shifted(own_keys, "ctx", distance))
            value_blocks.append(shifted(values, "ctx", distance))
    all_keys = jnp.concatenate(key_blocks + [own_keys], 0)
    all_keys, own_values = lax.optimization_barrier((all_keys, values))
    all_values = jnp.concatenate(value_blocks + [own_values], 0)
    span = all_keys.shape[0]
    tpos = ctx_index * tok_rows + row_iota
    if not use_tree:
        upos = ctx_index * tok_rows - halo_blocks * tok_rows + jnp.arange(span, dtype=jnp.int32)
    allowed = (
        (upos[None, :] <= tpos[:, None])
        & (upos[None, :] > tpos[:, None] - WINDOW)
        & (upos[None, :] >= tok_start[:, None])
    )
    coef_rows = token_coefficient[None, :, None]
    query_rows = queries[0].reshape(tok_rows, kv_heads, group_size, HEAD_SIZE)
    grad_rows = output_gradient[0].reshape(tok_rows, kv_heads, group_size, HEAD_SIZE)
    key_rows = all_keys.reshape(span, kv_heads, HEAD_SIZE)
    value_rows = all_values.reshape(span, kv_heads, HEAD_SIZE)
    scores = ATTN_SCALE * jnp.einsum(
        "tjgd,ljd->jgtl", query_rows, key_rows, preferred_element_type=jnp.float32
    )
    masked = jnp.where(allowed[None, None], scores, NEG_FILL)
    row_max = jnp.max(masked, -1, keepdims=True)
    weights_exp = jnp.where(allowed[None, None], jnp.exp(masked - row_max), 0.0)
    attn_probs = weights_exp / jnp.sum(weights_exp, -1, keepdims=True)
    prob_grad = coef_rows[None] * jnp.einsum(
        "tjgd,ljd->jgtl", grad_rows, value_rows, preferred_element_type=jnp.float32
    )
    row_delta = jnp.sum(attn_probs * prob_grad, -1, keepdims=True)
    score_grad = (ATTN_SCALE * attn_probs * (prob_grad - row_delta)).astype(jnp.bfloat16)
    query_grad = jnp.einsum(
        "jgtl,ljd->tjgd", score_grad, key_rows, preferred_element_type=jnp.float32
    ).astype(jnp.bfloat16).reshape(tok_rows, kv_heads * group_size * HEAD_SIZE)
    key_parts = jnp.einsum(
        "jgtl,tjgd->ljd", score_grad, query_rows, preferred_element_type=jnp.float32
    ).reshape(span, width_kv)
    weighted = (attn_probs * coef_rows[None]).astype(jnp.bfloat16)
    value_parts = jnp.einsum(
        "jgtl,tjgd->ljd", weighted, grad_rows, preferred_element_type=jnp.float32
    ).reshape(span, width_kv)
    key_total = key_parts[halo_blocks * tok_rows :]
    value_total = value_parts[halo_blocks * tok_rows :]
    if use_tree:
        slot_rows = lambda parts: [
            parts[k * tok_rows : (k + 1) * tok_rows].astype(jnp.bfloat16) for k in range(halo_blocks)
        ]
        key_total = key_total + tree_return(slot_rows(key_parts), levels)
        value_total = value_total + tree_return(slot_rows(value_parts), levels)
    else:
        for distance in range(1, halo_blocks + 1):
            block_start = (halo_blocks - distance) * tok_rows
            send_keys = key_parts[block_start : block_start + tok_rows].astype(jnp.bfloat16)
            send_values = value_parts[block_start : block_start + tok_rows].astype(jnp.bfloat16)
            back_keys, back_values = shifted((send_keys, send_values), "ctx", -distance)
            key_total = key_total + back_keys.astype(jnp.float32)
            value_total = value_total + back_values.astype(jnp.float32)
    key_grad = key_total.astype(jnp.bfloat16)
    value_gradient = value_total.astype(jnp.bfloat16)
    rank_middle = jnp.einsum(
        "sj,zj->sz", value_gradient, adapter_up, preferred_element_type=jnp.float32
    ).astype(jnp.bfloat16)
    if split_pair:
        projected = jnp.einsum(
            "tk,dk->td",
            lax.dynamic_slice_in_dim(value_gradient, mine_at, half_cols, 1),
            rows_half,
            preferred_element_type=jnp.float32,
        ) + jnp.einsum(
            "tk,dk->td",
            lax.dynamic_slice_in_dim(value_gradient, other_at, half_cols, 1),
            other_half,
            preferred_element_type=jnp.float32,
        )
    else:
        projected = jnp.einsum(
            "tk,dk->td", value_gradient, full_weight, preferred_element_type=jnp.float32
        )
    input_grad = (
        projected
        + ADAPTER_SCALE
        * jnp.einsum("pb,wb->pw", rank_middle, adapter_down, preferred_element_type=jnp.float32)
    ).astype(jnp.bfloat16)
    up_factor = ADAPTER_SCALE * jnp.einsum(
        "tr,tk->rk", rank_projection, value_gradient, preferred_element_type=jnp.float32
    )
    down_factor = ADAPTER_SCALE * jnp.einsum(
        "td,tr->dr", hidden_rows, rank_middle, preferred_element_type=jnp.float32
    )
    down_size = down_factor.size
    flat = jnp.concatenate([down_factor.reshape(-1), up_factor.reshape(-1)], 0)
    flat = butterfly_sum(flat.reshape(-1, HEAD_SIZE), ("pair", "ctx")).reshape(-1)
    down_gradient = flat[:down_size].reshape(down_factor.shape)
    up_gradient = flat[down_size:].reshape(up_factor.shape)
    return (input_grad[None], query_grad[None], key_grad[None], down_gradient, up_gradient)


def solution(mesh):
    return jax.shard_map(
        shards,
        mesh=mesh,
        in_specs=(
            P(("grp", "pair"), "ctx", None),
            P(("grp", "pair"), "ctx", None),
            P(("grp", "pair"), "ctx", None),
            P("ctx", None),
            P(),
            P(),
            P(("grp", "pair"), "ctx", None),
            P(("grp", "pair"), "ctx"),
            P(("grp", "pair"), "ctx"),
            P(("grp", "pair"), "ctx"),
        ),
        out_specs=(
            P(("grp", "pair"), "ctx", None),
            P(("grp", "pair"), "ctx", None),
            P(("grp", "pair"), "ctx", None),
            P("grp", None),
            P("grp", None),
        ),
        check_vma=False,
    )
```

```python
import jax
import jax.numpy as jnp
from jax import lax
from jax.sharding import PartitionSpec as P

HEAD_SIZE = 128
WINDOW = 1024
SEGS = 8


DPO_BETA = 0.1
LOSS_SCALE = 256.0
ADAPTER_SCALE = 2.0
ATTN_SCALE = 168.0 ** (-0.5)
NEG_FILL = -1e30


def from_partner(shard, axis, stride):
    return lax.ppermute(shard, axis, [(i, i ^ 1 << stride) for i in range(lax.axis_size(axis))])


def butterfly_sum(parts, axes):
    for axis in axes:
        size = lax.axis_size(axis)
        if size & (size - 1):
            parts = lax.psum(parts, axis)
            continue
        stride = 0
        while 1 << stride < size:
            got = from_partner(parts, axis, stride)
            parts = jax.tree.map(jnp.add, parts, got)
            stride += 1
    return parts


def tree_spread(block, levels):
    count = 2 * levels
    climbed = []
    held = block
    for step in range(1, levels):
        held = lax.ppermute(held, "ctx", [(c - 2, c) for c in range(2 * step, count)])
        climbed.append(held)
    crossed = [lax.ppermute(block, "ctx", [(c - 1, c) for c in range(1, count, 2)])]
    for step in range(1, levels):
        crossed.append(
            lax.ppermute(climbed[step - 1], "ctx", [(c ^ 1, c) for c in range(2 * step, count)])
        )
    return climbed + crossed


def tree_gather(block, ctx_index, levels):
    count = 2 * levels
    partner = jnp.bitwise_xor(ctx_index, 1)
    got = [block]
    owners = [ctx_index]
    valid = [ctx_index >= 0]
    up, down = block, block
    ups, downs = [], []
    for step in range(1, levels):
        up = lax.ppermute(up, "ctx", [(c - 2, c) for c in range(2 * step, count)])
        down = lax.ppermute(down, "ctx", [(c + 2, c) for c in range(0, count - 2 * step)])
        ups.append(up)
        downs.append(down)
        got += [up, down]
        owners += [ctx_index - 2 * step, ctx_index + 2 * step]
        valid += [ctx_index >= 2 * step, ctx_index < count - 2 * step]
    got.append(lax.ppermute(block, "ctx", [(c ^ 1, c) for c in range(count)]))
    owners.append(partner)
    valid.append(ctx_index >= 0)
    for step in range(1, levels):
        both = lax.ppermute(
            jnp.concatenate([ups[step - 1], downs[step - 1]], 0), "ctx", [(c ^ 1, c) for c in range(count)]
        )
        got += [both[: block.shape[0]], both[block.shape[0] :]]
        owners += [partner - 2 * step, partner + 2 * step]
        valid += [ctx_index >= 2 * step, ctx_index < count - 2 * step]
    rows = block.shape[0]
    whole = jnp.zeros(((count + 1) * rows,) + block.shape[1:], block.dtype)
    for piece, owner, ok in zip(got, owners, valid):
        place = jnp.where(ok, owner, count) * rows
        whole = lax.dynamic_update_slice_in_dim(whole, piece, place, 0)
    return whole[: count * rows]


def tree_slots(ctx_index, levels):
    partner = jnp.bitwise_xor(ctx_index, 1)
    owners, valid = [], []
    for step in range(1, levels):
        owners.append(ctx_index - 2 * step)
        valid.append(ctx_index >= 2 * step)
    owners.append(ctx_index - 1)
    valid.append(ctx_index % 2 == 1)
    for step in range(1, levels):
        owners.append(partner - 2 * step)
        valid.append(ctx_index >= 2 * step)
    return owners, valid


def tree_return(slot_parts, levels):
    count = 2 * levels
    climbed = slot_parts[: levels - 1]
    crossed = slot_parts[levels - 1 :]
    back = [lax.ppermute(crossed[0], "ctx", [(c, c - 1) for c in range(1, count, 2)])]
    for step in range(1, levels):
        back.append(
            lax.ppermute(crossed[step], "ctx", [(c, c ^ 1) for c in range(2 * step, count)])
        )
    total = back[0].astype(jnp.float32)
    carry = None
    for step in range(levels - 1, 0, -1):
        acc = climbed[step - 1].astype(jnp.float32) + back[step].astype(jnp.float32)
        if carry is not None:
            acc = acc + carry.astype(jnp.float32)
        carry = lax.ppermute(
            acc.astype(jnp.bfloat16), "ctx", [(c, c - 2) for c in range(2 * step, count)]
        )
    if carry is not None:
        total = total + carry.astype(jnp.float32)
    return total


def shifted(block, axis, distance):
    devices = range(lax.axis_size(axis))
    route = [(i - distance, i) for i in devices if i - distance in devices]
    return lax.ppermute(block, axis, route)


def shards(
    normed_input,
    queries,
    keys,
    value_projection,
    adapter_down,
    adapter_up,
    output_gradient,
    policy_logprob,
    reference_logprob,
    token_pair_index,
):
    tok_rows = normed_input.shape[1]
    width_kv = keys.shape[2]
    kv_heads = width_kv // HEAD_SIZE
    group_size = queries.shape[2] // width_kv
    hidden_rows = normed_input[0]
    own_keys = keys[0]
    pair_index = lax.axis_index("pair")
    ctx_index = lax.axis_index("ctx")
    half_cols = width_kv // 2
    own_half = lax.dynamic_slice_in_dim(value_projection, pair_index * half_cols, half_cols, 1)
    ctx_count = lax.axis_size("ctx")
    if ctx_count % 2 == 0 and 4 <= ctx_count <= 8:
        rows_half = tree_gather(own_half, ctx_index, ctx_count // 2)
    else:
        rows_half = lax.all_gather(own_half, "ctx", axis=0, tiled=True)
    if lax.axis_size("pair") == 2:
        other_half = from_partner(rows_half, "pair", 0)
        full_weight = jnp.zeros((rows_half.shape[0], width_kv), rows_half.dtype)
        full_weight = lax.dynamic_update_slice_in_dim(full_weight, rows_half, pair_index * half_cols, 1)
        full_weight = lax.dynamic_update_slice_in_dim(
            full_weight, other_half, (1 - pair_index) * half_cols, 1
        )
    else:
        full_weight = lax.all_gather(rows_half, "pair", axis=1, tiled=True)
    rank_projection = jnp.dot(hidden_rows, adapter_down, preferred_element_type=jnp.float32).astype(
        jnp.bfloat16
    )
    values = (
        jnp.dot(hidden_rows, full_weight, preferred_element_type=jnp.float32)
        + ADAPTER_SCALE * jnp.dot(rank_projection, adapter_up, preferred_element_type=jnp.float32)
    ).astype(jnp.bfloat16)
    segment_labels = token_pair_index[0]
    seg_table = (segment_labels[:, None] == jnp.arange(SEGS, dtype=jnp.int32)[None, :]).astype(
        jnp.float32
    )
    log_gap = policy_logprob[0] - reference_logprob[0]
    part_diff = jnp.sum(seg_table * log_gap[:, None], 0)
    part_count = jnp.sum(seg_table, 0)
    both_sums = butterfly_sum(jnp.concatenate([part_diff, part_count], 0), ("ctx",))
    own_diff, counts = both_sums[:SEGS], both_sums[SEGS:]
    other_diff = from_partner(own_diff, "pair", 0)
    direction = 1.0 - 2.0 * pair_index.astype(jnp.float32)
    margin = DPO_BETA * (direction * (own_diff - other_diff))
    coef = -direction * DPO_BETA * LOSS_SCALE * jax.nn.sigmoid(-margin)
    starts = jnp.cumsum(counts) - counts
    tok_start = jnp.sum(seg_table * starts[None, :], 1).astype(jnp.int32)
    token_coefficient = jnp.sum(seg_table * coef[None, :], 1)
    ctx_size = lax.axis_size("ctx")
    halo_blocks = min(WINDOW // tok_rows, ctx_size - 1)
    use_tree = halo_blocks == ctx_size - 1 and ctx_size % 2 == 0 and ctx_size >= 4
    levels = ctx_size // 2
    row_iota = jnp.arange(tok_rows, dtype=jnp.int32)
    if use_tree:
        key_blocks = tree_spread(own_keys, levels)
        value_blocks = tree_spread(values, levels)
        owners, valid = tree_slots(ctx_index, levels)
        far = jnp.int32(1 << 30)
        upos = jnp.concatenate(
            [jnp.where(ok, owner * tok_rows + row_iota, far) for owner, ok in zip(owners, valid)]
            + [ctx_index * tok_rows + row_iota],
            0,
        )
    else:
        key_blocks = []
        value_blocks = []
        for distance in range(halo_blocks, 0, -1):
            key_blocks.append(shifted(own_keys, "ctx", distance))
            value_blocks.append(shifted(values, "ctx", distance))
    all_keys = jnp.concatenate(key_blocks + [own_keys], 0)
    all_keys, own_values = lax.optimization_barrier((all_keys, values))
    all_values = jnp.concatenate(value_blocks + [own_values], 0)
    span = all_keys.shape[0]
    tpos = ctx_index * tok_rows + row_iota
    if not use_tree:
        upos = ctx_index * tok_rows - halo_blocks * tok_rows + jnp.arange(span, dtype=jnp.int32)
    allowed = (
        (upos[None, :] <= tpos[:, None])
        & (upos[None, :] > tpos[:, None] - WINDOW)
        & (upos[None, :] >= tok_start[:, None])
    )
    coef_rows = token_coefficient[None, :, None]
    query_rows = queries[0].reshape(tok_rows, kv_heads, group_size, HEAD_SIZE)
    grad_rows = output_gradient[0].reshape(tok_rows, kv_heads, group_size, HEAD_SIZE)
    key_rows = all_keys.reshape(span, kv_heads, HEAD_SIZE)
    value_rows = all_values.reshape(span, kv_heads, HEAD_SIZE)
    scores = ATTN_SCALE * jnp.einsum(
        "tjgd,ljd->jgtl", query_rows, key_rows, preferred_element_type=jnp.float32
    )
    masked = jnp.where(allowed[None, None], scores, NEG_FILL)
    row_max = jnp.max(masked, -1, keepdims=True)
    weights_exp = jnp.where(allowed[None, None], jnp.exp(masked - row_max), 0.0)
    attn_probs = weights_exp / jnp.sum(weights_exp, -1, keepdims=True)
    prob_grad = coef_rows[None] * jnp.einsum(
        "tjgd,ljd->jgtl", grad_rows, value_rows, preferred_element_type=jnp.float32
    )
    row_delta = jnp.sum(attn_probs * prob_grad, -1, keepdims=True)
    score_grad = (ATTN_SCALE * attn_probs * (prob_grad - row_delta)).astype(jnp.bfloat16)
    query_grad = jnp.einsum(
        "jgtl,ljd->tjgd", score_grad, key_rows, preferred_element_type=jnp.float32
    ).astype(jnp.bfloat16).reshape(tok_rows, kv_heads * group_size * HEAD_SIZE)
    key_parts = jnp.einsum(
        "jgtl,tjgd->ljd", score_grad, query_rows, preferred_element_type=jnp.float32
    ).reshape(span, width_kv)
    weighted = (attn_probs * coef_rows[None]).astype(jnp.bfloat16)
    value_parts = jnp.einsum(
        "jgtl,tjgd->ljd", weighted, grad_rows, preferred_element_type=jnp.float32
    ).reshape(span, width_kv)
    key_total = key_parts[halo_blocks * tok_rows :]
    value_total = value_parts[halo_blocks * tok_rows :]
    if use_tree:
        slot_rows = lambda parts: [
            parts[k * tok_rows : (k + 1) * tok_rows].astype(jnp.bfloat16) for k in range(halo_blocks)
        ]
        key_total = key_total + tree_return(slot_rows(key_parts), levels)
        value_total = value_total + tree_return(slot_rows(value_parts), levels)
    else:
        for distance in range(1, halo_blocks + 1):
            block_start = (halo_blocks - distance) * tok_rows
            send_keys = key_parts[block_start : block_start + tok_rows].astype(jnp.bfloat16)
            send_values = value_parts[block_start : block_start + tok_rows].astype(jnp.bfloat16)
            back_keys, back_values = shifted((send_keys, send_values), "ctx", -distance)
            key_total = key_total + back_keys.astype(jnp.float32)
            value_total = value_total + back_values.astype(jnp.float32)
    key_grad = key_total.astype(jnp.bfloat16)
    value_gradient = value_total.astype(jnp.bfloat16)
    rank_middle = jnp.einsum(
        "sj,zj->sz", value_gradient, adapter_up, preferred_element_type=jnp.float32
    ).astype(jnp.bfloat16)
    input_grad = (
        jnp.einsum("tk,dk->td", value_gradient, full_weight, preferred_element_type=jnp.float32)
        + ADAPTER_SCALE
        * jnp.einsum("pb,wb->pw", rank_middle, adapter_down, preferred_element_type=jnp.float32)
    ).astype(jnp.bfloat16)
    up_factor = ADAPTER_SCALE * jnp.einsum(
        "tr,tk->rk", rank_projection, value_gradient, preferred_element_type=jnp.float32
    )
    down_factor = ADAPTER_SCALE * jnp.einsum(
        "td,tr->dr", hidden_rows, rank_middle, preferred_element_type=jnp.float32
    )
    down_size = down_factor.size
    flat = jnp.concatenate([down_factor.reshape(-1), up_factor.reshape(-1)], 0)
    flat = butterfly_sum(flat.reshape(-1, HEAD_SIZE), ("pair", "ctx")).reshape(-1)
    down_gradient = flat[:down_size].reshape(down_factor.shape)
    up_gradient = flat[down_size:].reshape(up_factor.shape)
    return (input_grad[None], query_grad[None], key_grad[None], down_gradient, up_gradient)


def solution(mesh):
    return jax.shard_map(
        shards,
        mesh=mesh,
        in_specs=(
            P(("grp", "pair"), "ctx", None),
            P(("grp", "pair"), "ctx", None),
            P(("grp", "pair"), "ctx", None),
            P("ctx", None),
            P(),
            P(),
            P(("grp", "pair"), "ctx", None),
            P(("grp", "pair"), "ctx"),
            P(("grp", "pair"), "ctx"),
            P(("grp", "pair"), "ctx"),
        ),
        out_specs=(
            P(("grp", "pair"), "ctx", None),
            P(("grp", "pair"), "ctx", None),
            P(("grp", "pair"), "ctx", None),
            P("grp", None),
            P("grp", None),
        ),
        check_vma=False,
    )
```

```python
import jax
import jax.numpy as jnp
from jax import lax
from jax.sharding import PartitionSpec as P

HEAD_SIZE = 128
WINDOW = 1024
SEGS = 8


DPO_BETA = 0.1
LOSS_SCALE = 256.0
ADAPTER_SCALE = 2.0
ATTN_SCALE = 168.0 ** (-0.5)
NEG_FILL = -1e30


def from_partner(shard, axis, stride):
    return lax.ppermute(shard, axis, [(i, i ^ 1 << stride) for i in range(lax.axis_size(axis))])


def butterfly_sum(parts, axes):
    for axis in axes:
        size = lax.axis_size(axis)
        if size & (size - 1):
            parts = lax.psum(parts, axis)
            continue
        stride = 0
        while 1 << stride < size:
            got = from_partner(parts, axis, stride)
            parts = jax.tree.map(jnp.add, parts, got)
            stride += 1
    return parts


def tree_spread(block, levels):
    count = 2 * levels
    climbed = []
    held = block
    for step in range(1, levels):
        held = lax.ppermute(held, "ctx", [(c - 2, c) for c in range(2 * step, count)])
        climbed.append(held)
    crossed = [lax.ppermute(block, "ctx", [(c - 1, c) for c in range(1, count, 2)])]
    for step in range(1, levels):
        crossed.append(
            lax.ppermute(climbed[step - 1], "ctx", [(c ^ 1, c) for c in range(2 * step, count)])
        )
    return climbed + crossed


def tree_gather(block, ctx_index, levels):
    count = 2 * levels
    partner = jnp.bitwise_xor(ctx_index, 1)
    got = [block]
    owners = [ctx_index]
    valid = [ctx_index >= 0]
    up, down = block, block
    ups, downs = [], []
    for step in range(1, levels):
        up = lax.ppermute(up, "ctx", [(c - 2, c) for c in range(2 * step, count)])
        down = lax.ppermute(down, "ctx", [(c + 2, c) for c in range(0, count - 2 * step)])
        ups.append(up)
        downs.append(down)
        got += [up, down]
        owners += [ctx_index - 2 * step, ctx_index + 2 * step]
        valid += [ctx_index >= 2 * step, ctx_index < count - 2 * step]
    got.append(lax.ppermute(block, "ctx", [(c ^ 1, c) for c in range(count)]))
    owners.append(partner)
    valid.append(ctx_index >= 0)
    for step in range(1, levels):
        got.append(lax.ppermute(ups[step - 1], "ctx", [(c ^ 1, c) for c in range(2 * step, count)]))
        got.append(
            lax.ppermute(downs[step - 1], "ctx", [(c ^ 1, c) for c in range(0, count - 2 * step)])
        )
        owners += [partner - 2 * step, partner + 2 * step]
        valid += [ctx_index >= 2 * step, ctx_index < count - 2 * step]
    rows = block.shape[0]
    whole = jnp.zeros(((count + 1) * rows,) + block.shape[1:], block.dtype)
    for piece, owner, ok in zip(got, owners, valid):
        place = jnp.where(ok, owner, count) * rows
        whole = lax.dynamic_update_slice_in_dim(whole, piece, place, 0)
    return whole[: count * rows]


def tree_slots(ctx_index, levels):
    partner = jnp.bitwise_xor(ctx_index, 1)
    owners, valid = [], []
    for step in range(1, levels):
        owners.append(ctx_index - 2 * step)
        valid.append(ctx_index >= 2 * step)
    owners.append(ctx_index - 1)
    valid.append(ctx_index % 2 == 1)
    for step in range(1, levels):
        owners.append(partner - 2 * step)
        valid.append(ctx_index >= 2 * step)
    return owners, valid


def tree_return(slot_parts, levels):
    count = 2 * levels
    climbed = slot_parts[: levels - 1]
    crossed = slot_parts[levels - 1 :]
    back = [lax.ppermute(crossed[0], "ctx", [(c, c - 1) for c in range(1, count, 2)])]
    for step in range(1, levels):
        back.append(
            lax.ppermute(crossed[step], "ctx", [(c, c ^ 1) for c in range(2 * step, count)])
        )
    total = back[0].astype(jnp.float32)
    carry = None
    for step in range(levels - 1, 0, -1):
        acc = climbed[step - 1].astype(jnp.float32) + back[step].astype(jnp.float32)
        if carry is not None:
            acc = acc + carry.astype(jnp.float32)
        carry = lax.ppermute(
            acc.astype(jnp.bfloat16), "ctx", [(c, c - 2) for c in range(2 * step, count)]
        )
    if carry is not None:
        total = total + carry.astype(jnp.float32)
    return total


def shifted(block, axis, distance):
    devices = range(lax.axis_size(axis))
    route = [(i - distance, i) for i in devices if i - distance in devices]
    return lax.ppermute(block, axis, route)


def shards(
    normed_input,
    queries,
    keys,
    value_projection,
    adapter_down,
    adapter_up,
    output_gradient,
    policy_logprob,
    reference_logprob,
    token_pair_index,
):
    tok_rows = normed_input.shape[1]
    width_kv = keys.shape[2]
    kv_heads = width_kv // HEAD_SIZE
    group_size = queries.shape[2] // width_kv
    hidden_rows = normed_input[0]
    own_keys = keys[0]
    pair_index = lax.axis_index("pair")
    ctx_index = lax.axis_index("ctx")
    half_cols = width_kv // 2
    own_half = lax.dynamic_slice_in_dim(value_projection, pair_index * half_cols, half_cols, 1)
    ctx_count = lax.axis_size("ctx")
    if ctx_count % 2 == 0 and 4 <= ctx_count <= 8:
        rows_half = tree_gather(own_half, ctx_index, ctx_count // 2)
    else:
        rows_half = lax.all_gather(own_half, "ctx", axis=0, tiled=True)
    if lax.axis_size("pair") == 2:
        other_half = from_partner(rows_half, "pair", 0)
        full_weight = jnp.zeros((rows_half.shape[0], width_kv), rows_half.dtype)
        full_weight = lax.dynamic_update_slice_in_dim(full_weight, rows_half, pair_index * half_cols, 1)
        full_weight = lax.dynamic_update_slice_in_dim(
            full_weight, other_half, (1 - pair_index) * half_cols, 1
        )
    else:
        full_weight = lax.all_gather(rows_half, "pair", axis=1, tiled=True)
    rank_projection = jnp.dot(hidden_rows, adapter_down, preferred_element_type=jnp.float32).astype(
        jnp.bfloat16
    )
    values = (
        jnp.dot(hidden_rows, full_weight, preferred_element_type=jnp.float32)
        + ADAPTER_SCALE * jnp.dot(rank_projection, adapter_up, preferred_element_type=jnp.float32)
    ).astype(jnp.bfloat16)
    segment_labels = token_pair_index[0]
    seg_table = (segment_labels[:, None] == jnp.arange(SEGS, dtype=jnp.int32)[None, :]).astype(
        jnp.float32
    )
    log_gap = policy_logprob[0] - reference_logprob[0]
    part_diff = jnp.sum(seg_table * log_gap[:, None], 0)
    part_count = jnp.sum(seg_table, 0)
    both_sums = butterfly_sum(jnp.concatenate([part_diff, part_count], 0), ("ctx",))
    own_diff, counts = both_sums[:SEGS], both_sums[SEGS:]
    other_diff = from_partner(own_diff, "pair", 0)
    direction = 1.0 - 2.0 * pair_index.astype(jnp.float32)
    margin = DPO_BETA * (direction * (own_diff - other_diff))
    coef = -direction * DPO_BETA * LOSS_SCALE * jax.nn.sigmoid(-margin)
    starts = jnp.cumsum(counts) - counts
    tok_start = jnp.sum(seg_table * starts[None, :], 1).astype(jnp.int32)
    token_coefficient = jnp.sum(seg_table * coef[None, :], 1)
    ctx_size = lax.axis_size("ctx")
    halo_blocks = min(WINDOW // tok_rows, ctx_size - 1)
    use_tree = halo_blocks == ctx_size - 1 and ctx_size % 2 == 0 and ctx_size >= 4
    levels = ctx_size // 2
    row_iota = jnp.arange(tok_rows, dtype=jnp.int32)
    if use_tree:
        key_blocks = tree_spread(own_keys, levels)
        value_blocks = tree_spread(values, levels)
        owners, valid = tree_slots(ctx_index, levels)
        far = jnp.int32(1 << 30)
        upos = jnp.concatenate(
            [jnp.where(ok, owner * tok_rows + row_iota, far) for owner, ok in zip(owners, valid)]
            + [ctx_index * tok_rows + row_iota],
            0,
        )
    else:
        key_blocks = []
        value_blocks = []
        for distance in range(halo_blocks, 0, -1):
            key_blocks.append(shifted(own_keys, "ctx", distance))
            value_blocks.append(shifted(values, "ctx", distance))
    all_keys = jnp.concatenate(key_blocks + [own_keys], 0)
    all_keys, own_values = lax.optimization_barrier((all_keys, values))
    all_values = jnp.concatenate(value_blocks + [own_values], 0)
    span = all_keys.shape[0]
    tpos = ctx_index * tok_rows + row_iota
    if not use_tree:
        upos = ctx_index * tok_rows - halo_blocks * tok_rows + jnp.arange(span, dtype=jnp.int32)
    allowed = (
        (upos[None, :] <= tpos[:, None])
        & (upos[None, :] > tpos[:, None] - WINDOW)
        & (upos[None, :] >= tok_start[:, None])
    )
    coef_rows = token_coefficient[None, :, None]
    query_rows = queries[0].reshape(tok_rows, kv_heads, group_size, HEAD_SIZE)
    grad_rows = output_gradient[0].reshape(tok_rows, kv_heads, group_size, HEAD_SIZE)
    key_rows = all_keys.reshape(span, kv_heads, HEAD_SIZE)
    value_rows = all_values.reshape(span, kv_heads, HEAD_SIZE)
    scores = ATTN_SCALE * jnp.einsum(
        "tjgd,ljd->jgtl", query_rows, key_rows, preferred_element_type=jnp.float32
    )
    masked = jnp.where(allowed[None, None], scores, NEG_FILL)
    row_max = jnp.max(masked, -1, keepdims=True)
    weights_exp = jnp.where(allowed[None, None], jnp.exp(masked - row_max), 0.0)
    attn_probs = weights_exp / jnp.sum(weights_exp, -1, keepdims=True)
    prob_grad = coef_rows[None] * jnp.einsum(
        "tjgd,ljd->jgtl", grad_rows, value_rows, preferred_element_type=jnp.float32
    )
    row_delta = jnp.sum(attn_probs * prob_grad, -1, keepdims=True)
    score_grad = (ATTN_SCALE * attn_probs * (prob_grad - row_delta)).astype(jnp.bfloat16)
    query_grad = jnp.einsum(
        "jgtl,ljd->tjgd", score_grad, key_rows, preferred_element_type=jnp.float32
    ).astype(jnp.bfloat16).reshape(tok_rows, kv_heads * group_size * HEAD_SIZE)
    key_parts = jnp.einsum(
        "jgtl,tjgd->ljd", score_grad, query_rows, preferred_element_type=jnp.float32
    ).reshape(span, width_kv)
    weighted = (attn_probs * coef_rows[None]).astype(jnp.bfloat16)
    value_parts = jnp.einsum(
        "jgtl,tjgd->ljd", weighted, grad_rows, preferred_element_type=jnp.float32
    ).reshape(span, width_kv)
    key_total = key_parts[halo_blocks * tok_rows :]
    value_total = value_parts[halo_blocks * tok_rows :]
    if use_tree:
        slot_rows = lambda parts: [
            parts[k * tok_rows : (k + 1) * tok_rows].astype(jnp.bfloat16) for k in range(halo_blocks)
        ]
        key_total = key_total + tree_return(slot_rows(key_parts), levels)
        value_total = value_total + tree_return(slot_rows(value_parts), levels)
    else:
        for distance in range(1, halo_blocks + 1):
            block_start = (halo_blocks - distance) * tok_rows
            send_keys = key_parts[block_start : block_start + tok_rows].astype(jnp.bfloat16)
            send_values = value_parts[block_start : block_start + tok_rows].astype(jnp.bfloat16)
            back_keys, back_values = shifted((send_keys, send_values), "ctx", -distance)
            key_total = key_total + back_keys.astype(jnp.float32)
            value_total = value_total + back_values.astype(jnp.float32)
    key_grad = key_total.astype(jnp.bfloat16)
    value_gradient = value_total.astype(jnp.bfloat16)
    rank_middle = jnp.einsum(
        "sj,zj->sz", value_gradient, adapter_up, preferred_element_type=jnp.float32
    ).astype(jnp.bfloat16)
    input_grad = (
        jnp.einsum("tk,dk->td", value_gradient, full_weight, preferred_element_type=jnp.float32)
        + ADAPTER_SCALE
        * jnp.einsum("pb,wb->pw", rank_middle, adapter_down, preferred_element_type=jnp.float32)
    ).astype(jnp.bfloat16)
    up_factor = ADAPTER_SCALE * jnp.einsum(
        "tr,tk->rk", rank_projection, value_gradient, preferred_element_type=jnp.float32
    )
    down_factor = ADAPTER_SCALE * jnp.einsum(
        "td,tr->dr", hidden_rows, rank_middle, preferred_element_type=jnp.float32
    )
    down_size = down_factor.size
    flat = jnp.concatenate([down_factor.reshape(-1), up_factor.reshape(-1)], 0)
    flat = butterfly_sum(flat.reshape(-1, HEAD_SIZE), ("ctx", "pair")).reshape(-1)
    down_gradient = flat[:down_size].reshape(down_factor.shape)
    up_gradient = flat[down_size:].reshape(up_factor.shape)
    return (input_grad[None], query_grad[None], key_grad[None], down_gradient, up_gradient)


def solution(mesh):
    return jax.shard_map(
        shards,
        mesh=mesh,
        in_specs=(
            P(("grp", "pair"), "ctx", None),
            P(("grp", "pair"), "ctx", None),
            P(("grp", "pair"), "ctx", None),
            P("ctx", None),
            P(),
            P(),
            P(("grp", "pair"), "ctx", None),
            P(("grp", "pair"), "ctx"),
            P(("grp", "pair"), "ctx"),
            P(("grp", "pair"), "ctx"),
        ),
        out_specs=(
            P(("grp", "pair"), "ctx", None),
            P(("grp", "pair"), "ctx", None),
            P(("grp", "pair"), "ctx", None),
            P("grp", None),
            P("grp", None),
        ),
        check_vma=False,
    )
```

```python
import jax
import jax.numpy as jnp
from jax import lax
from jax.sharding import PartitionSpec as P

HEAD_SIZE = 128
WINDOW = 1024
SEGS = 8


DPO_BETA = 0.1
LOSS_SCALE = 256.0
ADAPTER_SCALE = 2.0
ATTN_SCALE = 168.0 ** (-0.5)
NEG_FILL = -1e30


def from_partner(shard, axis, stride):
    return lax.ppermute(shard, axis, [(i, i ^ 1 << stride) for i in range(lax.axis_size(axis))])


def butterfly_sum(parts, axes, far_first=False):
    for axis in axes:
        size = lax.axis_size(axis)
        if size & (size - 1):
            parts = lax.psum(parts, axis)
            continue
        strides = list(range(size.bit_length() - 1))
        for stride in reversed(strides) if far_first else strides:
            got = from_partner(parts, axis, stride)
            parts = jax.tree.map(jnp.add, parts, got)
    return parts


def tree_spread(block, levels):
    count = 2 * levels
    climbed = []
    held = block
    for step in range(1, levels):
        held = lax.ppermute(held, "ctx", [(c - 2, c) for c in range(2 * step, count)])
        climbed.append(held)
    crossed = [lax.ppermute(block, "ctx", [(c - 1, c) for c in range(1, count, 2)])]
    for step in range(1, levels):
        crossed.append(
            lax.ppermute(climbed[step - 1], "ctx", [(c ^ 1, c) for c in range(2 * step, count)])
        )
    return climbed + crossed


def tree_gather(block, ctx_index, levels):
    count = 2 * levels
    partner = jnp.bitwise_xor(ctx_index, 1)
    got = [block]
    owners = [ctx_index]
    valid = [ctx_index >= 0]
    up, down = block, block
    ups, downs = [], []
    for step in range(1, levels):
        up = lax.ppermute(up, "ctx", [(c - 2, c) for c in range(2 * step, count)])
        down = lax.ppermute(down, "ctx", [(c + 2, c) for c in range(0, count - 2 * step)])
        ups.append(up)
        downs.append(down)
        got += [up, down]
        owners += [ctx_index - 2 * step, ctx_index + 2 * step]
        valid += [ctx_index >= 2 * step, ctx_index < count - 2 * step]
    got.append(lax.ppermute(block, "ctx", [(c ^ 1, c) for c in range(count)]))
    owners.append(partner)
    valid.append(ctx_index >= 0)
    for step in range(1, levels):
        got.append(lax.ppermute(ups[step - 1], "ctx", [(c ^ 1, c) for c in range(2 * step, count)]))
        got.append(
            lax.ppermute(downs[step - 1], "ctx", [(c ^ 1, c) for c in range(0, count - 2 * step)])
        )
        owners += [partner - 2 * step, partner + 2 * step]
        valid += [ctx_index >= 2 * step, ctx_index < count - 2 * step]
    rows = block.shape[0]
    whole = jnp.zeros(((count + 1) * rows,) + block.shape[1:], block.dtype)
    for piece, owner, ok in zip(got, owners, valid):
        place = jnp.where(ok, owner, count) * rows
        whole = lax.dynamic_update_slice_in_dim(whole, piece, place, 0)
    return whole[: count * rows]


def tree_slots(ctx_index, levels):
    partner = jnp.bitwise_xor(ctx_index, 1)
    owners, valid = [], []
    for step in range(1, levels):
        owners.append(ctx_index - 2 * step)
        valid.append(ctx_index >= 2 * step)
    owners.append(ctx_index - 1)
    valid.append(ctx_index % 2 == 1)
    for step in range(1, levels):
        owners.append(partner - 2 * step)
        valid.append(ctx_index >= 2 * step)
    return owners, valid


def tree_return(slot_parts, levels):
    count = 2 * levels
    climbed = slot_parts[: levels - 1]
    crossed = slot_parts[levels - 1 :]
    back = [lax.ppermute(crossed[0], "ctx", [(c, c - 1) for c in range(1, count, 2)])]
    for step in range(1, levels):
        back.append(
            lax.ppermute(crossed[step], "ctx", [(c, c ^ 1) for c in range(2 * step, count)])
        )
    total = back[0].astype(jnp.float32)
    carry = None
    for step in range(levels - 1, 0, -1):
        acc = climbed[step - 1].astype(jnp.float32) + back[step].astype(jnp.float32)
        if carry is not None:
            acc = acc + carry.astype(jnp.float32)
        carry = lax.ppermute(
            acc.astype(jnp.bfloat16), "ctx", [(c, c - 2) for c in range(2 * step, count)]
        )
    if carry is not None:
        total = total + carry.astype(jnp.float32)
    return total


def shifted(block, axis, distance):
    devices = range(lax.axis_size(axis))
    route = [(i - distance, i) for i in devices if i - distance in devices]
    return lax.ppermute(block, axis, route)


def shards(
    normed_input,
    queries,
    keys,
    value_projection,
    adapter_down,
    adapter_up,
    output_gradient,
    policy_logprob,
    reference_logprob,
    token_pair_index,
):
    tok_rows = normed_input.shape[1]
    width_kv = keys.shape[2]
    kv_heads = width_kv // HEAD_SIZE
    group_size = queries.shape[2] // width_kv
    hidden_rows = normed_input[0]
    own_keys = keys[0]
    pair_index = lax.axis_index("pair")
    ctx_index = lax.axis_index("ctx")
    half_cols = width_kv // 2
    own_half = lax.dynamic_slice_in_dim(value_projection, pair_index * half_cols, half_cols, 1)
    ctx_count = lax.axis_size("ctx")
    if ctx_count % 2 == 0 and 4 <= ctx_count <= 8:
        rows_half = tree_gather(own_half, ctx_index, ctx_count // 2)
    else:
        rows_half = lax.all_gather(own_half, "ctx", axis=0, tiled=True)
    if lax.axis_size("pair") == 2:
        other_half = from_partner(rows_half, "pair", 0)
        full_weight = jnp.zeros((rows_half.shape[0], width_kv), rows_half.dtype)
        full_weight = lax.dynamic_update_slice_in_dim(full_weight, rows_half, pair_index * half_cols, 1)
        full_weight = lax.dynamic_update_slice_in_dim(
            full_weight, other_half, (1 - pair_index) * half_cols, 1
        )
    else:
        full_weight = lax.all_gather(rows_half, "pair", axis=1, tiled=True)
    rank_projection = jnp.dot(hidden_rows, adapter_down, preferred_element_type=jnp.float32).astype(
        jnp.bfloat16
    )
    values = (
        jnp.dot(hidden_rows, full_weight, preferred_element_type=jnp.float32)
        + ADAPTER_SCALE * jnp.dot(rank_projection, adapter_up, preferred_element_type=jnp.float32)
    ).astype(jnp.bfloat16)
    segment_labels = token_pair_index[0]
    seg_table = (segment_labels[:, None] == jnp.arange(SEGS, dtype=jnp.int32)[None, :]).astype(
        jnp.float32
    )
    log_gap = policy_logprob[0] - reference_logprob[0]
    part_diff = jnp.sum(seg_table * log_gap[:, None], 0)
    part_count = jnp.sum(seg_table, 0)
    both_sums = butterfly_sum(jnp.concatenate([part_diff, part_count], 0), ("ctx",))
    own_diff, counts = both_sums[:SEGS], both_sums[SEGS:]
    other_diff = from_partner(own_diff, "pair", 0)
    direction = 1.0 - 2.0 * pair_index.astype(jnp.float32)
    margin = DPO_BETA * (direction * (own_diff - other_diff))
    coef = -direction * DPO_BETA * LOSS_SCALE * jax.nn.sigmoid(-margin)
    starts = jnp.cumsum(counts) - counts
    tok_start = jnp.sum(seg_table * starts[None, :], 1).astype(jnp.int32)
    token_coefficient = jnp.sum(seg_table * coef[None, :], 1)
    ctx_size = lax.axis_size("ctx")
    halo_blocks = min(WINDOW // tok_rows, ctx_size - 1)
    use_tree = halo_blocks == ctx_size - 1 and ctx_size % 2 == 0 and ctx_size >= 4
    levels = ctx_size // 2
    row_iota = jnp.arange(tok_rows, dtype=jnp.int32)
    if use_tree:
        key_blocks = tree_spread(own_keys, levels)
        value_blocks = tree_spread(values, levels)
        owners, valid = tree_slots(ctx_index, levels)
        far = jnp.int32(1 << 30)
        upos = jnp.concatenate(
            [jnp.where(ok, owner * tok_rows + row_iota, far) for owner, ok in zip(owners, valid)]
            + [ctx_index * tok_rows + row_iota],
            0,
        )
    else:
        key_blocks = []
        value_blocks = []
        for distance in range(halo_blocks, 0, -1):
            key_blocks.append(shifted(own_keys, "ctx", distance))
            value_blocks.append(shifted(values, "ctx", distance))
    all_keys = jnp.concatenate(key_blocks + [own_keys], 0)
    all_keys, own_values = lax.optimization_barrier((all_keys, values))
    all_values = jnp.concatenate(value_blocks + [own_values], 0)
    span = all_keys.shape[0]
    tpos = ctx_index * tok_rows + row_iota
    if not use_tree:
        upos = ctx_index * tok_rows - halo_blocks * tok_rows + jnp.arange(span, dtype=jnp.int32)
    allowed = (
        (upos[None, :] <= tpos[:, None])
        & (upos[None, :] > tpos[:, None] - WINDOW)
        & (upos[None, :] >= tok_start[:, None])
    )
    coef_rows = token_coefficient[None, :, None]
    query_rows = queries[0].reshape(tok_rows, kv_heads, group_size, HEAD_SIZE)
    grad_rows = output_gradient[0].reshape(tok_rows, kv_heads, group_size, HEAD_SIZE)
    key_rows = all_keys.reshape(span, kv_heads, HEAD_SIZE)
    value_rows = all_values.reshape(span, kv_heads, HEAD_SIZE)
    scores = ATTN_SCALE * jnp.einsum(
        "tjgd,ljd->jgtl", query_rows, key_rows, preferred_element_type=jnp.float32
    )
    masked = jnp.where(allowed[None, None], scores, NEG_FILL)
    row_max = jnp.max(masked, -1, keepdims=True)
    weights_exp = jnp.where(allowed[None, None], jnp.exp(masked - row_max), 0.0)
    attn_probs = weights_exp / jnp.sum(weights_exp, -1, keepdims=True)
    prob_grad = coef_rows[None] * jnp.einsum(
        "tjgd,ljd->jgtl", grad_rows, value_rows, preferred_element_type=jnp.float32
    )
    row_delta = jnp.sum(attn_probs * prob_grad, -1, keepdims=True)
    score_grad = (ATTN_SCALE * attn_probs * (prob_grad - row_delta)).astype(jnp.bfloat16)
    query_grad = jnp.einsum(
        "jgtl,ljd->tjgd", score_grad, key_rows, preferred_element_type=jnp.float32
    ).astype(jnp.bfloat16).reshape(tok_rows, kv_heads * group_size * HEAD_SIZE)
    key_parts = jnp.einsum(
        "jgtl,tjgd->ljd", score_grad, query_rows, preferred_element_type=jnp.float32
    ).reshape(span, width_kv)
    weighted = (attn_probs * coef_rows[None]).astype(jnp.bfloat16)
    value_parts = jnp.einsum(
        "jgtl,tjgd->ljd", weighted, grad_rows, preferred_element_type=jnp.float32
    ).reshape(span, width_kv)
    key_total = key_parts[halo_blocks * tok_rows :]
    value_total = value_parts[halo_blocks * tok_rows :]
    if use_tree:
        slot_rows = lambda parts: [
            parts[k * tok_rows : (k + 1) * tok_rows].astype(jnp.bfloat16) for k in range(halo_blocks)
        ]
        key_total = key_total + tree_return(slot_rows(key_parts), levels)
        value_total = value_total + tree_return(slot_rows(value_parts), levels)
    else:
        for distance in range(1, halo_blocks + 1):
            block_start = (halo_blocks - distance) * tok_rows
            send_keys = key_parts[block_start : block_start + tok_rows].astype(jnp.bfloat16)
            send_values = value_parts[block_start : block_start + tok_rows].astype(jnp.bfloat16)
            back_keys, back_values = shifted((send_keys, send_values), "ctx", -distance)
            key_total = key_total + back_keys.astype(jnp.float32)
            value_total = value_total + back_values.astype(jnp.float32)
    key_grad = key_total.astype(jnp.bfloat16)
    value_gradient = value_total.astype(jnp.bfloat16)
    rank_middle = jnp.einsum(
        "sj,zj->sz", value_gradient, adapter_up, preferred_element_type=jnp.float32
    ).astype(jnp.bfloat16)
    input_grad = (
        jnp.einsum("tk,dk->td", value_gradient, full_weight, preferred_element_type=jnp.float32)
        + ADAPTER_SCALE
        * jnp.einsum("pb,wb->pw", rank_middle, adapter_down, preferred_element_type=jnp.float32)
    ).astype(jnp.bfloat16)
    up_factor = ADAPTER_SCALE * jnp.einsum(
        "tr,tk->rk", rank_projection, value_gradient, preferred_element_type=jnp.float32
    )
    down_factor = ADAPTER_SCALE * jnp.einsum(
        "td,tr->dr", hidden_rows, rank_middle, preferred_element_type=jnp.float32
    )
    down_size = down_factor.size
    flat = jnp.concatenate([down_factor.reshape(-1), up_factor.reshape(-1)], 0)
    flat = butterfly_sum(flat.reshape(-1, HEAD_SIZE), ("ctx", "pair"), far_first=True).reshape(-1)
    down_gradient = flat[:down_size].reshape(down_factor.shape)
    up_gradient = flat[down_size:].reshape(up_factor.shape)
    return (input_grad[None], query_grad[None], key_grad[None], down_gradient, up_gradient)


def solution(mesh):
    return jax.shard_map(
        shards,
        mesh=mesh,
        in_specs=(
            P(("grp", "pair"), "ctx", None),
            P(("grp", "pair"), "ctx", None),
            P(("grp", "pair"), "ctx", None),
            P("ctx", None),
            P(),
            P(),
            P(("grp", "pair"), "ctx", None),
            P(("grp", "pair"), "ctx"),
            P(("grp", "pair"), "ctx"),
            P(("grp", "pair"), "ctx"),
        ),
        out_specs=(
            P(("grp", "pair"), "ctx", None),
            P(("grp", "pair"), "ctx", None),
            P(("grp", "pair"), "ctx", None),
            P("grp", None),
            P("grp", None),
        ),
        check_vma=False,
    )
```

```python
import jax
import jax.numpy as jnp
from jax import lax
from jax.sharding import PartitionSpec as P

HEAD_SIZE = 128
WINDOW = 1024
SEGS = 8


DPO_BETA = 0.1
LOSS_SCALE = 256.0
ADAPTER_SCALE = 2.0
ATTN_SCALE = 168.0 ** (-0.5)
NEG_FILL = -1e30


def from_partner(shard, axis, stride):
    return lax.ppermute(shard, axis, [(i, i ^ 1 << stride) for i in range(lax.axis_size(axis))])


def butterfly_sum(parts, axes, far_first=False):
    for axis in axes:
        size = lax.axis_size(axis)
        if size & (size - 1):
            parts = lax.psum(parts, axis)
            continue
        strides = list(range(size.bit_length() - 1))
        for stride in reversed(strides) if far_first else strides:
            got = from_partner(parts, axis, stride)
            parts = jax.tree.map(jnp.add, parts, got)
    return parts


def tree_spread(block, levels):
    count = 2 * levels
    climbed = []
    held = block
    for step in range(1, levels):
        held = lax.ppermute(held, "ctx", [(c - 2, c) for c in range(2 * step, count)])
        climbed.append(held)
    crossed = [lax.ppermute(block, "ctx", [(c - 1, c) for c in range(1, count, 2)])]
    for step in range(1, levels):
        crossed.append(
            lax.ppermute(climbed[step - 1], "ctx", [(c ^ 1, c) for c in range(2 * step, count)])
        )
    return climbed + crossed


def tree_gather(block, ctx_index, levels):
    count = 2 * levels
    partner = jnp.bitwise_xor(ctx_index, 1)
    got = [block]
    owners = [ctx_index]
    valid = [ctx_index >= 0]
    up, down = block, block
    ups, downs = [], []
    for step in range(1, levels):
        up = lax.ppermute(up, "ctx", [(c - 2, c) for c in range(2 * step, count)])
        down = lax.ppermute(down, "ctx", [(c + 2, c) for c in range(0, count - 2 * step)])
        ups.append(up)
        downs.append(down)
        got += [up, down]
        owners += [ctx_index - 2 * step, ctx_index + 2 * step]
        valid += [ctx_index >= 2 * step, ctx_index < count - 2 * step]
    got.append(lax.ppermute(block, "ctx", [(c ^ 1, c) for c in range(count)]))
    owners.append(partner)
    valid.append(ctx_index >= 0)
    for step in range(1, levels):
        got.append(lax.ppermute(ups[step - 1], "ctx", [(c ^ 1, c) for c in range(2 * step, count)]))
        got.append(
            lax.ppermute(downs[step - 1], "ctx", [(c ^ 1, c) for c in range(0, count - 2 * step)])
        )
        owners += [partner - 2 * step, partner + 2 * step]
        valid += [ctx_index >= 2 * step, ctx_index < count - 2 * step]
    rows = block.shape[0]
    whole = jnp.zeros(((count + 1) * rows,) + block.shape[1:], block.dtype)
    for piece, owner, ok in zip(got, owners, valid):
        place = jnp.where(ok, owner, count) * rows
        whole = lax.dynamic_update_slice_in_dim(whole, piece, place, 0)
    return whole[: count * rows]


def tree_slots(ctx_index, levels):
    partner = jnp.bitwise_xor(ctx_index, 1)
    owners, valid = [], []
    for step in range(1, levels):
        owners.append(ctx_index - 2 * step)
        valid.append(ctx_index >= 2 * step)
    owners.append(ctx_index - 1)
    valid.append(ctx_index % 2 == 1)
    for step in range(1, levels):
        owners.append(partner - 2 * step)
        valid.append(ctx_index >= 2 * step)
    return owners, valid


def tree_return(slot_parts, levels):
    count = 2 * levels
    climbed = slot_parts[: levels - 1]
    crossed = slot_parts[levels - 1 :]
    back = [lax.ppermute(crossed[0], "ctx", [(c, c - 1) for c in range(1, count, 2)])]
    for step in range(1, levels):
        back.append(
            lax.ppermute(crossed[step], "ctx", [(c, c ^ 1) for c in range(2 * step, count)])
        )
    total = back[0].astype(jnp.float32)
    carry = None
    for step in range(levels - 1, 0, -1):
        acc = climbed[step - 1].astype(jnp.float32) + back[step].astype(jnp.float32)
        if carry is not None:
            acc = acc + carry.astype(jnp.float32)
        carry = lax.ppermute(
            acc.astype(jnp.bfloat16), "ctx", [(c, c - 2) for c in range(2 * step, count)]
        )
    if carry is not None:
        total = total + carry.astype(jnp.float32)
    return total


def shifted(block, axis, distance):
    devices = range(lax.axis_size(axis))
    route = [(i - distance, i) for i in devices if i - distance in devices]
    return lax.ppermute(block, axis, route)


def shards(
    normed_input,
    queries,
    keys,
    value_projection,
    adapter_down,
    adapter_up,
    output_gradient,
    policy_logprob,
    reference_logprob,
    token_pair_index,
):
    tok_rows = normed_input.shape[1]
    width_kv = keys.shape[2]
    kv_heads = width_kv // HEAD_SIZE
    group_size = queries.shape[2] // width_kv
    hidden_rows = normed_input[0]
    own_keys = keys[0]
    pair_index = lax.axis_index("pair")
    ctx_index = lax.axis_index("ctx")
    half_cols = width_kv // 2
    own_half = lax.dynamic_slice_in_dim(value_projection, pair_index * half_cols, half_cols, 1)
    ctx_count = lax.axis_size("ctx")
    if ctx_count % 2 == 0 and 4 <= ctx_count <= 8:
        rows_half = tree_gather(own_half, ctx_index, ctx_count // 2)
    else:
        rows_half = lax.all_gather(own_half, "ctx", axis=0, tiled=True)
    if lax.axis_size("pair") == 2:
        other_half = from_partner(rows_half, "pair", 0)
        full_weight = jnp.zeros((rows_half.shape[0], width_kv), rows_half.dtype)
        full_weight = lax.dynamic_update_slice_in_dim(full_weight, rows_half, pair_index * half_cols, 1)
        full_weight = lax.dynamic_update_slice_in_dim(
            full_weight, other_half, (1 - pair_index) * half_cols, 1
        )
    else:
        full_weight = lax.all_gather(rows_half, "pair", axis=1, tiled=True)
    rank_projection = jnp.dot(hidden_rows, adapter_down, preferred_element_type=jnp.float32).astype(
        jnp.bfloat16
    )
    values = (
        jnp.dot(hidden_rows, full_weight, preferred_element_type=jnp.float32)
        + ADAPTER_SCALE * jnp.dot(rank_projection, adapter_up, preferred_element_type=jnp.float32)
    ).astype(jnp.bfloat16)
    segment_labels = token_pair_index[0]
    seg_table = (segment_labels[:, None] == jnp.arange(SEGS, dtype=jnp.int32)[None, :]).astype(
        jnp.float32
    )
    log_gap = policy_logprob[0] - reference_logprob[0]
    part_diff = jnp.sum(seg_table * log_gap[:, None], 0)
    part_count = jnp.sum(seg_table, 0)
    both_sums = butterfly_sum(jnp.concatenate([part_diff, part_count], 0), ("ctx",), far_first=True)
    own_diff, counts = both_sums[:SEGS], both_sums[SEGS:]
    other_diff = from_partner(own_diff, "pair", 0)
    direction = 1.0 - 2.0 * pair_index.astype(jnp.float32)
    margin = DPO_BETA * (direction * (own_diff - other_diff))
    coef = -direction * DPO_BETA * LOSS_SCALE * jax.nn.sigmoid(-margin)
    starts = jnp.cumsum(counts) - counts
    tok_start = jnp.sum(seg_table * starts[None, :], 1).astype(jnp.int32)
    token_coefficient = jnp.sum(seg_table * coef[None, :], 1)
    ctx_size = lax.axis_size("ctx")
    halo_blocks = min(WINDOW // tok_rows, ctx_size - 1)
    use_tree = halo_blocks == ctx_size - 1 and ctx_size % 2 == 0 and ctx_size >= 4
    levels = ctx_size // 2
    row_iota = jnp.arange(tok_rows, dtype=jnp.int32)
    if use_tree:
        key_blocks = tree_spread(own_keys, levels)
        value_blocks = tree_spread(values, levels)
        owners, valid = tree_slots(ctx_index, levels)
        far = jnp.int32(1 << 30)
        upos = jnp.concatenate(
            [jnp.where(ok, owner * tok_rows + row_iota, far) for owner, ok in zip(owners, valid)]
            + [ctx_index * tok_rows + row_iota],
            0,
        )
    else:
        key_blocks = []
        value_blocks = []
        for distance in range(halo_blocks, 0, -1):
            key_blocks.append(shifted(own_keys, "ctx", distance))
            value_blocks.append(shifted(values, "ctx", distance))
    all_keys = jnp.concatenate(key_blocks + [own_keys], 0)
    all_keys, own_values = lax.optimization_barrier((all_keys, values))
    all_values = jnp.concatenate(value_blocks + [own_values], 0)
    span = all_keys.shape[0]
    tpos = ctx_index * tok_rows + row_iota
    if not use_tree:
        upos = ctx_index * tok_rows - halo_blocks * tok_rows + jnp.arange(span, dtype=jnp.int32)
    allowed = (
        (upos[None, :] <= tpos[:, None])
        & (upos[None, :] > tpos[:, None] - WINDOW)
        & (upos[None, :] >= tok_start[:, None])
    )
    coef_rows = token_coefficient[None, :, None]
    query_rows = queries[0].reshape(tok_rows, kv_heads, group_size, HEAD_SIZE)
    grad_rows = output_gradient[0].reshape(tok_rows, kv_heads, group_size, HEAD_SIZE)
    key_rows = all_keys.reshape(span, kv_heads, HEAD_SIZE)
    value_rows = all_values.reshape(span, kv_heads, HEAD_SIZE)
    scores = ATTN_SCALE * jnp.einsum(
        "tjgd,ljd->jgtl", query_rows, key_rows, preferred_element_type=jnp.float32
    )
    masked = jnp.where(allowed[None, None], scores, NEG_FILL)
    row_max = jnp.max(masked, -1, keepdims=True)
    weights_exp = jnp.where(allowed[None, None], jnp.exp(masked - row_max), 0.0)
    attn_probs = weights_exp / jnp.sum(weights_exp, -1, keepdims=True)
    prob_grad = coef_rows[None] * jnp.einsum(
        "tjgd,ljd->jgtl", grad_rows, value_rows, preferred_element_type=jnp.float32
    )
    row_delta = jnp.sum(attn_probs * prob_grad, -1, keepdims=True)
    score_grad = (ATTN_SCALE * attn_probs * (prob_grad - row_delta)).astype(jnp.bfloat16)
    query_grad = jnp.einsum(
        "jgtl,ljd->tjgd", score_grad, key_rows, preferred_element_type=jnp.float32
    ).astype(jnp.bfloat16).reshape(tok_rows, kv_heads * group_size * HEAD_SIZE)
    key_parts = jnp.einsum(
        "jgtl,tjgd->ljd", score_grad, query_rows, preferred_element_type=jnp.float32
    ).reshape(span, width_kv)
    weighted = (attn_probs * coef_rows[None]).astype(jnp.bfloat16)
    value_parts = jnp.einsum(
        "jgtl,tjgd->ljd", weighted, grad_rows, preferred_element_type=jnp.float32
    ).reshape(span, width_kv)
    key_total = key_parts[halo_blocks * tok_rows :]
    value_total = value_parts[halo_blocks * tok_rows :]
    if use_tree:
        slot_rows = lambda parts: [
            parts[k * tok_rows : (k + 1) * tok_rows].astype(jnp.bfloat16) for k in range(halo_blocks)
        ]
        key_total = key_total + tree_return(slot_rows(key_parts), levels)
        value_total = value_total + tree_return(slot_rows(value_parts), levels)
    else:
        for distance in range(1, halo_blocks + 1):
            block_start = (halo_blocks - distance) * tok_rows
            send_keys = key_parts[block_start : block_start + tok_rows].astype(jnp.bfloat16)
            send_values = value_parts[block_start : block_start + tok_rows].astype(jnp.bfloat16)
            back_keys, back_values = shifted((send_keys, send_values), "ctx", -distance)
            key_total = key_total + back_keys.astype(jnp.float32)
            value_total = value_total + back_values.astype(jnp.float32)
    key_grad = key_total.astype(jnp.bfloat16)
    value_gradient = value_total.astype(jnp.bfloat16)
    rank_middle = jnp.einsum(
        "sj,zj->sz", value_gradient, adapter_up, preferred_element_type=jnp.float32
    ).astype(jnp.bfloat16)
    input_grad = (
        jnp.einsum("tk,dk->td", value_gradient, full_weight, preferred_element_type=jnp.float32)
        + ADAPTER_SCALE
        * jnp.einsum("pb,wb->pw", rank_middle, adapter_down, preferred_element_type=jnp.float32)
    ).astype(jnp.bfloat16)
    up_factor = ADAPTER_SCALE * jnp.einsum(
        "tr,tk->rk", rank_projection, value_gradient, preferred_element_type=jnp.float32
    )
    down_factor = ADAPTER_SCALE * jnp.einsum(
        "td,tr->dr", hidden_rows, rank_middle, preferred_element_type=jnp.float32
    )
    down_size = down_factor.size
    flat = jnp.concatenate([down_factor.reshape(-1), up_factor.reshape(-1)], 0)
    flat = butterfly_sum(flat.reshape(-1, HEAD_SIZE), ("ctx", "pair"), far_first=True).reshape(-1)
    down_gradient = flat[:down_size].reshape(down_factor.shape)
    up_gradient = flat[down_size:].reshape(up_factor.shape)
    return (input_grad[None], query_grad[None], key_grad[None], down_gradient, up_gradient)


def solution(mesh):
    return jax.shard_map(
        shards,
        mesh=mesh,
        in_specs=(
            P(("grp", "pair"), "ctx", None),
            P(("grp", "pair"), "ctx", None),
            P(("grp", "pair"), "ctx", None),
            P("ctx", None),
            P(),
            P(),
            P(("grp", "pair"), "ctx", None),
            P(("grp", "pair"), "ctx"),
            P(("grp", "pair"), "ctx"),
            P(("grp", "pair"), "ctx"),
        ),
        out_specs=(
            P(("grp", "pair"), "ctx", None),
            P(("grp", "pair"), "ctx", None),
            P(("grp", "pair"), "ctx", None),
            P("grp", None),
            P("grp", None),
        ),
        check_vma=False,
    )
```

```python
import jax
import jax.numpy as jnp
from jax import lax
from jax.sharding import PartitionSpec as P

HEAD_SIZE = 128
WINDOW = 1024
SEGS = 8


DPO_BETA = 0.1
LOSS_SCALE = 256.0
ADAPTER_SCALE = 2.0
ATTN_SCALE = 168.0 ** (-0.5)
NEG_FILL = -1e30


def from_partner(shard, axis, stride):
    return lax.ppermute(shard, axis, [(i, i ^ 1 << stride) for i in range(lax.axis_size(axis))])


def butterfly_sum(parts, axes, far_first=False):
    for axis in axes:
        size = lax.axis_size(axis)
        if size & (size - 1):
            parts = lax.psum(parts, axis)
            continue
        strides = list(range(size.bit_length() - 1))
        for stride in reversed(strides) if far_first else strides:
            got = from_partner(parts, axis, stride)
            parts = jax.tree.map(jnp.add, parts, got)
    return parts


def tree_spread(block, levels):
    count = 2 * levels
    climbed = []
    held = block
    for step in range(1, levels):
        held = lax.ppermute(held, "ctx", [(c - 2, c) for c in range(2 * step, count)])
        climbed.append(held)
    crossed = [lax.ppermute(block, "ctx", [(c - 1, c) for c in range(1, count, 2)])]
    for step in range(1, levels):
        crossed.append(
            lax.ppermute(climbed[step - 1], "ctx", [(c ^ 1, c) for c in range(2 * step, count)])
        )
    return climbed + crossed


def tree_gather(block, ctx_index, levels):
    count = 2 * levels
    partner = jnp.bitwise_xor(ctx_index, 1)
    got = [block, lax.ppermute(block, "ctx", [(c ^ 1, c) for c in range(count)])]
    owners = [ctx_index, partner]
    valid = [ctx_index >= 0, ctx_index >= 0]
    up, down = block, block
    ups, downs = [], []
    for step in range(1, levels):
        up = lax.ppermute(up, "ctx", [(c - 2, c) for c in range(2 * step, count)])
        down = lax.ppermute(down, "ctx", [(c + 2, c) for c in range(0, count - 2 * step)])
        ups.append(up)
        downs.append(down)
        got += [up, down]
        owners += [ctx_index - 2 * step, ctx_index + 2 * step]
        valid += [ctx_index >= 2 * step, ctx_index < count - 2 * step]
    for step in range(1, levels):
        got.append(lax.ppermute(ups[step - 1], "ctx", [(c ^ 1, c) for c in range(2 * step, count)]))
        got.append(
            lax.ppermute(downs[step - 1], "ctx", [(c ^ 1, c) for c in range(0, count - 2 * step)])
        )
        owners += [partner - 2 * step, partner + 2 * step]
        valid += [ctx_index >= 2 * step, ctx_index < count - 2 * step]
    rows = block.shape[0]
    whole = jnp.zeros(((count + 1) * rows,) + block.shape[1:], block.dtype)
    for piece, owner, ok in zip(got, owners, valid):
        place = jnp.where(ok, owner, count) * rows
        whole = lax.dynamic_update_slice_in_dim(whole, piece, place, 0)
    return whole[: count * rows]


def tree_slots(ctx_index, levels):
    partner = jnp.bitwise_xor(ctx_index, 1)
    owners, valid = [], []
    for step in range(1, levels):
        owners.append(ctx_index - 2 * step)
        valid.append(ctx_index >= 2 * step)
    owners.append(ctx_index - 1)
    valid.append(ctx_index % 2 == 1)
    for step in range(1, levels):
        owners.append(partner - 2 * step)
        valid.append(ctx_index >= 2 * step)
    return owners, valid


def tree_return(slot_parts, levels):
    count = 2 * levels
    climbed = slot_parts[: levels - 1]
    crossed = slot_parts[levels - 1 :]
    back = [lax.ppermute(crossed[0], "ctx", [(c, c - 1) for c in range(1, count, 2)])]
    for step in range(1, levels):
        back.append(
            lax.ppermute(crossed[step], "ctx", [(c, c ^ 1) for c in range(2 * step, count)])
        )
    total = back[0].astype(jnp.float32)
    carry = None
    for step in range(levels - 1, 0, -1):
        acc = climbed[step - 1].astype(jnp.float32) + back[step].astype(jnp.float32)
        if carry is not None:
            acc = acc + carry.astype(jnp.float32)
        carry = lax.ppermute(
            acc.astype(jnp.bfloat16), "ctx", [(c, c - 2) for c in range(2 * step, count)]
        )
    if carry is not None:
        total = total + carry.astype(jnp.float32)
    return total


def shifted(block, axis, distance):
    devices = range(lax.axis_size(axis))
    route = [(i - distance, i) for i in devices if i - distance in devices]
    return lax.ppermute(block, axis, route)


def shards(
    normed_input,
    queries,
    keys,
    value_projection,
    adapter_down,
    adapter_up,
    output_gradient,
    policy_logprob,
    reference_logprob,
    token_pair_index,
):
    tok_rows = normed_input.shape[1]
    width_kv = keys.shape[2]
    kv_heads = width_kv // HEAD_SIZE
    group_size = queries.shape[2] // width_kv
    hidden_rows = normed_input[0]
    own_keys = keys[0]
    pair_index = lax.axis_index("pair")
    ctx_index = lax.axis_index("ctx")
    half_cols = width_kv // 2
    own_half = lax.dynamic_slice_in_dim(value_projection, pair_index * half_cols, half_cols, 1)
    ctx_count = lax.axis_size("ctx")
    if ctx_count % 2 == 0 and 4 <= ctx_count <= 8:
        rows_half = tree_gather(own_half, ctx_index, ctx_count // 2)
    else:
        rows_half = lax.all_gather(own_half, "ctx", axis=0, tiled=True)
    if lax.axis_size("pair") == 2:
        other_half = from_partner(rows_half, "pair", 0)
        full_weight = jnp.zeros((rows_half.shape[0], width_kv), rows_half.dtype)
        full_weight = lax.dynamic_update_slice_in_dim(full_weight, rows_half, pair_index * half_cols, 1)
        full_weight = lax.dynamic_update_slice_in_dim(
            full_weight, other_half, (1 - pair_index) * half_cols, 1
        )
    else:
        full_weight = lax.all_gather(rows_half, "pair", axis=1, tiled=True)
    rank_projection = jnp.dot(hidden_rows, adapter_down, preferred_element_type=jnp.float32).astype(
        jnp.bfloat16
    )
    values = (
        jnp.dot(hidden_rows, full_weight, preferred_element_type=jnp.float32)
        + ADAPTER_SCALE * jnp.dot(rank_projection, adapter_up, preferred_element_type=jnp.float32)
    ).astype(jnp.bfloat16)
    segment_labels = token_pair_index[0]
    seg_table = (segment_labels[:, None] == jnp.arange(SEGS, dtype=jnp.int32)[None, :]).astype(
        jnp.float32
    )
    log_gap = policy_logprob[0] - reference_logprob[0]
    part_diff = jnp.sum(seg_table * log_gap[:, None], 0)
    part_count = jnp.sum(seg_table, 0)
    both_sums = butterfly_sum(jnp.concatenate([part_diff, part_count], 0), ("ctx",), far_first=True)
    own_diff, counts = both_sums[:SEGS], both_sums[SEGS:]
    other_diff = from_partner(own_diff, "pair", 0)
    direction = 1.0 - 2.0 * pair_index.astype(jnp.float32)
    margin = DPO_BETA * (direction * (own_diff - other_diff))
    coef = -direction * DPO_BETA * LOSS_SCALE * jax.nn.sigmoid(-margin)
    starts = jnp.cumsum(counts) - counts
    tok_start = jnp.sum(seg_table * starts[None, :], 1).astype(jnp.int32)
    token_coefficient = jnp.sum(seg_table * coef[None, :], 1)
    ctx_size = lax.axis_size("ctx")
    halo_blocks = min(WINDOW // tok_rows, ctx_size - 1)
    use_tree = halo_blocks == ctx_size - 1 and ctx_size % 2 == 0 and ctx_size >= 4
    levels = ctx_size // 2
    row_iota = jnp.arange(tok_rows, dtype=jnp.int32)
    if use_tree:
        key_blocks = tree_spread(own_keys, levels)
        value_blocks = tree_spread(values, levels)
        owners, valid = tree_slots(ctx_index, levels)
        far = jnp.int32(1 << 30)
        upos = jnp.concatenate(
            [jnp.where(ok, owner * tok_rows + row_iota, far) for owner, ok in zip(owners, valid)]
            + [ctx_index * tok_rows + row_iota],
            0,
        )
    else:
        key_blocks = []
        value_blocks = []
        for distance in range(halo_blocks, 0, -1):
            key_blocks.append(shifted(own_keys, "ctx", distance))
            value_blocks.append(shifted(values, "ctx", distance))
    all_keys = jnp.concatenate(key_blocks + [own_keys], 0)
    all_keys, own_values = lax.optimization_barrier((all_keys, values))
    all_values = jnp.concatenate(value_blocks + [own_values], 0)
    span = all_keys.shape[0]
    tpos = ctx_index * tok_rows + row_iota
    if not use_tree:
        upos = ctx_index * tok_rows - halo_blocks * tok_rows + jnp.arange(span, dtype=jnp.int32)
    allowed = (
        (upos[None, :] <= tpos[:, None])
        & (upos[None, :] > tpos[:, None] - WINDOW)
        & (upos[None, :] >= tok_start[:, None])
    )
    coef_rows = token_coefficient[None, :, None]
    query_rows = queries[0].reshape(tok_rows, kv_heads, group_size, HEAD_SIZE)
    grad_rows = output_gradient[0].reshape(tok_rows, kv_heads, group_size, HEAD_SIZE)
    key_rows = all_keys.reshape(span, kv_heads, HEAD_SIZE)
    value_rows = all_values.reshape(span, kv_heads, HEAD_SIZE)
    scores = ATTN_SCALE * jnp.einsum(
        "tjgd,ljd->jgtl", query_rows, key_rows, preferred_element_type=jnp.float32
    )
    masked = jnp.where(allowed[None, None], scores, NEG_FILL)
    row_max = jnp.max(masked, -1, keepdims=True)
    weights_exp = jnp.where(allowed[None, None], jnp.exp(masked - row_max), 0.0)
    attn_probs = weights_exp / jnp.sum(weights_exp, -1, keepdims=True)
    prob_grad = coef_rows[None] * jnp.einsum(
        "tjgd,ljd->jgtl", grad_rows, value_rows, preferred_element_type=jnp.float32
    )
    row_delta = jnp.sum(attn_probs * prob_grad, -1, keepdims=True)
    score_grad = (ATTN_SCALE * attn_probs * (prob_grad - row_delta)).astype(jnp.bfloat16)
    query_grad = jnp.einsum(
        "jgtl,ljd->tjgd", score_grad, key_rows, preferred_element_type=jnp.float32
    ).astype(jnp.bfloat16).reshape(tok_rows, kv_heads * group_size * HEAD_SIZE)
    key_parts = jnp.einsum(
        "jgtl,tjgd->ljd", score_grad, query_rows, preferred_element_type=jnp.float32
    ).reshape(span, width_kv)
    weighted = (attn_probs * coef_rows[None]).astype(jnp.bfloat16)
    value_parts = jnp.einsum(
        "jgtl,tjgd->ljd", weighted, grad_rows, preferred_element_type=jnp.float32
    ).reshape(span, width_kv)
    key_total = key_parts[halo_blocks * tok_rows :]
    value_total = value_parts[halo_blocks * tok_rows :]
    if use_tree:
        slot_rows = lambda parts: [
            parts[k * tok_rows : (k + 1) * tok_rows].astype(jnp.bfloat16) for k in range(halo_blocks)
        ]
        key_total = key_total + tree_return(slot_rows(key_parts), levels)
        value_total = value_total + tree_return(slot_rows(value_parts), levels)
    else:
        for distance in range(1, halo_blocks + 1):
            block_start = (halo_blocks - distance) * tok_rows
            send_keys = key_parts[block_start : block_start + tok_rows].astype(jnp.bfloat16)
            send_values = value_parts[block_start : block_start + tok_rows].astype(jnp.bfloat16)
            back_keys, back_values = shifted((send_keys, send_values), "ctx", -distance)
            key_total = key_total + back_keys.astype(jnp.float32)
            value_total = value_total + back_values.astype(jnp.float32)
    key_grad = key_total.astype(jnp.bfloat16)
    value_gradient = value_total.astype(jnp.bfloat16)
    rank_middle = jnp.einsum(
        "sj,zj->sz", value_gradient, adapter_up, preferred_element_type=jnp.float32
    ).astype(jnp.bfloat16)
    input_grad = (
        jnp.einsum("tk,dk->td", value_gradient, full_weight, preferred_element_type=jnp.float32)
        + ADAPTER_SCALE
        * jnp.einsum("pb,wb->pw", rank_middle, adapter_down, preferred_element_type=jnp.float32)
    ).astype(jnp.bfloat16)
    up_factor = ADAPTER_SCALE * jnp.einsum(
        "tr,tk->rk", rank_projection, value_gradient, preferred_element_type=jnp.float32
    )
    down_factor = ADAPTER_SCALE * jnp.einsum(
        "td,tr->dr", hidden_rows, rank_middle, preferred_element_type=jnp.float32
    )
    down_size = down_factor.size
    flat = jnp.concatenate([down_factor.reshape(-1), up_factor.reshape(-1)], 0)
    flat = butterfly_sum(flat.reshape(-1, HEAD_SIZE), ("ctx", "pair"), far_first=True).reshape(-1)
    down_gradient = flat[:down_size].reshape(down_factor.shape)
    up_gradient = flat[down_size:].reshape(up_factor.shape)
    return (input_grad[None], query_grad[None], key_grad[None], down_gradient, up_gradient)


def solution(mesh):
    return jax.shard_map(
        shards,
        mesh=mesh,
        in_specs=(
            P(("grp", "pair"), "ctx", None),
            P(("grp", "pair"), "ctx", None),
            P(("grp", "pair"), "ctx", None),
            P("ctx", None),
            P(),
            P(),
            P(("grp", "pair"), "ctx", None),
            P(("grp", "pair"), "ctx"),
            P(("grp", "pair"), "ctx"),
            P(("grp", "pair"), "ctx"),
        ),
        out_specs=(
            P(("grp", "pair"), "ctx", None),
            P(("grp", "pair"), "ctx", None),
            P(("grp", "pair"), "ctx", None),
            P("grp", None),
            P("grp", None),
        ),
        check_vma=False,
    )
```

```python
import jax
import jax.numpy as jnp
from jax import lax
from jax.sharding import PartitionSpec as P

HEAD_SIZE = 128
WINDOW = 1024
SEGS = 8


DPO_BETA = 0.1
LOSS_SCALE = 256.0
ADAPTER_SCALE = 2.0
ATTN_SCALE = 168.0 ** (-0.5)
NEG_FILL = -1e30


def from_partner(shard, axis, stride):
    return lax.ppermute(shard, axis, [(i, i ^ 1 << stride) for i in range(lax.axis_size(axis))])


def butterfly_sum(parts, axes, far_first=False):
    for axis in axes:
        size = lax.axis_size(axis)
        if size & (size - 1):
            parts = lax.psum(parts, axis)
            continue
        strides = list(range(size.bit_length() - 1))
        for stride in reversed(strides) if far_first else strides:
            got = from_partner(parts, axis, stride)
            parts = jax.tree.map(jnp.add, parts, got)
    return parts


def tree_spread(block, levels):
    count = 2 * levels
    crossed = [lax.ppermute(block, "ctx", [(c - 1, c) for c in range(1, count, 2)])]
    climbed = []
    held = block
    for step in range(1, levels):
        held = lax.ppermute(held, "ctx", [(c - 2, c) for c in range(2 * step, count)])
        climbed.append(held)
    for step in range(1, levels):
        crossed.append(
            lax.ppermute(climbed[step - 1], "ctx", [(c ^ 1, c) for c in range(2 * step, count)])
        )
    return climbed + crossed


def tree_gather(block, ctx_index, levels):
    count = 2 * levels
    partner = jnp.bitwise_xor(ctx_index, 1)
    got = [block, lax.ppermute(block, "ctx", [(c ^ 1, c) for c in range(count)])]
    owners = [ctx_index, partner]
    valid = [ctx_index >= 0, ctx_index >= 0]
    up, down = block, block
    ups, downs = [], []
    for step in range(1, levels):
        up = lax.ppermute(up, "ctx", [(c - 2, c) for c in range(2 * step, count)])
        down = lax.ppermute(down, "ctx", [(c + 2, c) for c in range(0, count - 2 * step)])
        ups.append(up)
        downs.append(down)
        got += [up, down]
        owners += [ctx_index - 2 * step, ctx_index + 2 * step]
        valid += [ctx_index >= 2 * step, ctx_index < count - 2 * step]
    for step in range(1, levels):
        got.append(lax.ppermute(ups[step - 1], "ctx", [(c ^ 1, c) for c in range(2 * step, count)]))
        got.append(
            lax.ppermute(downs[step - 1], "ctx", [(c ^ 1, c) for c in range(0, count - 2 * step)])
        )
        owners += [partner - 2 * step, partner + 2 * step]
        valid += [ctx_index >= 2 * step, ctx_index < count - 2 * step]
    rows = block.shape[0]
    whole = jnp.zeros(((count + 1) * rows,) + block.shape[1:], block.dtype)
    for piece, owner, ok in zip(got, owners, valid):
        place = jnp.where(ok, owner, count) * rows
        whole = lax.dynamic_update_slice_in_dim(whole, piece, place, 0)
    return whole[: count * rows]


def tree_slots(ctx_index, levels):
    partner = jnp.bitwise_xor(ctx_index, 1)
    owners, valid = [], []
    for step in range(1, levels):
        owners.append(ctx_index - 2 * step)
        valid.append(ctx_index >= 2 * step)
    owners.append(ctx_index - 1)
    valid.append(ctx_index % 2 == 1)
    for step in range(1, levels):
        owners.append(partner - 2 * step)
        valid.append(ctx_index >= 2 * step)
    return owners, valid


def tree_return(slot_parts, levels):
    count = 2 * levels
    climbed = slot_parts[: levels - 1]
    crossed = slot_parts[levels - 1 :]
    back = [lax.ppermute(crossed[0], "ctx", [(c, c - 1) for c in range(1, count, 2)])]
    for step in range(1, levels):
        back.append(
            lax.ppermute(crossed[step], "ctx", [(c, c ^ 1) for c in range(2 * step, count)])
        )
    total = back[0].astype(jnp.float32)
    carry = None
    for step in range(levels - 1, 0, -1):
        acc = climbed[step - 1].astype(jnp.float32) + back[step].astype(jnp.float32)
        if carry is not None:
            acc = acc + carry.astype(jnp.float32)
        carry = lax.ppermute(
            acc.astype(jnp.bfloat16), "ctx", [(c, c - 2) for c in range(2 * step, count)]
        )
    if carry is not None:
        total = total + carry.astype(jnp.float32)
    return total


def shifted(block, axis, distance):
    devices = range(lax.axis_size(axis))
    route = [(i - distance, i) for i in devices if i - distance in devices]
    return lax.ppermute(block, axis, route)


def shards(
    normed_input,
    queries,
    keys,
    value_projection,
    adapter_down,
    adapter_up,
    output_gradient,
    policy_logprob,
    reference_logprob,
    token_pair_index,
):
    tok_rows = normed_input.shape[1]
    width_kv = keys.shape[2]
    kv_heads = width_kv // HEAD_SIZE
    group_size = queries.shape[2] // width_kv
    hidden_rows = normed_input[0]
    own_keys = keys[0]
    pair_index = lax.axis_index("pair")
    ctx_index = lax.axis_index("ctx")
    half_cols = width_kv // 2
    own_half = lax.dynamic_slice_in_dim(value_projection, pair_index * half_cols, half_cols, 1)
    ctx_count = lax.axis_size("ctx")
    if ctx_count % 2 == 0 and 4 <= ctx_count <= 8:
        rows_half = tree_gather(own_half, ctx_index, ctx_count // 2)
    else:
        rows_half = lax.all_gather(own_half, "ctx", axis=0, tiled=True)
    if lax.axis_size("pair") == 2:
        other_half = from_partner(rows_half, "pair", 0)
        full_weight = jnp.zeros((rows_half.shape[0], width_kv), rows_half.dtype)
        full_weight = lax.dynamic_update_slice_in_dim(full_weight, rows_half, pair_index * half_cols, 1)
        full_weight = lax.dynamic_update_slice_in_dim(
            full_weight, other_half, (1 - pair_index) * half_cols, 1
        )
    else:
        full_weight = lax.all_gather(rows_half, "pair", axis=1, tiled=True)
    rank_projection = jnp.dot(hidden_rows, adapter_down, preferred_element_type=jnp.float32).astype(
        jnp.bfloat16
    )
    values = (
        jnp.dot(hidden_rows, full_weight, preferred_element_type=jnp.float32)
        + ADAPTER_SCALE * jnp.dot(rank_projection, adapter_up, preferred_element_type=jnp.float32)
    ).astype(jnp.bfloat16)
    segment_labels = token_pair_index[0]
    seg_table = (segment_labels[:, None] == jnp.arange(SEGS, dtype=jnp.int32)[None, :]).astype(
        jnp.float32
    )
    log_gap = policy_logprob[0] - reference_logprob[0]
    part_diff = jnp.sum(seg_table * log_gap[:, None], 0)
    part_count = jnp.sum(seg_table, 0)
    both_sums = butterfly_sum(jnp.concatenate([part_diff, part_count], 0), ("ctx",), far_first=True)
    own_diff, counts = both_sums[:SEGS], both_sums[SEGS:]
    other_diff = from_partner(own_diff, "pair", 0)
    direction = 1.0 - 2.0 * pair_index.astype(jnp.float32)
    margin = DPO_BETA * (direction * (own_diff - other_diff))
    coef = -direction * DPO_BETA * LOSS_SCALE * jax.nn.sigmoid(-margin)
    starts = jnp.cumsum(counts) - counts
    tok_start = jnp.sum(seg_table * starts[None, :], 1).astype(jnp.int32)
    token_coefficient = jnp.sum(seg_table * coef[None, :], 1)
    ctx_size = lax.axis_size("ctx")
    halo_blocks = min(WINDOW // tok_rows, ctx_size - 1)
    use_tree = halo_blocks == ctx_size - 1 and ctx_size % 2 == 0 and ctx_size >= 4
    levels = ctx_size // 2
    row_iota = jnp.arange(tok_rows, dtype=jnp.int32)
    if use_tree:
        key_blocks = tree_spread(own_keys, levels)
        value_blocks = tree_spread(values, levels)
        owners, valid = tree_slots(ctx_index, levels)
        far = jnp.int32(1 << 30)
        upos = jnp.concatenate(
            [jnp.where(ok, owner * tok_rows + row_iota, far) for owner, ok in zip(owners, valid)]
            + [ctx_index * tok_rows + row_iota],
            0,
        )
    else:
        key_blocks = []
        value_blocks = []
        for distance in range(halo_blocks, 0, -1):
            key_blocks.append(shifted(own_keys, "ctx", distance))
            value_blocks.append(shifted(values, "ctx", distance))
    all_keys = jnp.concatenate(key_blocks + [own_keys], 0)
    all_keys, own_values = lax.optimization_barrier((all_keys, values))
    all_values = jnp.concatenate(value_blocks + [own_values], 0)
    span = all_keys.shape[0]
    tpos = ctx_index * tok_rows + row_iota
    if not use_tree:
        upos = ctx_index * tok_rows - halo_blocks * tok_rows + jnp.arange(span, dtype=jnp.int32)
    allowed = (
        (upos[None, :] <= tpos[:, None])
        & (upos[None, :] > tpos[:, None] - WINDOW)
        & (upos[None, :] >= tok_start[:, None])
    )
    coef_rows = token_coefficient[None, :, None]
    query_rows = queries[0].reshape(tok_rows, kv_heads, group_size, HEAD_SIZE)
    grad_rows = output_gradient[0].reshape(tok_rows, kv_heads, group_size, HEAD_SIZE)
    key_rows = all_keys.reshape(span, kv_heads, HEAD_SIZE)
    value_rows = all_values.reshape(span, kv_heads, HEAD_SIZE)
    scores = ATTN_SCALE * jnp.einsum(
        "tjgd,ljd->jgtl", query_rows, key_rows, preferred_element_type=jnp.float32
    )
    masked = jnp.where(allowed[None, None], scores, NEG_FILL)
    row_max = jnp.max(masked, -1, keepdims=True)
    weights_exp = jnp.where(allowed[None, None], jnp.exp(masked - row_max), 0.0)
    attn_probs = weights_exp / jnp.sum(weights_exp, -1, keepdims=True)
    prob_grad = coef_rows[None] * jnp.einsum(
        "tjgd,ljd->jgtl", grad_rows, value_rows, preferred_element_type=jnp.float32
    )
    row_delta = jnp.sum(attn_probs * prob_grad, -1, keepdims=True)
    score_grad = (ATTN_SCALE * attn_probs * (prob_grad - row_delta)).astype(jnp.bfloat16)
    query_grad = jnp.einsum(
        "jgtl,ljd->tjgd", score_grad, key_rows, preferred_element_type=jnp.float32
    ).astype(jnp.bfloat16).reshape(tok_rows, kv_heads * group_size * HEAD_SIZE)
    key_parts = jnp.einsum(
        "jgtl,tjgd->ljd", score_grad, query_rows, preferred_element_type=jnp.float32
    ).reshape(span, width_kv)
    weighted = (attn_probs * coef_rows[None]).astype(jnp.bfloat16)
    value_parts = jnp.einsum(
        "jgtl,tjgd->ljd", weighted, grad_rows, preferred_element_type=jnp.float32
    ).reshape(span, width_kv)
    key_total = key_parts[halo_blocks * tok_rows :]
    value_total = value_parts[halo_blocks * tok_rows :]
    if use_tree:
        slot_rows = lambda parts: [
            parts[k * tok_rows : (k + 1) * tok_rows].astype(jnp.bfloat16) for k in range(halo_blocks)
        ]
        key_total = key_total + tree_return(slot_rows(key_parts), levels)
        value_total = value_total + tree_return(slot_rows(value_parts), levels)
    else:
        for distance in range(1, halo_blocks + 1):
            block_start = (halo_blocks - distance) * tok_rows
            send_keys = key_parts[block_start : block_start + tok_rows].astype(jnp.bfloat16)
            send_values = value_parts[block_start : block_start + tok_rows].astype(jnp.bfloat16)
            back_keys, back_values = shifted((send_keys, send_values), "ctx", -distance)
            key_total = key_total + back_keys.astype(jnp.float32)
            value_total = value_total + back_values.astype(jnp.float32)
    key_grad = key_total.astype(jnp.bfloat16)
    value_gradient = value_total.astype(jnp.bfloat16)
    rank_middle = jnp.einsum(
        "sj,zj->sz", value_gradient, adapter_up, preferred_element_type=jnp.float32
    ).astype(jnp.bfloat16)
    input_grad = (
        jnp.einsum("tk,dk->td", value_gradient, full_weight, preferred_element_type=jnp.float32)
        + ADAPTER_SCALE
        * jnp.einsum("pb,wb->pw", rank_middle, adapter_down, preferred_element_type=jnp.float32)
    ).astype(jnp.bfloat16)
    up_factor = ADAPTER_SCALE * jnp.einsum(
        "tr,tk->rk", rank_projection, value_gradient, preferred_element_type=jnp.float32
    )
    down_factor = ADAPTER_SCALE * jnp.einsum(
        "td,tr->dr", hidden_rows, rank_middle, preferred_element_type=jnp.float32
    )
    down_size = down_factor.size
    flat = jnp.concatenate([down_factor.reshape(-1), up_factor.reshape(-1)], 0)
    flat = butterfly_sum(flat.reshape(-1, HEAD_SIZE), ("ctx", "pair"), far_first=True).reshape(-1)
    down_gradient = flat[:down_size].reshape(down_factor.shape)
    up_gradient = flat[down_size:].reshape(up_factor.shape)
    return (input_grad[None], query_grad[None], key_grad[None], down_gradient, up_gradient)


def solution(mesh):
    return jax.shard_map(
        shards,
        mesh=mesh,
        in_specs=(
            P(("grp", "pair"), "ctx", None),
            P(("grp", "pair"), "ctx", None),
            P(("grp", "pair"), "ctx", None),
            P("ctx", None),
            P(),
            P(),
            P(("grp", "pair"), "ctx", None),
            P(("grp", "pair"), "ctx"),
            P(("grp", "pair"), "ctx"),
            P(("grp", "pair"), "ctx"),
        ),
        out_specs=(
            P(("grp", "pair"), "ctx", None),
            P(("grp", "pair"), "ctx", None),
            P(("grp", "pair"), "ctx", None),
            P("grp", None),
            P("grp", None),
        ),
        check_vma=False,
    )
```

```python
import jax
import jax.numpy as jnp
from jax import lax
from jax.sharding import PartitionSpec as P

HEAD_SIZE = 128
WINDOW = 1024
SEGS = 8


DPO_BETA = 0.1
LOSS_SCALE = 256.0
ADAPTER_SCALE = 2.0
ATTN_SCALE = 168.0 ** (-0.5)
NEG_FILL = -1e30


def from_partner(shard, axis, stride):
    return lax.ppermute(shard, axis, [(i, i ^ 1 << stride) for i in range(lax.axis_size(axis))])


def butterfly_sum(parts, axes, far_first=False):
    for axis in axes:
        size = lax.axis_size(axis)
        if size & (size - 1):
            parts = lax.psum(parts, axis)
            continue
        strides = list(range(size.bit_length() - 1))
        for stride in reversed(strides) if far_first else strides:
            got = from_partner(parts, axis, stride)
            parts = jax.tree.map(jnp.add, parts, got)
    return parts


def tree_spread(block, levels):
    count = 2 * levels
    climbed = []
    held = block
    for step in range(1, levels):
        held = lax.ppermute(held, "ctx", [(c - 2, c) for c in range(2 * step, count)])
        climbed.append(held)
    crossed = [lax.ppermute(block, "ctx", [(c - 1, c) for c in range(1, count, 2)])]
    for step in range(1, levels):
        crossed.append(
            lax.ppermute(climbed[step - 1], "ctx", [(c ^ 1, c) for c in range(2 * step, count)])
        )
    return climbed + crossed


def tree_gather(block, ctx_index, levels):
    count = 2 * levels
    partner = jnp.bitwise_xor(ctx_index, 1)
    got = [block, lax.ppermute(block, "ctx", [(c ^ 1, c) for c in range(count)])]
    owners = [ctx_index, partner]
    valid = [ctx_index >= 0, ctx_index >= 0]
    up, down = block, block
    ups, downs = [], []
    for step in range(1, levels):
        up = lax.ppermute(up, "ctx", [(c - 2, c) for c in range(2 * step, count)])
        down = lax.ppermute(down, "ctx", [(c + 2, c) for c in range(0, count - 2 * step)])
        ups.append(up)
        downs.append(down)
        got += [up, down]
        owners += [ctx_index - 2 * step, ctx_index + 2 * step]
        valid += [ctx_index >= 2 * step, ctx_index < count - 2 * step]
    for step in range(1, levels):
        got.append(lax.ppermute(ups[step - 1], "ctx", [(c ^ 1, c) for c in range(2 * step, count)]))
        got.append(
            lax.ppermute(downs[step - 1], "ctx", [(c ^ 1, c) for c in range(0, count - 2 * step)])
        )
        owners += [partner - 2 * step, partner + 2 * step]
        valid += [ctx_index >= 2 * step, ctx_index < count - 2 * step]
    rows = block.shape[0]
    whole = jnp.zeros(((count + 1) * rows,) + block.shape[1:], block.dtype)
    for piece, owner, ok in zip(got, owners, valid):
        place = jnp.where(ok, owner, count) * rows
        whole = lax.dynamic_update_slice_in_dim(whole, piece, place, 0)
    return whole[: count * rows]


def tree_slots(ctx_index, levels):
    partner = jnp.bitwise_xor(ctx_index, 1)
    owners, valid = [], []
    for step in range(1, levels):
        owners.append(ctx_index - 2 * step)
        valid.append(ctx_index >= 2 * step)
    owners.append(ctx_index - 1)
    valid.append(ctx_index % 2 == 1)
    for step in range(1, levels):
        owners.append(partner - 2 * step)
        valid.append(ctx_index >= 2 * step)
    return owners, valid


def tree_return(slot_parts, levels):
    count = 2 * levels
    climbed = slot_parts[: levels - 1]
    crossed = slot_parts[levels - 1 :]
    back = [None]
    for step in range(1, levels):
        back.append(
            lax.ppermute(crossed[step], "ctx", [(c, c ^ 1) for c in range(2 * step, count)])
        )
    total = None
    carry = None
    for step in range(levels - 1, 0, -1):
        acc = climbed[step - 1].astype(jnp.float32) + back[step].astype(jnp.float32)
        if carry is not None:
            acc = acc + carry.astype(jnp.float32)
        carry = lax.ppermute(
            acc.astype(jnp.bfloat16), "ctx", [(c, c - 2) for c in range(2 * step, count)]
        )
    total = lax.ppermute(crossed[0], "ctx", [(c, c - 1) for c in range(1, count, 2)])
    total = total.astype(jnp.float32)
    if carry is not None:
        total = total + carry.astype(jnp.float32)
    return total


def shifted(block, axis, distance):
    devices = range(lax.axis_size(axis))
    route = [(i - distance, i) for i in devices if i - distance in devices]
    return lax.ppermute(block, axis, route)


def shards(
    normed_input,
    queries,
    keys,
    value_projection,
    adapter_down,
    adapter_up,
    output_gradient,
    policy_logprob,
    reference_logprob,
    token_pair_index,
):
    tok_rows = normed_input.shape[1]
    width_kv = keys.shape[2]
    kv_heads = width_kv // HEAD_SIZE
    group_size = queries.shape[2] // width_kv
    hidden_rows = normed_input[0]
    own_keys = keys[0]
    pair_index = lax.axis_index("pair")
    ctx_index = lax.axis_index("ctx")
    half_cols = width_kv // 2
    own_half = lax.dynamic_slice_in_dim(value_projection, pair_index * half_cols, half_cols, 1)
    ctx_count = lax.axis_size("ctx")
    if ctx_count % 2 == 0 and 4 <= ctx_count <= 8:
        rows_half = tree_gather(own_half, ctx_index, ctx_count // 2)
    else:
        rows_half = lax.all_gather(own_half, "ctx", axis=0, tiled=True)
    if lax.axis_size("pair") == 2:
        other_half = from_partner(rows_half, "pair", 0)
        full_weight = jnp.zeros((rows_half.shape[0], width_kv), rows_half.dtype)
        full_weight = lax.dynamic_update_slice_in_dim(full_weight, rows_half, pair_index * half_cols, 1)
        full_weight = lax.dynamic_update_slice_in_dim(
            full_weight, other_half, (1 - pair_index) * half_cols, 1
        )
    else:
        full_weight = lax.all_gather(rows_half, "pair", axis=1, tiled=True)
    rank_projection = jnp.dot(hidden_rows, adapter_down, preferred_element_type=jnp.float32).astype(
        jnp.bfloat16
    )
    values = (
        jnp.dot(hidden_rows, full_weight, preferred_element_type=jnp.float32)
        + ADAPTER_SCALE * jnp.dot(rank_projection, adapter_up, preferred_element_type=jnp.float32)
    ).astype(jnp.bfloat16)
    segment_labels = token_pair_index[0]
    seg_table = (segment_labels[:, None] == jnp.arange(SEGS, dtype=jnp.int32)[None, :]).astype(
        jnp.float32
    )
    log_gap = policy_logprob[0] - reference_logprob[0]
    part_diff = jnp.sum(seg_table * log_gap[:, None], 0)
    part_count = jnp.sum(seg_table, 0)
    both_sums = butterfly_sum(jnp.concatenate([part_diff, part_count], 0), ("ctx",), far_first=True)
    own_diff, counts = both_sums[:SEGS], both_sums[SEGS:]
    other_diff = from_partner(own_diff, "pair", 0)
    direction = 1.0 - 2.0 * pair_index.astype(jnp.float32)
    margin = DPO_BETA * (direction * (own_diff - other_diff))
    coef = -direction * DPO_BETA * LOSS_SCALE * jax.nn.sigmoid(-margin)
    starts = jnp.cumsum(counts) - counts
    tok_start = jnp.sum(seg_table * starts[None, :], 1).astype(jnp.int32)
    token_coefficient = jnp.sum(seg_table * coef[None, :], 1)
    ctx_size = lax.axis_size("ctx")
    halo_blocks = min(WINDOW // tok_rows, ctx_size - 1)
    use_tree = halo_blocks == ctx_size - 1 and ctx_size % 2 == 0 and ctx_size >= 4
    levels = ctx_size // 2
    row_iota = jnp.arange(tok_rows, dtype=jnp.int32)
    if use_tree:
        key_blocks = tree_spread(own_keys, levels)
        value_blocks = tree_spread(values, levels)
        owners, valid = tree_slots(ctx_index, levels)
        far = jnp.int32(1 << 30)
        upos = jnp.concatenate(
            [jnp.where(ok, owner * tok_rows + row_iota, far) for owner, ok in zip(owners, valid)]
            + [ctx_index * tok_rows + row_iota],
            0,
        )
    else:
        key_blocks = []
        value_blocks = []
        for distance in range(halo_blocks, 0, -1):
            key_blocks.append(shifted(own_keys, "ctx", distance))
            value_blocks.append(shifted(values, "ctx", distance))
    all_keys = jnp.concatenate(key_blocks + [own_keys], 0)
    all_keys, own_values = lax.optimization_barrier((all_keys, values))
    all_values = jnp.concatenate(value_blocks + [own_values], 0)
    span = all_keys.shape[0]
    tpos = ctx_index * tok_rows + row_iota
    if not use_tree:
        upos = ctx_index * tok_rows - halo_blocks * tok_rows + jnp.arange(span, dtype=jnp.int32)
    allowed = (
        (upos[None, :] <= tpos[:, None])
        & (upos[None, :] > tpos[:, None] - WINDOW)
        & (upos[None, :] >= tok_start[:, None])
    )
    coef_rows = token_coefficient[None, :, None]
    query_rows = queries[0].reshape(tok_rows, kv_heads, group_size, HEAD_SIZE)
    grad_rows = output_gradient[0].reshape(tok_rows, kv_heads, group_size, HEAD_SIZE)
    key_rows = all_keys.reshape(span, kv_heads, HEAD_SIZE)
    value_rows = all_values.reshape(span, kv_heads, HEAD_SIZE)
    scores = ATTN_SCALE * jnp.einsum(
        "tjgd,ljd->jgtl", query_rows, key_rows, preferred_element_type=jnp.float32
    )
    masked = jnp.where(allowed[None, None], scores, NEG_FILL)
    row_max = jnp.max(masked, -1, keepdims=True)
    weights_exp = jnp.where(allowed[None, None], jnp.exp(masked - row_max), 0.0)
    attn_probs = weights_exp / jnp.sum(weights_exp, -1, keepdims=True)
    prob_grad = coef_rows[None] * jnp.einsum(
        "tjgd,ljd->jgtl", grad_rows, value_rows, preferred_element_type=jnp.float32
    )
    row_delta = jnp.sum(attn_probs * prob_grad, -1, keepdims=True)
    score_grad = (ATTN_SCALE * attn_probs * (prob_grad - row_delta)).astype(jnp.bfloat16)
    query_grad = jnp.einsum(
        "jgtl,ljd->tjgd", score_grad, key_rows, preferred_element_type=jnp.float32
    ).astype(jnp.bfloat16).reshape(tok_rows, kv_heads * group_size * HEAD_SIZE)
    key_parts = jnp.einsum(
        "jgtl,tjgd->ljd", score_grad, query_rows, preferred_element_type=jnp.float32
    ).reshape(span, width_kv)
    weighted = (attn_probs * coef_rows[None]).astype(jnp.bfloat16)
    value_parts = jnp.einsum(
        "jgtl,tjgd->ljd", weighted, grad_rows, preferred_element_type=jnp.float32
    ).reshape(span, width_kv)
    key_total = key_parts[halo_blocks * tok_rows :]
    value_total = value_parts[halo_blocks * tok_rows :]
    if use_tree:
        slot_rows = lambda parts: [
            parts[k * tok_rows : (k + 1) * tok_rows].astype(jnp.bfloat16) for k in range(halo_blocks)
        ]
        key_total = key_total + tree_return(slot_rows(key_parts), levels)
        value_total = value_total + tree_return(slot_rows(value_parts), levels)
    else:
        for distance in range(1, halo_blocks + 1):
            block_start = (halo_blocks - distance) * tok_rows
            send_keys = key_parts[block_start : block_start + tok_rows].astype(jnp.bfloat16)
            send_values = value_parts[block_start : block_start + tok_rows].astype(jnp.bfloat16)
            back_keys, back_values = shifted((send_keys, send_values), "ctx", -distance)
            key_total = key_total + back_keys.astype(jnp.float32)
            value_total = value_total + back_values.astype(jnp.float32)
    key_grad = key_total.astype(jnp.bfloat16)
    value_gradient = value_total.astype(jnp.bfloat16)
    rank_middle = jnp.einsum(
        "sj,zj->sz", value_gradient, adapter_up, preferred_element_type=jnp.float32
    ).astype(jnp.bfloat16)
    input_grad = (
        jnp.einsum("tk,dk->td", value_gradient, full_weight, preferred_element_type=jnp.float32)
        + ADAPTER_SCALE
        * jnp.einsum("pb,wb->pw", rank_middle, adapter_down, preferred_element_type=jnp.float32)
    ).astype(jnp.bfloat16)
    up_factor = ADAPTER_SCALE * jnp.einsum(
        "tr,tk->rk", rank_projection, value_gradient, preferred_element_type=jnp.float32
    )
    down_factor = ADAPTER_SCALE * jnp.einsum(
        "td,tr->dr", hidden_rows, rank_middle, preferred_element_type=jnp.float32
    )
    down_size = down_factor.size
    flat = jnp.concatenate([down_factor.reshape(-1), up_factor.reshape(-1)], 0)
    flat = butterfly_sum(flat.reshape(-1, HEAD_SIZE), ("ctx", "pair"), far_first=True).reshape(-1)
    down_gradient = flat[:down_size].reshape(down_factor.shape)
    up_gradient = flat[down_size:].reshape(up_factor.shape)
    return (input_grad[None], query_grad[None], key_grad[None], down_gradient, up_gradient)


def solution(mesh):
    return jax.shard_map(
        shards,
        mesh=mesh,
        in_specs=(
            P(("grp", "pair"), "ctx", None),
            P(("grp", "pair"), "ctx", None),
            P(("grp", "pair"), "ctx", None),
            P("ctx", None),
            P(),
            P(),
            P(("grp", "pair"), "ctx", None),
            P(("grp", "pair"), "ctx"),
            P(("grp", "pair"), "ctx"),
            P(("grp", "pair"), "ctx"),
        ),
        out_specs=(
            P(("grp", "pair"), "ctx", None),
            P(("grp", "pair"), "ctx", None),
            P(("grp", "pair"), "ctx", None),
            P("grp", None),
            P("grp", None),
        ),
        check_vma=False,
    )
```
